128 devices in a mesh: space: 32 (over x, z, core), feat: 4 (over y).
Axes of the slice: x: 4, y: 4, z: 4, core: 2. Of those that a mesh axis runs over, the one named last changes fastest.
Arguments:
- inputs: bfloat16 [2, 96, 180, 1024], P(None, 'space', None, 'feat'), may hold values from -15 to 15
- cotangent: bfloat16 [2, 96, 180, 1024], P(None, 'space', None, 'feat'), may hold values from -6 to 6
- spec_w1: float32 [2, 8, 128, 128], P(None, 'feat'), may hold values from -0.375 to 0.375
- spec_b1: float32 [2, 1024], P(None, 'feat'), may hold values from -0.3 to 0.3
- spec_w2: float32 [2, 8, 128, 128], P(None, 'feat'), may hold values from -0.375 to 0.375
- spec_b2: float32 [2, 1024], P(None, 'feat'), may hold values from -0.3 to 0.3
- up_weight: bfloat16 [1024, 4096], P(None, 'feat'), may hold values from -0.1875 to 0.1875
- down_weight: bfloat16 [4096, 1024], P('feat'), may hold values from -0.09375 to 0.09375
Outputs:
- output: bfloat16 [2, 96, 180, 1024], P(None, 'space', None, 'feat')
- grad_input: bfloat16 [2, 96, 180, 1024], P(None, 'space', None, 'feat')
The draws below stay inside these ranges and needn't reach their ends.
All inputs are finite; a program needn't handle non-finite values.
Results may differ from the reference program's by a relative error of at most 0.0102.
Values may be sent and summed in bfloat16 or wider, within the bound.
No kernel may reach another device: no remote copies, remote signals or barrier semaphores. Data moves between devices by JAX's collectives and lax.ppermute only.
A program may use at most 128 MiB of HBM per device.

```python
import math
import jax
import jax.numpy as jnp
from jax import lax

D = 1024
BLOCKS = 8
W = 180
BATCH = 2
FF = 4096
H = 96


def draw_inputs(key, part):
    key_base, key_column, key_row = jax.random.split(key, 3)
    position = jnp.arange(D, dtype=jnp.int32).astype(jnp.float32) / D
    column_scale = 10.0 ** (0.5 * position + 0.5 * jax.random.uniform(key_column, (D,), jnp.float32))
    row_scale = 10.0 ** jax.random.uniform(key_row, (BATCH, H, W, 1), jnp.float32)
    base_vals = jnp.clip(jax.random.normal(key_base, (BATCH, H, W, D), jnp.float32), -5.0, 5.0)
    return (0.03 * base_vals * column_scale * row_scale).astype(jnp.bfloat16)


def level_of(stream_key, shape, shards, low, top_value):
    def one(dim, parts):
        steps = jax.random.uniform(jax.random.fold_in(jax.random.fold_in(stream_key, 6), dim), (parts,), jnp.float32, low / len(shards), top_value / len(shards))
        return jnp.repeat(jnp.exp(steps), shape[dim] // parts).reshape((-1,) + (1,) * (len(shape) - dim - 1))

    gain = one(*shards[0])
    for cut in shards[1:]:
        gain = gain * one(*cut)
    return gain


def gaussian(own_key, dims, spread, reach, cuts=(), held_as=jnp.bfloat16):
    drawn = jax.random.normal(own_key, dims, jnp.float32) * spread
    if len(cuts) > 0:
        drawn = level_of(own_key, dims, cuts, -0.22, 0.18) * drawn
    return jnp.clip(drawn, min=-reach, max=reach).astype(held_as)


def setup_inputs(seed: int = 0) -> dict:
    key_list = jax.random.split(jax.random.key(seed), 9)
    inputs = draw_inputs(jax.random.fold_in(key_list[8], 71), 0)
    cotangent = gaussian(key_list[1], (BATCH, H, W, D), 1.0, 6.0, ((1, 32), (3, 4)))
    spec_w1 = gaussian(key_list[2], (2, BLOCKS, D // BLOCKS, D // BLOCKS), (2 * D // BLOCKS) ** -0.5, 0.375, ((1, 4),), jnp.float32)
    spec_b1 = gaussian(key_list[3], (2, D), 0.05, 0.3, ((1, 4),), jnp.float32)
    spec_w2 = gaussian(key_list[4], (2, BLOCKS, D // BLOCKS, D // BLOCKS), (2 * D // BLOCKS) ** -0.5, 0.375, ((1, 4),), jnp.float32)
    spec_b2 = gaussian(key_list[5], (2, D), 0.05, 0.3, ((1, 4),), jnp.float32)
    up_weight = gaussian(key_list[6], (D, FF), D ** -0.5, 0.1875, ((1, 4),))
    down_weight = gaussian(key_list[7], (FF, D), FF ** -0.5, 0.09375, ((0, 4),))
    return {"inputs": inputs, "cotangent": cotangent, "spec_w1": spec_w1, "spec_b1": spec_b1, "spec_w2": spec_w2, "spec_b2": spec_b2, "up_weight": up_weight, "down_weight": down_weight}


EPSILON = 1e-05
SHRINK_LEVEL = 0.1
HIGHEST = lax.Precision.HIGHEST

def longitude_tables(width_lon):
    mode_count = width_lon // 2 + 1
    cell_index = jnp.arange(width_lon, dtype=jnp.int32)[:, None]
    wave_number = jnp.arange(mode_count, dtype=jnp.int32)[None, :]
    phase_angle = 2.0 * math.pi / width_lon * (cell_index * wave_number % width_lon).astype(jnp.float32)
    scaling = 1.0 / math.sqrt(width_lon)
    cos_fwd = jnp.cos(phase_angle) * scaling
    sin_fwd = -jnp.sin(phase_angle) * scaling
    doubled = jnp.where((wave_number == 0) | (wave_number * 2 == width_lon), 1.0, 2.0).astype(jnp.float32)
    return (cos_fwd, sin_fwd, cos_fwd * doubled, sin_fwd * doubled)

def latitude_tables(length):
    index_row = jnp.arange(length, dtype=jnp.int32)
    phase_angle = 2.0 * math.pi / length * (index_row[:, None] * index_row[None, :] % length).astype(jnp.float32)
    scaling = 1.0 / math.sqrt(length)
    return (jnp.cos(phase_angle) * scaling, -jnp.sin(phase_angle) * scaling)

def lat_apply(table, field):
    return jnp.einsum('gh,bhkc->bgkc', table, field, precision=HIGHEST)

def complex_latitude(table_cos, table_sin, real_part, imag_part, inverse):
    if inverse:
        return (lat_apply(table_cos, real_part) + lat_apply(table_sin, imag_part), lat_apply(table_cos, imag_part) - lat_apply(table_sin, real_part))
    return (lat_apply(table_cos, real_part) - lat_apply(table_sin, imag_part), lat_apply(table_cos, imag_part) + lat_apply(table_sin, real_part))

def lon_forward(field, table):
    return jnp.einsum('brwc,wk->brkc', field, table, precision=HIGHEST)

def lon_back(spec, table):
    return jnp.einsum('brkc,wk->brwc', spec, table, precision=HIGHEST)

def to_blocks(field, block_size):
    return field.reshape(field.shape[:-1] + (field.shape[-1] // block_size, block_size))

def block_mult(field, weights):
    return jnp.einsum('...nc,nce->...ne', field, weights, precision=HIGHEST)

def block_product(real_part, imag_part, weights):
    return (block_mult(real_part, weights[0]) - block_mult(imag_part, weights[1]), block_mult(real_part, weights[1]) + block_mult(imag_part, weights[0]))

def spectral_filter(field, spec_w1, spec_b1, spec_w2, spec_b2, tables_lon, tables_lat, block_size):
    cos_fwd, sin_fwd, cos_inv, sin_inv = tables_lon
    table_cos, table_sin = tables_lat
    spec_real, spec_imag = complex_latitude(table_cos, table_sin, lon_forward(field, cos_fwd), lon_forward(field, sin_fwd), False)
    bias_one = to_blocks(spec_b1, block_size)
    bias_two = to_blocks(spec_b2, block_size)
    first_real, first_imag = block_product(to_blocks(spec_real, block_size), to_blocks(spec_imag, block_size), spec_w1)
    first_real = jax.nn.relu(first_real + bias_one[0])
    first_imag = jax.nn.relu(first_imag + bias_one[1])
    second_real, second_imag = block_product(first_real, first_imag, spec_w2)
    second_real = second_real + bias_two[0]
    second_imag = second_imag + bias_two[1]
    shrunk_real = (second_real - jnp.clip(second_real, -SHRINK_LEVEL, SHRINK_LEVEL)).reshape(spec_real.shape)
    shrunk_imag = (second_imag - jnp.clip(second_imag, -SHRINK_LEVEL, SHRINK_LEVEL)).reshape(spec_real.shape)
    back_real, back_imag = complex_latitude(table_cos, table_sin, shrunk_real, shrunk_imag, True)
    return lon_back(back_real, cos_inv) + lon_back(back_imag, sin_inv)

def norm_stats(values, full_width):
    mean_val = lax.optimization_barrier(jnp.sum(values, axis=-1, keepdims=True)) / full_width
    square_mean = lax.optimization_barrier(jnp.sum(values * values, axis=-1, keepdims=True)) / full_width
    return (mean_val, lax.rsqrt(square_mean - mean_val * mean_val + EPSILON))

def norm_back(grad_val, normalized, rstd_val, full_width):
    first_mean = lax.optimization_barrier(jnp.sum(grad_val, axis=-1, keepdims=True)) / full_width
    second_mean = lax.optimization_barrier(jnp.sum(grad_val * normalized, axis=-1, keepdims=True)) / full_width
    return rstd_val * (grad_val - first_mean - normalized * second_mean)

def gelu_value(field):
    return 0.5 * field * (1.0 + lax.erf(field * (1.0 / math.sqrt(2.0))))

def gelu_slope(field):
    return 0.5 * (1.0 + lax.erf(field * (1.0 / math.sqrt(2.0)))) + field * jnp.exp(-0.5 * field * field) * (1.0 / math.sqrt(2.0 * math.pi))

def reference(inputs, cotangent, spec_w1, spec_b1, spec_w2, spec_b2, up_weight, down_weight):
    full_width = inputs.shape[3]
    block_size = spec_w1.shape[2]
    tables_lon = longitude_tables(inputs.shape[2])
    tables_lat = latitude_tables(inputs.shape[1])
    values = inputs.astype(jnp.float32)
    mean_one, rstd_one = norm_stats(values, full_width)
    normed = (values - mean_one) * rstd_one

    def apply_filter(field):
        return spectral_filter(field, spec_w1, spec_b1, spec_w2, spec_b2, tables_lon, tables_lat, block_size)
    filtered, pull_back = jax.vjp(apply_filter, normed)
    residual = (filtered + normed + values).astype(jnp.bfloat16)
    residual_vals = residual.astype(jnp.float32)
    mean_two, rstd_two = norm_stats(residual_vals, full_width)
    vhat = (residual_vals - mean_two) * rstd_two
    flat_norm = vhat.astype(jnp.bfloat16).reshape(-1, full_width)
    hidden = jnp.dot(flat_norm, up_weight, preferred_element_type=jnp.float32)
    activated = gelu_value(hidden).astype(jnp.bfloat16)
    mixed = jnp.dot(activated, down_weight, preferred_element_type=jnp.float32).reshape(values.shape)
    output = (residual_vals + mixed).astype(jnp.bfloat16)
    grad_act = jnp.dot(cotangent.reshape(-1, full_width), down_weight.T, preferred_element_type=jnp.float32)
    grad_hidden = (grad_act * gelu_slope(hidden)).astype(jnp.bfloat16)
    grad_vhat = jnp.dot(grad_hidden, up_weight.T, preferred_element_type=jnp.float32).reshape(values.shape)
    grad_residual = cotangent.astype(jnp.float32) + norm_back(grad_vhat, vhat, rstd_two, full_width)
    grad_filter, = pull_back(grad_residual)
    grad_normed = grad_residual + grad_filter
    grad_input = (grad_residual + norm_back(grad_normed, normed, rstd_one, full_width)).astype(jnp.bfloat16)
    return (output, grad_input)
```

```python
import math

import jax
import jax.numpy as jnp
from jax import lax
from jax.sharding import PartitionSpec as P

EPSILON = 1e-05
SHRINK_LEVEL = 0.1
HIGHEST = lax.Precision.HIGHEST


def longitude_tables(width_lon):
    mode_count = width_lon // 2 + 1
    cell_index = jnp.arange(width_lon, dtype=jnp.int32)[:, None]
    wave_number = jnp.arange(mode_count, dtype=jnp.int32)[None, :]
    phase_angle = (
        2.0 * math.pi / width_lon * (cell_index * wave_number % width_lon).astype(jnp.float32)
    )
    scaling = 1.0 / math.sqrt(width_lon)
    cos_fwd = jnp.cos(phase_angle) * scaling
    sin_fwd = -jnp.sin(phase_angle) * scaling
    doubled = jnp.where((wave_number == 0) | (wave_number * 2 == width_lon), 1.0, 2.0).astype(
        jnp.float32
    )
    return (cos_fwd, sin_fwd, cos_fwd * doubled, sin_fwd * doubled)


def padded_tables(width_lon, multiple):
    tables = longitude_tables(width_lon)
    modes = tables[0].shape[1]
    extra = -modes % multiple
    return tuple(jnp.pad(table, ((0, 0), (0, extra))) for table in tables)


def lat_apply(table, field):
    return jnp.einsum("gh,bhkc->bgkc", table, field, precision=HIGHEST)


def complex_latitude(table_cos, table_sin, real_part, imag_part, inverse):
    if inverse:
        return (
            lat_apply(table_cos, real_part) + lat_apply(table_sin, imag_part),
            lat_apply(table_cos, imag_part) - lat_apply(table_sin, real_part),
        )
    return (
        lat_apply(table_cos, real_part) - lat_apply(table_sin, imag_part),
        lat_apply(table_cos, imag_part) + lat_apply(table_sin, real_part),
    )


def lon_forward(field, table):
    return jnp.einsum("brwc,wk->brkc", field, table, precision=HIGHEST)


def lon_back(spec, table):
    return jnp.einsum("brkc,wk->brwc", spec, table, precision=HIGHEST)


def to_blocks(field, block_size):
    return field.reshape(field.shape[:-1] + (field.shape[-1] // block_size, block_size))


def block_mult(field, weights):
    return jnp.einsum("...nc,nce->...ne", field, weights, precision=HIGHEST)


def block_mult_back(field, weights):
    return jnp.einsum("...ne,nce->...nc", field, weights, precision=HIGHEST)


def block_product(real_part, imag_part, weights):
    return (
        block_mult(real_part, weights[0]) - block_mult(imag_part, weights[1]),
        block_mult(real_part, weights[1]) + block_mult(imag_part, weights[0]),
    )


def block_adjoint(real_part, imag_part, weights):
    return (
        block_mult_back(real_part, weights[0]) + block_mult_back(imag_part, weights[1]),
        block_mult_back(imag_part, weights[0]) - block_mult_back(real_part, weights[1]),
    )


def latitude_tables(length):
    index_row = jnp.arange(length, dtype=jnp.int32)
    phase_angle = (
        2.0 * math.pi / length * (index_row[:, None] * index_row[None, :] % length).astype(jnp.float32)
    )
    scaling = 1.0 / math.sqrt(length)
    return (jnp.cos(phase_angle) * scaling, -jnp.sin(phase_angle) * scaling)


def to_columns(real_part, imag_part):
    stacked = jnp.stack([real_part, imag_part])
    moved = lax.all_to_all(stacked, "space", 3, 2, tiled=True)
    return (moved[0], moved[1])


def to_rows(real_part, imag_part):
    stacked = jnp.stack([real_part, imag_part])
    moved = lax.all_to_all(stacked, "space", 2, 3, tiled=True)
    return (moved[0], moved[1])


def enter_spectrum(real_part, imag_part):
    length = real_part.shape[1] * lax.axis_size("space")
    table_cos, table_sin = latitude_tables(length)
    real_part, imag_part = to_columns(real_part, imag_part)
    return complex_latitude(table_cos, table_sin, real_part, imag_part, False)


def leave_spectrum(real_part, imag_part):
    table_cos, table_sin = latitude_tables(real_part.shape[1])
    real_part, imag_part = complex_latitude(table_cos, table_sin, real_part, imag_part, True)
    return to_rows(real_part, imag_part)


def token_sums(first_term, second_term):
    return lax.psum((first_term, second_term), "feat")


def channel_share(term):
    return lax.psum_scatter(
        term.astype(jnp.bfloat16), "feat", scatter_dimension=3, tiled=True
    ).astype(jnp.float32)


def gelu_value(field):
    return 0.5 * field * (1.0 + lax.erf(field * (1.0 / math.sqrt(2.0))))


def gelu_slope(field):
    return 0.5 * (1.0 + lax.erf(field * (1.0 / math.sqrt(2.0)))) + field * jnp.exp(
        -0.5 * field * field
    ) * (1.0 / math.sqrt(2.0 * math.pi))


def per_device(inputs, cotangent, spec_w1, spec_b1, spec_w2, spec_b2, up_weight, down_weight):
    full_width = up_weight.shape[0]
    block_size = spec_w1.shape[2]
    cos_fwd, sin_fwd, cos_inv, sin_inv = padded_tables(inputs.shape[2], lax.axis_size("space"))
    values = inputs.astype(jnp.float32)
    first_sum, second_sum = token_sums(jnp.sum(values, axis=-1), jnp.sum(values * values, axis=-1))
    mean_one = first_sum[..., None] / full_width
    rstd_one = lax.rsqrt(second_sum[..., None] / full_width - mean_one * mean_one + EPSILON)
    normed = (values - mean_one) * rstd_one
    spec_real, spec_imag = enter_spectrum(
        lon_forward(normed, cos_fwd), lon_forward(normed, sin_fwd)
    )
    spec_shape = spec_real.shape
    bias_one = to_blocks(spec_b1, block_size)
    bias_two = to_blocks(spec_b2, block_size)
    first_real, first_imag = block_product(
        to_blocks(spec_real, block_size), to_blocks(spec_imag, block_size), spec_w1
    )
    first_real = jax.nn.relu(first_real + bias_one[0])
    first_imag = jax.nn.relu(first_imag + bias_one[1])
    second_real, second_imag = block_product(first_real, first_imag, spec_w2)
    second_real = second_real + bias_two[0]
    second_imag = second_imag + bias_two[1]
    shrunk_real = (second_real - jnp.clip(second_real, -SHRINK_LEVEL, SHRINK_LEVEL)).reshape(
        spec_shape
    )
    shrunk_imag = (second_imag - jnp.clip(second_imag, -SHRINK_LEVEL, SHRINK_LEVEL)).reshape(
        spec_shape
    )
    back_real, back_imag = leave_spectrum(shrunk_real, shrunk_imag)
    filtered = lon_back(back_real, cos_inv) + lon_back(back_imag, sin_inv)
    residual = (filtered + normed + values).astype(jnp.bfloat16)
    residual_vals = residual.astype(jnp.float32)
    whole_residual, whole_cotangent = (
        lax.all_gather(residual, "feat", axis=3, tiled=True),
        lax.all_gather(cotangent, "feat", axis=3, tiled=True),
    )
    whole_vals = whole_residual.astype(jnp.float32)
    mean_two = jnp.sum(whole_vals, axis=-1, keepdims=True) / full_width
    square_two = jnp.sum(whole_vals * whole_vals, axis=-1, keepdims=True) / full_width
    rstd_two = lax.rsqrt(square_two - mean_two * mean_two + EPSILON)
    vhat = (whole_vals - mean_two) * rstd_two
    hidden = jnp.einsum(
        "brwd,dh->brwh", vhat.astype(jnp.bfloat16), up_weight, preferred_element_type=jnp.float32
    )
    activated = gelu_value(hidden).astype(jnp.bfloat16)
    mixed_term = jnp.einsum(
        "brwh,hd->brwd", activated, down_weight, preferred_element_type=jnp.float32
    )
    output = (residual_vals + channel_share(mixed_term)).astype(jnp.bfloat16)
    grad_act = jnp.einsum(
        "brwd,hd->brwh", whole_cotangent, down_weight, preferred_element_type=jnp.float32
    )
    grad_hidden = (grad_act * gelu_slope(hidden)).astype(jnp.bfloat16)
    grad_term = jnp.einsum(
        "brwh,dh->brwd", grad_hidden, up_weight, preferred_element_type=jnp.float32
    )
    grad_vhat = channel_share(grad_term)
    own_hat = (residual_vals - mean_two) * rstd_two
    total_one, total_two = token_sums(
        jnp.sum(grad_vhat, axis=-1), jnp.sum(grad_vhat * own_hat, axis=-1)
    )
    grad_residual = cotangent.astype(jnp.float32) + rstd_two * (
        grad_vhat
        - total_one[..., None] / full_width
        - own_hat * (total_two[..., None] / full_width)
    )
    grad_real, grad_imag = enter_spectrum(
        lon_forward(grad_residual, cos_inv), lon_forward(grad_residual, sin_inv)
    )
    grad_real = jnp.where(
        jnp.abs(second_real) > SHRINK_LEVEL, to_blocks(grad_real, block_size), 0.0
    )
    grad_imag = jnp.where(
        jnp.abs(second_imag) > SHRINK_LEVEL, to_blocks(grad_imag, block_size), 0.0
    )
    first_grad_real, first_grad_imag = block_adjoint(grad_real, grad_imag, spec_w2)
    first_grad_real = jnp.where(first_real > 0.0, first_grad_real, 0.0)
    first_grad_imag = jnp.where(first_imag > 0.0, first_grad_imag, 0.0)
    spec_grad_real, spec_grad_imag = block_adjoint(first_grad_real, first_grad_imag, spec_w1)
    rows_real, rows_imag = leave_spectrum(
        spec_grad_real.reshape(spec_shape), spec_grad_imag.reshape(spec_shape)
    )
    grad_normed = grad_residual + lon_back(rows_real, cos_fwd) + lon_back(rows_imag, sin_fwd)
    norm_one, norm_two = token_sums(
        jnp.sum(grad_normed, axis=-1), jnp.sum(grad_normed * normed, axis=-1)
    )
    grad_input = grad_residual + rstd_one * (
        grad_normed - norm_one[..., None] / full_width - normed * (norm_two[..., None] / full_width)
    )
    return (output, grad_input.astype(jnp.bfloat16))


def solution(mesh):
    return jax.shard_map(
        per_device,
        mesh=mesh,
        in_specs=(
            P(None, "space", None, "feat"),
            P(None, "space", None, "feat"),
            P(None, "feat", None, None),
            P(None, "feat"),
            P(None, "feat", None, None),
            P(None, "feat"),
            P(None, "feat"),
            P("feat", None),
        ),
        out_specs=(P(None, "space", None, "feat"), P(None, "space", None, "feat")),
        check_vma=False,
    )
```

```python
import math

import jax
import jax.numpy as jnp
from jax import lax
from jax.sharding import PartitionSpec as P

EPSILON = 1e-05
SHRINK_LEVEL = 0.1
HIGHEST = lax.Precision.HIGHEST


def longitude_tables(width_lon):
    mode_count = width_lon // 2 + 1
    cell_index = jnp.arange(width_lon, dtype=jnp.int32)[:, None]
    wave_number = jnp.arange(mode_count, dtype=jnp.int32)[None, :]
    phase_angle = (
        2.0 * math.pi / width_lon * (cell_index * wave_number % width_lon).astype(jnp.float32)
    )
    scaling = 1.0 / math.sqrt(width_lon)
    cos_fwd = jnp.cos(phase_angle) * scaling
    sin_fwd = -jnp.sin(phase_angle) * scaling
    doubled = jnp.where((wave_number == 0) | (wave_number * 2 == width_lon), 1.0, 2.0).astype(
        jnp.float32
    )
    return (cos_fwd, sin_fwd, cos_fwd * doubled, sin_fwd * doubled)


def padded_tables(width_lon, multiple):
    tables = longitude_tables(width_lon)
    modes = tables[0].shape[1]
    extra = -modes % multiple
    return tuple(jnp.pad(table, ((0, 0), (0, extra))) for table in tables)


def lat_apply(table, field):
    return jnp.einsum("gh,bhkc->bgkc", table, field, precision=HIGHEST)


def complex_latitude(table_cos, table_sin, real_part, imag_part, inverse):
    if inverse:
        return (
            lat_apply(table_cos, real_part) + lat_apply(table_sin, imag_part),
            lat_apply(table_cos, imag_part) - lat_apply(table_sin, real_part),
        )
    return (
        lat_apply(table_cos, real_part) - lat_apply(table_sin, imag_part),
        lat_apply(table_cos, imag_part) + lat_apply(table_sin, real_part),
    )


def lon_forward(field, table):
    return jnp.einsum("brwc,wk->brkc", field, table, precision=HIGHEST)


def lon_back(spec, table):
    return jnp.einsum("brkc,wk->brwc", spec, table, precision=HIGHEST)


def to_blocks(field, block_size):
    return field.reshape(field.shape[:-1] + (field.shape[-1] // block_size, block_size))


def block_mult(field, weights):
    return jnp.einsum("...nc,nce->...ne", field, weights, precision=HIGHEST)


def block_mult_back(field, weights):
    return jnp.einsum("...ne,nce->...nc", field, weights, precision=HIGHEST)


def block_product(real_part, imag_part, weights):
    return (
        block_mult(real_part, weights[0]) - block_mult(imag_part, weights[1]),
        block_mult(real_part, weights[1]) + block_mult(imag_part, weights[0]),
    )


def block_adjoint(real_part, imag_part, weights):
    return (
        block_mult_back(real_part, weights[0]) + block_mult_back(imag_part, weights[1]),
        block_mult_back(imag_part, weights[0]) - block_mult_back(real_part, weights[1]),
    )


def latitude_tables(length):
    index_row = jnp.arange(length, dtype=jnp.int32)
    phase_angle = (
        2.0 * math.pi / length * (index_row[:, None] * index_row[None, :] % length).astype(jnp.float32)
    )
    scaling = 1.0 / math.sqrt(length)
    return (jnp.cos(phase_angle) * scaling, -jnp.sin(phase_angle) * scaling)


def to_columns(real_part, imag_part):
    stacked = jnp.stack([real_part, imag_part])
    moved = lax.all_to_all(stacked, "space", 3, 2, tiled=True)
    return (moved[0], moved[1])


def to_rows(real_part, imag_part):
    stacked = jnp.stack([real_part, imag_part])
    moved = lax.all_to_all(stacked, "space", 2, 3, tiled=True)
    return (moved[0], moved[1])


def enter_spectrum(real_part, imag_part):
    length = real_part.shape[1] * lax.axis_size("space")
    table_cos, table_sin = latitude_tables(length)
    real_part, imag_part = to_columns(real_part, imag_part)
    return complex_latitude(table_cos, table_sin, real_part, imag_part, False)


def leave_spectrum(real_part, imag_part):
    table_cos, table_sin = latitude_tables(real_part.shape[1])
    real_part, imag_part = complex_latitude(table_cos, table_sin, real_part, imag_part, True)
    return to_rows(real_part, imag_part)


def token_sums(first_term, second_term):
    pair = jnp.stack([first_term, second_term])
    count = lax.axis_size("feat")
    bit = 1
    while bit < count:
        pair = pair + lax.ppermute(pair, "feat", [(i, i ^ bit) for i in range(count)])
        bit *= 2
    return (pair[0], pair[1])


def ring_send(block):
    count = lax.axis_size("feat")
    return [block] + [
        lax.ppermute(block, "feat", [(i, (i + shift) % count) for i in range(count)])
        for shift in range(1, count)
    ]


def ring_assemble(parts):
    count = len(parts)
    position = lax.axis_index("feat")
    block = parts[0]
    width = block.shape[-1]
    whole = jnp.zeros(block.shape[:-1] + (width * count,), block.dtype)
    for shift, moved in enumerate(parts):
        source = (position + count - shift) % count
        whole = lax.dynamic_update_slice_in_dim(whole, moved, source * width, axis=block.ndim - 1)
    return whole


def channel_share(term):
    return lax.psum_scatter(
        term.astype(jnp.bfloat16), "feat", scatter_dimension=3, tiled=True
    ).astype(jnp.float32)


def gelu_value(field):
    return 0.5 * field * (1.0 + lax.erf(field * (1.0 / math.sqrt(2.0))))


def gelu_slope(field):
    return 0.5 * (1.0 + lax.erf(field * (1.0 / math.sqrt(2.0)))) + field * jnp.exp(
        -0.5 * field * field
    ) * (1.0 / math.sqrt(2.0 * math.pi))


def per_device(inputs, cotangent, spec_w1, spec_b1, spec_w2, spec_b2, up_weight, down_weight):
    full_width = up_weight.shape[0]
    block_size = spec_w1.shape[2]
    cos_fwd, sin_fwd, cos_inv, sin_inv = padded_tables(inputs.shape[2], lax.axis_size("space"))
    values = inputs.astype(jnp.float32)
    cotangent_parts = ring_send(cotangent)
    first_sum, second_sum = token_sums(jnp.sum(values, axis=-1), jnp.sum(values * values, axis=-1))
    mean_one = first_sum[..., None] / full_width
    rstd_one = lax.rsqrt(second_sum[..., None] / full_width - mean_one * mean_one + EPSILON)
    normed = (values - mean_one) * rstd_one
    spec_real, spec_imag = enter_spectrum(
        lon_forward(normed, cos_fwd), lon_forward(normed, sin_fwd)
    )
    spec_shape = spec_real.shape
    bias_one = to_blocks(spec_b1, block_size)
    bias_two = to_blocks(spec_b2, block_size)
    first_real, first_imag = block_product(
        to_blocks(spec_real, block_size), to_blocks(spec_imag, block_size), spec_w1
    )
    first_real = jax.nn.relu(first_real + bias_one[0])
    first_imag = jax.nn.relu(first_imag + bias_one[1])
    second_real, second_imag = block_product(first_real, first_imag, spec_w2)
    second_real = second_real + bias_two[0]
    second_imag = second_imag + bias_two[1]
    shrunk_real = (second_real - jnp.clip(second_real, -SHRINK_LEVEL, SHRINK_LEVEL)).reshape(
        spec_shape
    )
    shrunk_imag = (second_imag - jnp.clip(second_imag, -SHRINK_LEVEL, SHRINK_LEVEL)).reshape(
        spec_shape
    )
    shrunk_real, shrunk_imag, cotangent_parts = lax.optimization_barrier(
        (shrunk_real, shrunk_imag, cotangent_parts)
    )
    whole_cotangent = ring_assemble(cotangent_parts)
    back_real, back_imag = leave_spectrum(shrunk_real, shrunk_imag)
    filtered = lon_back(back_real, cos_inv) + lon_back(back_imag, sin_inv)
    residual = (filtered + normed + values).astype(jnp.bfloat16)
    residual_vals = residual.astype(jnp.float32)
    whole_residual = lax.all_gather(residual, "feat", axis=3, tiled=True)
    whole_vals = whole_residual.astype(jnp.float32)
    mean_two = jnp.sum(whole_vals, axis=-1, keepdims=True) / full_width
    square_two = jnp.sum(whole_vals * whole_vals, axis=-1, keepdims=True) / full_width
    rstd_two = lax.rsqrt(square_two - mean_two * mean_two + EPSILON)
    vhat = (whole_vals - mean_two) * rstd_two
    hidden = jnp.einsum(
        "brwd,dh->brwh", vhat.astype(jnp.bfloat16), up_weight, preferred_element_type=jnp.float32
    )
    activated = gelu_value(hidden).astype(jnp.bfloat16)
    mixed_term = jnp.einsum(
        "brwh,hd->brwd", activated, down_weight, preferred_element_type=jnp.float32
    )
    output = (residual_vals + channel_share(mixed_term)).astype(jnp.bfloat16)
    grad_act = jnp.einsum(
        "brwd,hd->brwh", whole_cotangent, down_weight, preferred_element_type=jnp.float32
    )
    grad_hidden = (grad_act * gelu_slope(hidden)).astype(jnp.bfloat16)
    grad_term = jnp.einsum(
        "brwh,dh->brwd", grad_hidden, up_weight, preferred_element_type=jnp.float32
    )
    total_one, total_two = token_sums(
        jnp.sum(grad_term, axis=-1), jnp.sum(grad_term * vhat, axis=-1)
    )
    grad_vhat = channel_share(grad_term)
    own_hat = (residual_vals - mean_two) * rstd_two
    grad_residual = cotangent.astype(jnp.float32) + rstd_two * (
        grad_vhat
        - total_one[..., None] / full_width
        - own_hat * (total_two[..., None] / full_width)
    )
    grad_real, grad_imag = enter_spectrum(
        lon_forward(grad_residual, cos_inv), lon_forward(grad_residual, sin_inv)
    )
    grad_real = jnp.where(
        jnp.abs(second_real) > SHRINK_LEVEL, to_blocks(grad_real, block_size), 0.0
    )
    grad_imag = jnp.where(
        jnp.abs(second_imag) > SHRINK_LEVEL, to_blocks(grad_imag, block_size), 0.0
    )
    first_grad_real, first_grad_imag = block_adjoint(grad_real, grad_imag, spec_w2)
    first_grad_real = jnp.where(first_real > 0.0, first_grad_real, 0.0)
    first_grad_imag = jnp.where(first_imag > 0.0, first_grad_imag, 0.0)
    spec_grad_real, spec_grad_imag = block_adjoint(first_grad_real, first_grad_imag, spec_w1)
    rows_real, rows_imag = leave_spectrum(
        spec_grad_real.reshape(spec_shape), spec_grad_imag.reshape(spec_shape)
    )
    grad_normed = grad_residual + lon_back(rows_real, cos_fwd) + lon_back(rows_imag, sin_fwd)
    norm_one, norm_two = token_sums(
        jnp.sum(grad_normed, axis=-1), jnp.sum(grad_normed * normed, axis=-1)
    )
    grad_input = grad_residual + rstd_one * (
        grad_normed - norm_one[..., None] / full_width - normed * (norm_two[..., None] / full_width)
    )
    return (output, grad_input.astype(jnp.bfloat16))


def solution(mesh):
    return jax.shard_map(
        per_device,
        mesh=mesh,
        in_specs=(
            P(None, "space", None, "feat"),
            P(None, "space", None, "feat"),
            P(None, "feat", None, None),
            P(None, "feat"),
            P(None, "feat", None, None),
            P(None, "feat"),
            P(None, "feat"),
            P("feat", None),
        ),
        out_specs=(P(None, "space", None, "feat"), P(None, "space", None, "feat")),
        check_vma=False,
    )
```

```python
import math

import jax
import jax.numpy as jnp
from jax import lax
from jax.sharding import PartitionSpec as P

EPSILON = 1e-05
SHRINK_LEVEL = 0.1
HIGHEST = lax.Precision.HIGHEST


def longitude_tables(width_lon):
    mode_count = width_lon // 2 + 1
    cell_index = jnp.arange(width_lon, dtype=jnp.int32)[:, None]
    wave_number = jnp.arange(mode_count, dtype=jnp.int32)[None, :]
    phase_angle = (
        2.0 * math.pi / width_lon * (cell_index * wave_number % width_lon).astype(jnp.float32)
    )
    scaling = 1.0 / math.sqrt(width_lon)
    cos_fwd = jnp.cos(phase_angle) * scaling
    sin_fwd = -jnp.sin(phase_angle) * scaling
    doubled = jnp.where((wave_number == 0) | (wave_number * 2 == width_lon), 1.0, 2.0).astype(
        jnp.float32
    )
    return (cos_fwd, sin_fwd, cos_fwd * doubled, sin_fwd * doubled)


def padded_tables(width_lon, multiple):
    tables = longitude_tables(width_lon)
    modes = tables[0].shape[1]
    extra = -modes % multiple
    return tuple(jnp.pad(table, ((0, 0), (0, extra))) for table in tables)


def lat_apply(table, field):
    return jnp.einsum("gh,bhkc->bgkc", table, field, precision=HIGHEST)


def complex_latitude(table_cos, table_sin, real_part, imag_part, inverse):
    if inverse:
        return (
            lat_apply(table_cos, real_part) + lat_apply(table_sin, imag_part),
            lat_apply(table_cos, imag_part) - lat_apply(table_sin, real_part),
        )
    return (
        lat_apply(table_cos, real_part) - lat_apply(table_sin, imag_part),
        lat_apply(table_cos, imag_part) + lat_apply(table_sin, real_part),
    )


def lon_forward(field, table):
    return jnp.einsum("brwc,wk->brkc", field, table, precision=HIGHEST)


def lon_back(spec, table):
    return jnp.einsum("brkc,wk->brwc", spec, table, precision=HIGHEST)


def to_blocks(field, block_size):
    return field.reshape(field.shape[:-1] + (field.shape[-1] // block_size, block_size))


def block_mult(field, weights):
    return jnp.einsum("...nc,nce->...ne", field, weights, precision=HIGHEST)


def block_mult_back(field, weights):
    return jnp.einsum("...ne,nce->...nc", field, weights, precision=HIGHEST)


def block_product(real_part, imag_part, weights):
    return (
        block_mult(real_part, weights[0]) - block_mult(imag_part, weights[1]),
        block_mult(real_part, weights[1]) + block_mult(imag_part, weights[0]),
    )


def block_adjoint(real_part, imag_part, weights):
    return (
        block_mult_back(real_part, weights[0]) + block_mult_back(imag_part, weights[1]),
        block_mult_back(imag_part, weights[0]) - block_mult_back(real_part, weights[1]),
    )


def latitude_tables(length):
    index_row = jnp.arange(length, dtype=jnp.int32)
    phase_angle = (
        2.0 * math.pi / length * (index_row[:, None] * index_row[None, :] % length).astype(jnp.float32)
    )
    scaling = 1.0 / math.sqrt(length)
    return (jnp.cos(phase_angle) * scaling, -jnp.sin(phase_angle) * scaling)


def to_columns(real_part, imag_part):
    stacked = jnp.stack([real_part, imag_part])
    moved = lax.all_to_all(stacked, "space", 3, 2, tiled=True)
    return (moved[0], moved[1])


def to_rows(real_part, imag_part):
    stacked = jnp.stack([real_part, imag_part])
    moved = lax.all_to_all(stacked, "space", 2, 3, tiled=True)
    return (moved[0], moved[1])


def enter_spectrum(real_part, imag_part):
    length = real_part.shape[1] * lax.axis_size("space")
    table_cos, table_sin = latitude_tables(length)
    real_part, imag_part = to_columns(real_part, imag_part)
    return complex_latitude(table_cos, table_sin, real_part, imag_part, False)


def leave_spectrum(real_part, imag_part):
    table_cos, table_sin = latitude_tables(real_part.shape[1])
    real_part, imag_part = complex_latitude(table_cos, table_sin, real_part, imag_part, True)
    return to_rows(real_part, imag_part)


def token_sums(first_term, second_term):
    pair = jnp.stack([first_term, second_term])
    count = lax.axis_size("feat")
    bit = 1
    while bit < count:
        pair = pair + lax.ppermute(pair, "feat", [(i, i ^ bit) for i in range(count)])
        bit *= 2
    return (pair[0], pair[1])


def ring_gather(block):
    count = lax.axis_size("feat")
    parts = [block] + [
        lax.ppermute(block, "feat", [(i, (i + count - shift) % count) for i in range(count)])
        for shift in range(1, count)
    ]
    return jnp.concatenate(parts, axis=-1)


def ring_scatter(term):
    count = lax.axis_size("feat")
    width = term.shape[-1] // count
    chunks = [term[..., shift * width : (shift + 1) * width] for shift in range(count)]
    total = chunks[0]
    for shift in range(1, count):
        moved = lax.ppermute(
            chunks[shift].astype(jnp.bfloat16),
            "feat",
            [(i, (i + shift) % count) for i in range(count)],
        )
        total = total + moved.astype(jnp.float32)
    return total


def rotated_rows(weight, axis):
    count = lax.axis_size("feat")
    width = weight.shape[axis] // count
    doubled = jnp.concatenate([weight, weight], axis=axis)
    start = lax.axis_index("feat") * width
    return lax.dynamic_slice_in_dim(doubled, start, weight.shape[axis], axis=axis)


def channel_share(term):
    return lax.psum_scatter(
        term.astype(jnp.bfloat16), "feat", scatter_dimension=3, tiled=True
    ).astype(jnp.float32)


def gelu_value(field):
    return 0.5 * field * (1.0 + lax.erf(field * (1.0 / math.sqrt(2.0))))


def gelu_slope(field):
    return 0.5 * (1.0 + lax.erf(field * (1.0 / math.sqrt(2.0)))) + field * jnp.exp(
        -0.5 * field * field
    ) * (1.0 / math.sqrt(2.0 * math.pi))


def per_device(inputs, cotangent, spec_w1, spec_b1, spec_w2, spec_b2, up_weight, down_weight):
    full_width = up_weight.shape[0]
    block_size = spec_w1.shape[2]
    cos_fwd, sin_fwd, cos_inv, sin_inv = padded_tables(inputs.shape[2], lax.axis_size("space"))
    values = inputs.astype(jnp.float32)
    cotangent_rot = ring_gather(cotangent)
    up_rot = rotated_rows(up_weight, 0)
    down_rot = rotated_rows(down_weight, 1)
    first_sum, second_sum = token_sums(jnp.sum(values, axis=-1), jnp.sum(values * values, axis=-1))
    mean_one = first_sum[..., None] / full_width
    rstd_one = lax.rsqrt(second_sum[..., None] / full_width - mean_one * mean_one + EPSILON)
    normed = (values - mean_one) * rstd_one
    spec_real, spec_imag = enter_spectrum(
        lon_forward(normed, cos_fwd), lon_forward(normed, sin_fwd)
    )
    spec_shape = spec_real.shape
    bias_one = to_blocks(spec_b1, block_size)
    bias_two = to_blocks(spec_b2, block_size)
    first_real, first_imag = block_product(
        to_blocks(spec_real, block_size), to_blocks(spec_imag, block_size), spec_w1
    )
    first_real = jax.nn.relu(first_real + bias_one[0])
    first_imag = jax.nn.relu(first_imag + bias_one[1])
    second_real, second_imag = block_product(first_real, first_imag, spec_w2)
    second_real = second_real + bias_two[0]
    second_imag = second_imag + bias_two[1]
    shrunk_real = (second_real - jnp.clip(second_real, -SHRINK_LEVEL, SHRINK_LEVEL)).reshape(
        spec_shape
    )
    shrunk_imag = (second_imag - jnp.clip(second_imag, -SHRINK_LEVEL, SHRINK_LEVEL)).reshape(
        spec_shape
    )
    shrunk_real, shrunk_imag, cotangent_rot, up_rot, down_rot = lax.optimization_barrier(
        (shrunk_real, shrunk_imag, cotangent_rot, up_rot, down_rot)
    )
    back_real, back_imag = leave_spectrum(shrunk_real, shrunk_imag)
    filtered = lon_back(back_real, cos_inv) + lon_back(back_imag, sin_inv)
    residual = (filtered + normed + values).astype(jnp.bfloat16)
    residual_vals = residual.astype(jnp.float32)
    whole_vals = ring_gather(residual).astype(jnp.float32)
    mean_two = jnp.sum(whole_vals, axis=-1, keepdims=True) / full_width
    square_two = jnp.sum(whole_vals * whole_vals, axis=-1, keepdims=True) / full_width
    rstd_two = lax.rsqrt(square_two - mean_two * mean_two + EPSILON)
    vhat = (whole_vals - mean_two) * rstd_two
    hidden = jnp.einsum(
        "brwd,dh->brwh", vhat.astype(jnp.bfloat16), up_rot, preferred_element_type=jnp.float32
    )
    activated = gelu_value(hidden).astype(jnp.bfloat16)
    mixed_term = jnp.einsum(
        "brwh,hd->brwd", activated, down_weight, preferred_element_type=jnp.float32
    )
    output = (residual_vals + channel_share(mixed_term)).astype(jnp.bfloat16)
    grad_act = jnp.einsum(
        "brwd,hd->brwh", cotangent_rot, down_rot, preferred_element_type=jnp.float32
    )
    grad_hidden = (grad_act * gelu_slope(hidden)).astype(jnp.bfloat16)
    grad_term = jnp.einsum(
        "brwh,dh->brwd", grad_hidden, up_rot, preferred_element_type=jnp.float32
    )
    total_one, total_two = token_sums(
        jnp.sum(grad_term, axis=-1), jnp.sum(grad_term * vhat, axis=-1)
    )
    grad_vhat = ring_scatter(grad_term)
    own_hat = (residual_vals - mean_two) * rstd_two
    grad_residual = cotangent.astype(jnp.float32) + rstd_two * (
        grad_vhat
        - total_one[..., None] / full_width
        - own_hat * (total_two[..., None] / full_width)
    )
    grad_real, grad_imag = enter_spectrum(
        lon_forward(grad_residual, cos_inv), lon_forward(grad_residual, sin_inv)
    )
    grad_real = jnp.where(
        jnp.abs(second_real) > SHRINK_LEVEL, to_blocks(grad_real, block_size), 0.0
    )
    grad_imag = jnp.where(
        jnp.abs(second_imag) > SHRINK_LEVEL, to_blocks(grad_imag, block_size), 0.0
    )
    first_grad_real, first_grad_imag = block_adjoint(grad_real, grad_imag, spec_w2)
    first_grad_real = jnp.where(first_real > 0.0, first_grad_real, 0.0)
    first_grad_imag = jnp.where(first_imag > 0.0, first_grad_imag, 0.0)
    spec_grad_real, spec_grad_imag = block_adjoint(first_grad_real, first_grad_imag, spec_w1)
    rows_real, rows_imag = leave_spectrum(
        spec_grad_real.reshape(spec_shape), spec_grad_imag.reshape(spec_shape)
    )
    grad_normed = grad_residual + lon_back(rows_real, cos_fwd) + lon_back(rows_imag, sin_fwd)
    norm_one, norm_two = token_sums(
        jnp.sum(grad_normed, axis=-1), jnp.sum(grad_normed * normed, axis=-1)
    )
    grad_input = grad_residual + rstd_one * (
        grad_normed - norm_one[..., None] / full_width - normed * (norm_two[..., None] / full_width)
    )
    return (output, grad_input.astype(jnp.bfloat16))


def solution(mesh):
    return jax.shard_map(
        per_device,
        mesh=mesh,
        in_specs=(
            P(None, "space", None, "feat"),
            P(None, "space", None, "feat"),
            P(None, "feat", None, None),
            P(None, "feat"),
            P(None, "feat", None, None),
            P(None, "feat"),
            P(None, "feat"),
            P("feat", None),
        ),
        out_specs=(P(None, "space", None, "feat"), P(None, "space", None, "feat")),
        check_vma=False,
    )
```

```python
import math

import jax
import jax.numpy as jnp
from jax import lax
from jax.sharding import PartitionSpec as P

EPSILON = 1e-05
SHRINK_LEVEL = 0.1
HIGHEST = lax.Precision.HIGHEST


def longitude_tables(width_lon):
    mode_count = width_lon // 2 + 1
    cell_index = jnp.arange(width_lon, dtype=jnp.int32)[:, None]
    wave_number = jnp.arange(mode_count, dtype=jnp.int32)[None, :]
    phase_angle = (
        2.0 * math.pi / width_lon * (cell_index * wave_number % width_lon).astype(jnp.float32)
    )
    scaling = 1.0 / math.sqrt(width_lon)
    cos_fwd = jnp.cos(phase_angle) * scaling
    sin_fwd = -jnp.sin(phase_angle) * scaling
    doubled = jnp.where((wave_number == 0) | (wave_number * 2 == width_lon), 1.0, 2.0).astype(
        jnp.float32
    )
    return (cos_fwd, sin_fwd, cos_fwd * doubled, sin_fwd * doubled)


def padded_tables(width_lon, multiple):
    tables = longitude_tables(width_lon)
    modes = tables[0].shape[1]
    extra = -modes % multiple
    return tuple(jnp.pad(table, ((0, 0), (0, extra))) for table in tables)


def lat_apply(table, field):
    return jnp.einsum("gh,bhkc->bgkc", table, field, precision=HIGHEST)


def complex_latitude(table_cos, table_sin, real_part, imag_part, inverse):
    if inverse:
        return (
            lat_apply(table_cos, real_part) + lat_apply(table_sin, imag_part),
            lat_apply(table_cos, imag_part) - lat_apply(table_sin, real_part),
        )
    return (
        lat_apply(table_cos, real_part) - lat_apply(table_sin, imag_part),
        lat_apply(table_cos, imag_part) + lat_apply(table_sin, real_part),
    )


def lon_forward(field, table):
    return jnp.einsum("brwc,wk->brkc", field, table, precision=HIGHEST)


def lon_back(spec, table):
    return jnp.einsum("brkc,wk->brwc", spec, table, precision=HIGHEST)


def to_blocks(field, block_size):
    return field.reshape(field.shape[:-1] + (field.shape[-1] // block_size, block_size))


def block_mult(field, weights):
    return jnp.einsum("...nc,nce->...ne", field, weights, precision=HIGHEST)


def block_mult_back(field, weights):
    return jnp.einsum("...ne,nce->...nc", field, weights, precision=HIGHEST)


def block_product(real_part, imag_part, weights):
    return (
        block_mult(real_part, weights[0]) - block_mult(imag_part, weights[1]),
        block_mult(real_part, weights[1]) + block_mult(imag_part, weights[0]),
    )


def block_adjoint(real_part, imag_part, weights):
    return (
        block_mult_back(real_part, weights[0]) + block_mult_back(imag_part, weights[1]),
        block_mult_back(imag_part, weights[0]) - block_mult_back(real_part, weights[1]),
    )


def latitude_tables(length):
    index_row = jnp.arange(length, dtype=jnp.int32)
    phase_angle = (
        2.0 * math.pi / length * (index_row[:, None] * index_row[None, :] % length).astype(jnp.float32)
    )
    scaling = 1.0 / math.sqrt(length)
    return (jnp.cos(phase_angle) * scaling, -jnp.sin(phase_angle) * scaling)


def to_columns(real_part, imag_part):
    stacked = jnp.stack([real_part, imag_part])
    moved = lax.all_to_all(stacked, "space", 3, 2, tiled=True)
    return (moved[0], moved[1])


def to_rows(real_part, imag_part):
    stacked = jnp.stack([real_part, imag_part])
    moved = lax.all_to_all(stacked, "space", 2, 3, tiled=True)
    return (moved[0], moved[1])


def enter_spectrum(real_part, imag_part):
    length = real_part.shape[1] * lax.axis_size("space")
    table_cos, table_sin = latitude_tables(length)
    real_part, imag_part = to_columns(real_part, imag_part)
    return complex_latitude(table_cos, table_sin, real_part, imag_part, False)


def leave_spectrum(real_part, imag_part):
    table_cos, table_sin = latitude_tables(real_part.shape[1])
    real_part, imag_part = complex_latitude(table_cos, table_sin, real_part, imag_part, True)
    return to_rows(real_part, imag_part)


def token_sums(first_term, second_term):
    pair = jnp.stack([first_term, second_term])
    count = lax.axis_size("feat")
    bit = 1
    while bit < count:
        pair = pair + lax.ppermute(pair, "feat", [(i, i ^ bit) for i in range(count)])
        bit *= 2
    return (pair[0], pair[1])


def ring_send(block):
    count = lax.axis_size("feat")
    return [block] + [
        lax.ppermute(block, "feat", [(i, (i + shift) % count) for i in range(count)])
        for shift in range(1, count)
    ]


def ring_assemble(parts):
    count = len(parts)
    position = lax.axis_index("feat")
    block = parts[0]
    width = block.shape[-1]
    whole = jnp.zeros(block.shape[:-1] + (width * count,), block.dtype)
    for shift, moved in enumerate(parts):
        source = (position + count - shift) % count
        whole = lax.dynamic_update_slice_in_dim(whole, moved, source * width, axis=block.ndim - 1)
    return whole


def channel_share(term):
    return lax.psum_scatter(
        term.astype(jnp.bfloat16), "feat", scatter_dimension=3, tiled=True
    ).astype(jnp.float32)


def gelu_value(field):
    return 0.5 * field * (1.0 + lax.erf(field * (1.0 / math.sqrt(2.0))))


def gelu_slope(field):
    return 0.5 * (1.0 + lax.erf(field * (1.0 / math.sqrt(2.0)))) + field * jnp.exp(
        -0.5 * field * field
    ) * (1.0 / math.sqrt(2.0 * math.pi))


def spectral_forward(field, spec_w1, spec_b1, spec_w2, spec_b2, cos_fwd, sin_fwd):
    block_size = spec_w1.shape[2]
    spec_real, spec_imag = enter_spectrum(lon_forward(field, cos_fwd), lon_forward(field, sin_fwd))
    spec_shape = spec_real.shape
    bias_one = to_blocks(spec_b1, block_size)
    bias_two = to_blocks(spec_b2, block_size)
    first_real, first_imag = block_product(
        to_blocks(spec_real, block_size), to_blocks(spec_imag, block_size), spec_w1
    )
    first_real = jax.nn.relu(first_real + bias_one[0])
    first_imag = jax.nn.relu(first_imag + bias_one[1])
    second_real, second_imag = block_product(first_real, first_imag, spec_w2)
    second_real = second_real + bias_two[0]
    second_imag = second_imag + bias_two[1]
    shrunk_real = (second_real - jnp.clip(second_real, -SHRINK_LEVEL, SHRINK_LEVEL)).reshape(
        spec_shape
    )
    shrunk_imag = (second_imag - jnp.clip(second_imag, -SHRINK_LEVEL, SHRINK_LEVEL)).reshape(
        spec_shape
    )
    back = complex_latitude_inverse(shrunk_real, shrunk_imag)
    return back, (first_real, first_imag, second_real, second_imag)


def complex_latitude_inverse(real_part, imag_part):
    table_cos, table_sin = latitude_tables(real_part.shape[1])
    return complex_latitude(table_cos, table_sin, real_part, imag_part, True)


def spectral_leave(back, cos_inv, sin_inv):
    back_real, back_imag = to_rows(*back)
    return lon_back(back_real, cos_inv) + lon_back(back_imag, sin_inv)


def spectral_backward(grad_field, saved, spec_w1, spec_w2, cos_fwd, sin_fwd, cos_inv, sin_inv):
    block_size = spec_w1.shape[2]
    first_real, first_imag, second_real, second_imag = saved
    grad_real, grad_imag = enter_spectrum(
        lon_forward(grad_field, cos_inv), lon_forward(grad_field, sin_inv)
    )
    spec_shape = grad_real.shape
    grad_real = jnp.where(
        jnp.abs(second_real) > SHRINK_LEVEL, to_blocks(grad_real, block_size), 0.0
    )
    grad_imag = jnp.where(
        jnp.abs(second_imag) > SHRINK_LEVEL, to_blocks(grad_imag, block_size), 0.0
    )
    first_grad_real, first_grad_imag = block_adjoint(grad_real, grad_imag, spec_w2)
    first_grad_real = jnp.where(first_real > 0.0, first_grad_real, 0.0)
    first_grad_imag = jnp.where(first_imag > 0.0, first_grad_imag, 0.0)
    spec_grad_real, spec_grad_imag = block_adjoint(first_grad_real, first_grad_imag, spec_w1)
    rows_real, rows_imag = leave_spectrum(
        spec_grad_real.reshape(spec_shape), spec_grad_imag.reshape(spec_shape)
    )
    return lon_back(rows_real, cos_fwd) + lon_back(rows_imag, sin_fwd)


def per_device(inputs, cotangent, spec_w1, spec_b1, spec_w2, spec_b2, up_weight, down_weight):
    full_width = up_weight.shape[0]
    block_size = spec_w1.shape[2]
    cos_fwd, sin_fwd, cos_inv, sin_inv = padded_tables(inputs.shape[2], lax.axis_size("space"))
    values = inputs.astype(jnp.float32)
    cotangent_parts = ring_send(cotangent)
    first_sum, second_sum = token_sums(jnp.sum(values, axis=-1), jnp.sum(values * values, axis=-1))
    mean_one = first_sum[..., None] / full_width
    rstd_one = lax.rsqrt(second_sum[..., None] / full_width - mean_one * mean_one + EPSILON)
    normed = (values - mean_one) * rstd_one
    block_count = spec_w1.shape[1]
    shrunk_parts, saved_parts = [], []
    for block in range(block_count):
        channels = slice(block * block_size, (block + 1) * block_size)
        shrunk, saved = spectral_forward(
            normed[..., channels],
            spec_w1[:, block : block + 1],
            spec_b1[:, channels],
            spec_w2[:, block : block + 1],
            spec_b2[:, channels],
            cos_fwd,
            sin_fwd,
        )
        shrunk_parts.append(shrunk)
        saved_parts.append(saved)
    shrunk_parts[-1], cotangent_parts = lax.optimization_barrier(
        (shrunk_parts[-1], cotangent_parts)
    )
    whole_cotangent = ring_assemble(cotangent_parts)
    filtered = jnp.concatenate(
        [spectral_leave(shrunk, cos_inv, sin_inv) for shrunk in shrunk_parts], axis=-1
    )
    residual = (filtered + normed + values).astype(jnp.bfloat16)
    residual_vals = residual.astype(jnp.float32)
    whole_residual = lax.all_gather(residual, "feat", axis=3, tiled=True)
    whole_vals = whole_residual.astype(jnp.float32)
    mean_two = jnp.sum(whole_vals, axis=-1, keepdims=True) / full_width
    square_two = jnp.sum(whole_vals * whole_vals, axis=-1, keepdims=True) / full_width
    rstd_two = lax.rsqrt(square_two - mean_two * mean_two + EPSILON)
    vhat = (whole_vals - mean_two) * rstd_two
    hidden = jnp.einsum(
        "brwd,dh->brwh", vhat.astype(jnp.bfloat16), up_weight, preferred_element_type=jnp.float32
    )
    activated = gelu_value(hidden).astype(jnp.bfloat16)
    mixed_term = jnp.einsum(
        "brwh,hd->brwd", activated, down_weight, preferred_element_type=jnp.float32
    )
    output = (residual_vals + channel_share(mixed_term)).astype(jnp.bfloat16)
    grad_act = jnp.einsum(
        "brwd,hd->brwh", whole_cotangent, down_weight, preferred_element_type=jnp.float32
    )
    grad_hidden = (grad_act * gelu_slope(hidden)).astype(jnp.bfloat16)
    grad_term = jnp.einsum(
        "brwh,dh->brwd", grad_hidden, up_weight, preferred_element_type=jnp.float32
    )
    total_one, total_two = token_sums(
        jnp.sum(grad_term, axis=-1), jnp.sum(grad_term * vhat, axis=-1)
    )
    grad_vhat = channel_share(grad_term)
    own_hat = (residual_vals - mean_two) * rstd_two
    grad_residual = cotangent.astype(jnp.float32) + rstd_two * (
        grad_vhat
        - total_one[..., None] / full_width
        - own_hat * (total_two[..., None] / full_width)
    )
    grad_filter = jnp.concatenate(
        [
            spectral_backward(
                grad_residual[..., block * block_size : (block + 1) * block_size],
                saved_parts[block],
                spec_w1[:, block : block + 1],
                spec_w2[:, block : block + 1],
                cos_fwd,
                sin_fwd,
                cos_inv,
                sin_inv,
            )
            for block in range(block_count)
        ],
        axis=-1,
    )
    grad_normed = grad_residual + grad_filter
    norm_one, norm_two = token_sums(
        jnp.sum(grad_normed, axis=-1), jnp.sum(grad_normed * normed, axis=-1)
    )
    grad_input = grad_residual + rstd_one * (
        grad_normed - norm_one[..., None] / full_width - normed * (norm_two[..., None] / full_width)
    )
    return (output, grad_input.astype(jnp.bfloat16))


def solution(mesh):
    return jax.shard_map(
        per_device,
        mesh=mesh,
        in_specs=(
            P(None, "space", None, "feat"),
            P(None, "space", None, "feat"),
            P(None, "feat", None, None),
            P(None, "feat"),
            P(None, "feat", None, None),
            P(None, "feat"),
            P(None, "feat"),
            P("feat", None),
        ),
        out_specs=(P(None, "space", None, "feat"), P(None, "space", None, "feat")),
        check_vma=False,
    )
```

```python
import math

import jax
import jax.numpy as jnp
from jax import lax
from jax.sharding import PartitionSpec as P

EPSILON = 1e-05
SHRINK_LEVEL = 0.1
HIGHEST = lax.Precision.HIGHEST


def longitude_tables(width_lon):
    mode_count = width_lon // 2 + 1
    cell_index = jnp.arange(width_lon, dtype=jnp.int32)[:, None]
    wave_number = jnp.arange(mode_count, dtype=jnp.int32)[None, :]
    phase_angle = (
        2.0 * math.pi / width_lon * (cell_index * wave_number % width_lon).astype(jnp.float32)
    )
    scaling = 1.0 / math.sqrt(width_lon)
    cos_fwd = jnp.cos(phase_angle) * scaling
    sin_fwd = -jnp.sin(phase_angle) * scaling
    doubled = jnp.where((wave_number == 0) | (wave_number * 2 == width_lon), 1.0, 2.0).astype(
        jnp.float32
    )
    return (cos_fwd, sin_fwd, cos_fwd * doubled, sin_fwd * doubled)


def padded_tables(width_lon, multiple):
    tables = longitude_tables(width_lon)
    modes = tables[0].shape[1]
    extra = -modes % multiple
    return tuple(jnp.pad(table, ((0, 0), (0, extra))) for table in tables)


def lat_apply(table, field):
    return jnp.einsum("gh,bhkc->bgkc", table, field, precision=HIGHEST)


def complex_latitude(table_cos, table_sin, real_part, imag_part, inverse):
    if inverse:
        return (
            lat_apply(table_cos, real_part) + lat_apply(table_sin, imag_part),
            lat_apply(table_cos, imag_part) - lat_apply(table_sin, real_part),
        )
    return (
        lat_apply(table_cos, real_part) - lat_apply(table_sin, imag_part),
        lat_apply(table_cos, imag_part) + lat_apply(table_sin, real_part),
    )


def lon_forward(field, table):
    return jnp.einsum("brwc,wk->brkc", field, table, precision=HIGHEST)


def lon_back(spec, table):
    return jnp.einsum("brkc,wk->brwc", spec, table, precision=HIGHEST)


def to_blocks(field, block_size):
    return field.reshape(field.shape[:-1] + (field.shape[-1] // block_size, block_size))


def block_mult(field, weights):
    return jnp.einsum("...nc,nce->...ne", field, weights, precision=HIGHEST)


def block_mult_back(field, weights):
    return jnp.einsum("...ne,nce->...nc", field, weights, precision=HIGHEST)


def block_product(real_part, imag_part, weights):
    return (
        block_mult(real_part, weights[0]) - block_mult(imag_part, weights[1]),
        block_mult(real_part, weights[1]) + block_mult(imag_part, weights[0]),
    )


def block_adjoint(real_part, imag_part, weights):
    return (
        block_mult_back(real_part, weights[0]) + block_mult_back(imag_part, weights[1]),
        block_mult_back(imag_part, weights[0]) - block_mult_back(real_part, weights[1]),
    )


def latitude_tables(length):
    index_row = jnp.arange(length, dtype=jnp.int32)
    phase_angle = (
        2.0 * math.pi / length * (index_row[:, None] * index_row[None, :] % length).astype(jnp.float32)
    )
    scaling = 1.0 / math.sqrt(length)
    return (jnp.cos(phase_angle) * scaling, -jnp.sin(phase_angle) * scaling)


def to_columns(real_part, imag_part):
    stacked = jnp.stack([real_part, imag_part])
    moved = lax.all_to_all(stacked, "space", 3, 2, tiled=True)
    return (moved[0], moved[1])


def to_rows(real_part, imag_part):
    stacked = jnp.stack([real_part, imag_part])
    moved = lax.all_to_all(stacked, "space", 2, 3, tiled=True)
    return (moved[0], moved[1])


def enter_spectrum(real_part, imag_part):
    length = real_part.shape[1] * lax.axis_size("space")
    table_cos, table_sin = latitude_tables(length)
    real_part, imag_part = to_columns(real_part, imag_part)
    return complex_latitude(table_cos, table_sin, real_part, imag_part, False)


def leave_spectrum(real_part, imag_part):
    table_cos, table_sin = latitude_tables(real_part.shape[1])
    real_part, imag_part = complex_latitude(table_cos, table_sin, real_part, imag_part, True)
    return to_rows(real_part, imag_part)


def token_sums(first_term, second_term):
    pair = jnp.stack([first_term, second_term])
    count = lax.axis_size("feat")
    position = lax.axis_index("feat")
    shifted = jnp.stack(
        [pair]
        + [
            lax.ppermute(pair, "feat", [(i, (i + count - shift) % count) for i in range(count)])
            for shift in range(1, count)
        ]
    )
    ordered = shifted[(jnp.arange(count) + count - position) % count]
    total = ordered[0]
    for source in range(1, count):
        total = total + ordered[source]
    return (total[0], total[1])


def ring_send(block):
    count = lax.axis_size("feat")
    return [block] + [
        lax.ppermute(block, "feat", [(i, (i + shift) % count) for i in range(count)])
        for shift in range(1, count)
    ]


def ring_assemble(parts):
    count = len(parts)
    position = lax.axis_index("feat")
    block = parts[0]
    width = block.shape[-1]
    whole = jnp.zeros(block.shape[:-1] + (width * count,), block.dtype)
    for shift, moved in enumerate(parts):
        source = (position + count - shift) % count
        whole = lax.dynamic_update_slice_in_dim(whole, moved, source * width, axis=block.ndim - 1)
    return whole


def channel_share(term):
    return lax.psum_scatter(
        term.astype(jnp.bfloat16), "feat", scatter_dimension=3, tiled=True
    ).astype(jnp.float32)


def gelu_value(field):
    return 0.5 * field * (1.0 + lax.erf(field * (1.0 / math.sqrt(2.0))))


def gelu_slope(field):
    return 0.5 * (1.0 + lax.erf(field * (1.0 / math.sqrt(2.0)))) + field * jnp.exp(
        -0.5 * field * field
    ) * (1.0 / math.sqrt(2.0 * math.pi))


def per_device(inputs, cotangent, spec_w1, spec_b1, spec_w2, spec_b2, up_weight, down_weight):
    full_width = up_weight.shape[0]
    block_size = spec_w1.shape[2]
    cos_fwd, sin_fwd, cos_inv, sin_inv = padded_tables(inputs.shape[2], lax.axis_size("space"))
    values = inputs.astype(jnp.float32)
    cotangent_parts = ring_send(cotangent)
    first_sum, second_sum = token_sums(jnp.sum(values, axis=-1), jnp.sum(values * values, axis=-1))
    mean_one = first_sum[..., None] / full_width
    rstd_one = lax.rsqrt(second_sum[..., None] / full_width - mean_one * mean_one + EPSILON)
    normed = (values - mean_one) * rstd_one
    spec_real, spec_imag = enter_spectrum(
        lon_forward(normed, cos_fwd), lon_forward(normed, sin_fwd)
    )
    spec_shape = spec_real.shape
    bias_one = to_blocks(spec_b1, block_size)
    bias_two = to_blocks(spec_b2, block_size)
    first_real, first_imag = block_product(
        to_blocks(spec_real, block_size), to_blocks(spec_imag, block_size), spec_w1
    )
    first_real = jax.nn.relu(first_real + bias_one[0])
    first_imag = jax.nn.relu(first_imag + bias_one[1])
    second_real, second_imag = block_product(first_real, first_imag, spec_w2)
    second_real = second_real + bias_two[0]
    second_imag = second_imag + bias_two[1]
    shrunk_real = (second_real - jnp.clip(second_real, -SHRINK_LEVEL, SHRINK_LEVEL)).reshape(
        spec_shape
    )
    shrunk_imag = (second_imag - jnp.clip(second_imag, -SHRINK_LEVEL, SHRINK_LEVEL)).reshape(
        spec_shape
    )
    shrunk_real, shrunk_imag, cotangent_parts = lax.optimization_barrier(
        (shrunk_real, shrunk_imag, cotangent_parts)
    )
    whole_cotangent = ring_assemble(cotangent_parts)
    back_real, back_imag = leave_spectrum(shrunk_real, shrunk_imag)
    filtered = lon_back(back_real, cos_inv) + lon_back(back_imag, sin_inv)
    residual = (filtered + normed + values).astype(jnp.bfloat16)
    residual_vals = residual.astype(jnp.float32)
    whole_residual = lax.all_gather(residual, "feat", axis=3, tiled=True)
    whole_vals = whole_residual.astype(jnp.float32)
    mean_two = jnp.sum(whole_vals, axis=-1, keepdims=True) / full_width
    square_two = jnp.sum(whole_vals * whole_vals, axis=-1, keepdims=True) / full_width
    rstd_two = lax.rsqrt(square_two - mean_two * mean_two + EPSILON)
    vhat = (whole_vals - mean_two) * rstd_two
    hidden = jnp.einsum(
        "brwd,dh->brwh", vhat.astype(jnp.bfloat16), up_weight, preferred_element_type=jnp.float32
    )
    activated = gelu_value(hidden).astype(jnp.bfloat16)
    mixed_term = jnp.einsum(
        "brwh,hd->brwd", activated, down_weight, preferred_element_type=jnp.float32
    )
    output = (residual_vals + channel_share(mixed_term)).astype(jnp.bfloat16)
    grad_act = jnp.einsum(
        "brwd,hd->brwh", whole_cotangent, down_weight, preferred_element_type=jnp.float32
    )
    grad_hidden = (grad_act * gelu_slope(hidden)).astype(jnp.bfloat16)
    grad_term = jnp.einsum(
        "brwh,dh->brwd", grad_hidden, up_weight, preferred_element_type=jnp.float32
    )
    total_one, total_two = token_sums(
        jnp.sum(grad_term, axis=-1), jnp.sum(grad_term * vhat, axis=-1)
    )
    grad_vhat = channel_share(grad_term)
    own_hat = (residual_vals - mean_two) * rstd_two
    grad_residual = cotangent.astype(jnp.float32) + rstd_two * (
        grad_vhat
        - total_one[..., None] / full_width
        - own_hat * (total_two[..., None] / full_width)
    )
    grad_real, grad_imag = enter_spectrum(
        lon_forward(grad_residual, cos_inv), lon_forward(grad_residual, sin_inv)
    )
    grad_real = jnp.where(
        jnp.abs(second_real) > SHRINK_LEVEL, to_blocks(grad_real, block_size), 0.0
    )
    grad_imag = jnp.where(
        jnp.abs(second_imag) > SHRINK_LEVEL, to_blocks(grad_imag, block_size), 0.0
    )
    first_grad_real, first_grad_imag = block_adjoint(grad_real, grad_imag, spec_w2)
    first_grad_real = jnp.where(first_real > 0.0, first_grad_real, 0.0)
    first_grad_imag = jnp.where(first_imag > 0.0, first_grad_imag, 0.0)
    spec_grad_real, spec_grad_imag = block_adjoint(first_grad_real, first_grad_imag, spec_w1)
    rows_real, rows_imag = leave_spectrum(
        spec_grad_real.reshape(spec_shape), spec_grad_imag.reshape(spec_shape)
    )
    grad_normed = grad_residual + lon_back(rows_real, cos_fwd) + lon_back(rows_imag, sin_fwd)
    norm_one, norm_two = token_sums(
        jnp.sum(grad_normed, axis=-1), jnp.sum(grad_normed * normed, axis=-1)
    )
    grad_input = grad_residual + rstd_one * (
        grad_normed - norm_one[..., None] / full_width - normed * (norm_two[..., None] / full_width)
    )
    return (output, grad_input.astype(jnp.bfloat16))


def solution(mesh):
    return jax.shard_map(
        per_device,
        mesh=mesh,
        in_specs=(
            P(None, "space", None, "feat"),
            P(None, "space", None, "feat"),
            P(None, "feat", None, None),
            P(None, "feat"),
            P(None, "feat", None, None),
            P(None, "feat"),
            P(None, "feat"),
            P("feat", None),
        ),
        out_specs=(P(None, "space", None, "feat"), P(None, "space", None, "feat")),
        check_vma=False,
    )
```

```python
import math

import jax
import jax.numpy as jnp
from jax import lax
from jax.sharding import PartitionSpec as P

EPSILON = 1e-05
SHRINK_LEVEL = 0.1
HIGHEST = lax.Precision.HIGHEST


def longitude_tables(width_lon):
    mode_count = width_lon // 2 + 1
    cell_index = jnp.arange(width_lon, dtype=jnp.int32)[:, None]
    wave_number = jnp.arange(mode_count, dtype=jnp.int32)[None, :]
    phase_angle = (
        2.0 * math.pi / width_lon * (cell_index * wave_number % width_lon).astype(jnp.float32)
    )
    scaling = 1.0 / math.sqrt(width_lon)
    cos_fwd = jnp.cos(phase_angle) * scaling
    sin_fwd = -jnp.sin(phase_angle) * scaling
    doubled = jnp.where((wave_number == 0) | (wave_number * 2 == width_lon), 1.0, 2.0).astype(
        jnp.float32
    )
    return (cos_fwd, sin_fwd, cos_fwd * doubled, sin_fwd * doubled)


def padded_tables(width_lon, multiple):
    tables = longitude_tables(width_lon)
    modes = tables[0].shape[1]
    extra = -modes % multiple
    return tuple(jnp.pad(table, ((0, 0), (0, extra))) for table in tables)


def lat_apply(table, field):
    return jnp.einsum("gh,bhkc->bgkc", table, field, precision=HIGHEST)


def complex_latitude(table_cos, table_sin, real_part, imag_part, inverse):
    if inverse:
        return (
            lat_apply(table_cos, real_part) + lat_apply(table_sin, imag_part),
            lat_apply(table_cos, imag_part) - lat_apply(table_sin, real_part),
        )
    return (
        lat_apply(table_cos, real_part) - lat_apply(table_sin, imag_part),
        lat_apply(table_cos, imag_part) + lat_apply(table_sin, real_part),
    )


def lon_forward(field, table):
    return jnp.einsum("brwc,wk->brkc", field, table, precision=HIGHEST)


def lon_back(spec, table):
    return jnp.einsum("brkc,wk->brwc", spec, table, precision=HIGHEST)


def to_blocks(field, block_size):
    return field.reshape(field.shape[:-1] + (field.shape[-1] // block_size, block_size))


def block_mult(field, weights):
    return jnp.einsum("...nc,nce->...ne", field, weights, precision=HIGHEST)


def block_mult_back(field, weights):
    return jnp.einsum("...ne,nce->...nc", field, weights, precision=HIGHEST)


def block_product(real_part, imag_part, weights):
    return (
        block_mult(real_part, weights[0]) - block_mult(imag_part, weights[1]),
        block_mult(real_part, weights[1]) + block_mult(imag_part, weights[0]),
    )


def block_adjoint(real_part, imag_part, weights):
    return (
        block_mult_back(real_part, weights[0]) + block_mult_back(imag_part, weights[1]),
        block_mult_back(imag_part, weights[0]) - block_mult_back(real_part, weights[1]),
    )


def latitude_tables(length):
    index_row = jnp.arange(length, dtype=jnp.int32)
    phase_angle = (
        2.0 * math.pi / length * (index_row[:, None] * index_row[None, :] % length).astype(jnp.float32)
    )
    scaling = 1.0 / math.sqrt(length)
    return (jnp.cos(phase_angle) * scaling, -jnp.sin(phase_angle) * scaling)


def to_columns(real_part, imag_part, link_type):
    stacked = jnp.stack([real_part, imag_part]).astype(link_type)
    moved = lax.all_to_all(stacked, "space", 3, 2, tiled=True).astype(jnp.float32)
    return (moved[0], moved[1])


def to_rows(real_part, imag_part, link_type):
    stacked = jnp.stack([real_part, imag_part]).astype(link_type)
    moved = lax.all_to_all(stacked, "space", 2, 3, tiled=True).astype(jnp.float32)
    return (moved[0], moved[1])


def enter_spectrum(real_part, imag_part, link_type=jnp.float32):
    length = real_part.shape[1] * lax.axis_size("space")
    table_cos, table_sin = latitude_tables(length)
    real_part, imag_part = to_columns(real_part, imag_part, link_type)
    return complex_latitude(table_cos, table_sin, real_part, imag_part, False)


def leave_spectrum(real_part, imag_part, link_type=jnp.float32):
    table_cos, table_sin = latitude_tables(real_part.shape[1])
    real_part, imag_part = complex_latitude(table_cos, table_sin, real_part, imag_part, True)
    return to_rows(real_part, imag_part, link_type)


def token_sums(first_term, second_term):
    pair = jnp.stack([first_term, second_term])
    count = lax.axis_size("feat")
    position = lax.axis_index("feat")
    shifted = jnp.stack(
        [pair]
        + [
            lax.ppermute(pair, "feat", [(i, (i + count - shift) % count) for i in range(count)])
            for shift in range(1, count)
        ]
    )
    ordered = shifted[(jnp.arange(count) + count - position) % count]
    total = ordered[0]
    for source in range(1, count):
        total = total + ordered[source]
    return (total[0], total[1])


def ring_send(block):
    count = lax.axis_size("feat")
    return [block] + [
        lax.ppermute(block, "feat", [(i, (i + shift) % count) for i in range(count)])
        for shift in range(1, count)
    ]


def ring_assemble(parts):
    count = len(parts)
    position = lax.axis_index("feat")
    block = parts[0]
    width = block.shape[-1]
    whole = jnp.zeros(block.shape[:-1] + (width * count,), block.dtype)
    for shift, moved in enumerate(parts):
        source = (position + count - shift) % count
        whole = lax.dynamic_update_slice_in_dim(whole, moved, source * width, axis=block.ndim - 1)
    return whole


def channel_share(term):
    return lax.psum_scatter(
        term.astype(jnp.bfloat16), "feat", scatter_dimension=3, tiled=True
    ).astype(jnp.float32)


def gelu_value(field):
    return 0.5 * field * (1.0 + lax.erf(field * (1.0 / math.sqrt(2.0))))


def gelu_slope(field):
    return 0.5 * (1.0 + lax.erf(field * (1.0 / math.sqrt(2.0)))) + field * jnp.exp(
        -0.5 * field * field
    ) * (1.0 / math.sqrt(2.0 * math.pi))


def per_device(inputs, cotangent, spec_w1, spec_b1, spec_w2, spec_b2, up_weight, down_weight):
    full_width = up_weight.shape[0]
    block_size = spec_w1.shape[2]
    cos_fwd, sin_fwd, cos_inv, sin_inv = padded_tables(inputs.shape[2], lax.axis_size("space"))
    values = inputs.astype(jnp.float32)
    cotangent_parts = ring_send(cotangent)
    first_sum, second_sum = token_sums(jnp.sum(values, axis=-1), jnp.sum(values * values, axis=-1))
    mean_one = first_sum[..., None] / full_width
    rstd_one = lax.rsqrt(second_sum[..., None] / full_width - mean_one * mean_one + EPSILON)
    normed = (values - mean_one) * rstd_one
    spec_real, spec_imag = enter_spectrum(
        lon_forward(normed, cos_fwd), lon_forward(normed, sin_fwd)
    )
    spec_shape = spec_real.shape
    bias_one = to_blocks(spec_b1, block_size)
    bias_two = to_blocks(spec_b2, block_size)
    first_real, first_imag = block_product(
        to_blocks(spec_real, block_size), to_blocks(spec_imag, block_size), spec_w1
    )
    first_real = jax.nn.relu(first_real + bias_one[0])
    first_imag = jax.nn.relu(first_imag + bias_one[1])
    second_real, second_imag = block_product(first_real, first_imag, spec_w2)
    second_real = second_real + bias_two[0]
    second_imag = second_imag + bias_two[1]
    shrunk_real = (second_real - jnp.clip(second_real, -SHRINK_LEVEL, SHRINK_LEVEL)).reshape(
        spec_shape
    )
    shrunk_imag = (second_imag - jnp.clip(second_imag, -SHRINK_LEVEL, SHRINK_LEVEL)).reshape(
        spec_shape
    )
    shrunk_real, shrunk_imag, cotangent_parts = lax.optimization_barrier(
        (shrunk_real, shrunk_imag, cotangent_parts)
    )
    whole_cotangent = ring_assemble(cotangent_parts)
    back_real, back_imag = leave_spectrum(shrunk_real, shrunk_imag)
    filtered = lon_back(back_real, cos_inv) + lon_back(back_imag, sin_inv)
    residual = (filtered + normed + values).astype(jnp.bfloat16)
    residual_vals = residual.astype(jnp.float32)
    whole_residual = lax.all_gather(residual, "feat", axis=3, tiled=True)
    whole_vals = whole_residual.astype(jnp.float32)
    mean_two = jnp.sum(whole_vals, axis=-1, keepdims=True) / full_width
    square_two = jnp.sum(whole_vals * whole_vals, axis=-1, keepdims=True) / full_width
    rstd_two = lax.rsqrt(square_two - mean_two * mean_two + EPSILON)
    vhat = (whole_vals - mean_two) * rstd_two
    hidden = jnp.einsum(
        "brwd,dh->brwh", vhat.astype(jnp.bfloat16), up_weight, preferred_element_type=jnp.float32
    )
    activated = gelu_value(hidden).astype(jnp.bfloat16)
    mixed_term = jnp.einsum(
        "brwh,hd->brwd", activated, down_weight, preferred_element_type=jnp.float32
    )
    output = (residual_vals + channel_share(mixed_term)).astype(jnp.bfloat16)
    grad_act = jnp.einsum(
        "brwd,hd->brwh", whole_cotangent, down_weight, preferred_element_type=jnp.float32
    )
    grad_hidden = (grad_act * gelu_slope(hidden)).astype(jnp.bfloat16)
    grad_term = jnp.einsum(
        "brwh,dh->brwd", grad_hidden, up_weight, preferred_element_type=jnp.float32
    )
    total_one, total_two = token_sums(
        jnp.sum(grad_term, axis=-1), jnp.sum(grad_term * vhat, axis=-1)
    )
    grad_vhat = channel_share(grad_term)
    own_hat = (residual_vals - mean_two) * rstd_two
    grad_residual = cotangent.astype(jnp.float32) + rstd_two * (
        grad_vhat
        - total_one[..., None] / full_width
        - own_hat * (total_two[..., None] / full_width)
    )
    grad_real, grad_imag = enter_spectrum(
        lon_forward(grad_residual, cos_inv), lon_forward(grad_residual, sin_inv), jnp.bfloat16
    )
    grad_real = jnp.where(
        jnp.abs(second_real) > SHRINK_LEVEL, to_blocks(grad_real, block_size), 0.0
    )
    grad_imag = jnp.where(
        jnp.abs(second_imag) > SHRINK_LEVEL, to_blocks(grad_imag, block_size), 0.0
    )
    first_grad_real, first_grad_imag = block_adjoint(grad_real, grad_imag, spec_w2)
    first_grad_real = jnp.where(first_real > 0.0, first_grad_real, 0.0)
    first_grad_imag = jnp.where(first_imag > 0.0, first_grad_imag, 0.0)
    spec_grad_real, spec_grad_imag = block_adjoint(first_grad_real, first_grad_imag, spec_w1)
    rows_real, rows_imag = leave_spectrum(
        spec_grad_real.reshape(spec_shape), spec_grad_imag.reshape(spec_shape), jnp.bfloat16
    )
    grad_normed = grad_residual + lon_back(rows_real, cos_fwd) + lon_back(rows_imag, sin_fwd)
    norm_one, norm_two = token_sums(
        jnp.sum(grad_normed, axis=-1), jnp.sum(grad_normed * normed, axis=-1)
    )
    grad_input = grad_residual + rstd_one * (
        grad_normed - norm_one[..., None] / full_width - normed * (norm_two[..., None] / full_width)
    )
    return (output, grad_input.astype(jnp.bfloat16))


def solution(mesh):
    return jax.shard_map(
        per_device,
        mesh=mesh,
        in_specs=(
            P(None, "space", None, "feat"),
            P(None, "space", None, "feat"),
            P(None, "feat", None, None),
            P(None, "feat"),
            P(None, "feat", None, None),
            P(None, "feat"),
            P(None, "feat"),
            P("feat", None),
        ),
        out_specs=(P(None, "space", None, "feat"), P(None, "space", None, "feat")),
        check_vma=False,
    )
```

```python
import math

import jax
import jax.numpy as jnp
from jax import lax
from jax.sharding import PartitionSpec as P

EPSILON = 1e-05
SHRINK_LEVEL = 0.1
HIGHEST = lax.Precision.HIGHEST


def longitude_tables(width_lon):
    mode_count = width_lon // 2 + 1
    cell_index = jnp.arange(width_lon, dtype=jnp.int32)[:, None]
    wave_number = jnp.arange(mode_count, dtype=jnp.int32)[None, :]
    phase_angle = (
        2.0 * math.pi / width_lon * (cell_index * wave_number % width_lon).astype(jnp.float32)
    )
    scaling = 1.0 / math.sqrt(width_lon)
    cos_fwd = jnp.cos(phase_angle) * scaling
    sin_fwd = -jnp.sin(phase_angle) * scaling
    doubled = jnp.where((wave_number == 0) | (wave_number * 2 == width_lon), 1.0, 2.0).astype(
        jnp.float32
    )
    return (cos_fwd, sin_fwd, cos_fwd * doubled, sin_fwd * doubled)


def padded_tables(width_lon, multiple):
    tables = longitude_tables(width_lon)
    modes = tables[0].shape[1]
    extra = -modes % multiple
    return tuple(jnp.pad(table, ((0, 0), (0, extra))) for table in tables)


def lat_apply(table, field):
    return jnp.einsum("gh,bhkc->bgkc", table, field, precision=HIGHEST)


def complex_latitude(table_cos, table_sin, real_part, imag_part, inverse):
    if inverse:
        return (
            lat_apply(table_cos, real_part) + lat_apply(table_sin, imag_part),
            lat_apply(table_cos, imag_part) - lat_apply(table_sin, real_part),
        )
    return (
        lat_apply(table_cos, real_part) - lat_apply(table_sin, imag_part),
        lat_apply(table_cos, imag_part) + lat_apply(table_sin, real_part),
    )


def lon_forward(field, table):
    return jnp.einsum("brwc,wk->brkc", field, table, precision=HIGHEST)


def lon_back(spec, table):
    return jnp.einsum("brkc,wk->brwc", spec, table, precision=HIGHEST)


def to_blocks(field, block_size):
    return field.reshape(field.shape[:-1] + (field.shape[-1] // block_size, block_size))


def block_mult(field, weights):
    return jnp.einsum("...nc,nce->...ne", field, weights, precision=HIGHEST)


def block_mult_back(field, weights):
    return jnp.einsum("...ne,nce->...nc", field, weights, precision=HIGHEST)


def block_product(real_part, imag_part, weights):
    return (
        block_mult(real_part, weights[0]) - block_mult(imag_part, weights[1]),
        block_mult(real_part, weights[1]) + block_mult(imag_part, weights[0]),
    )


def block_adjoint(real_part, imag_part, weights):
    return (
        block_mult_back(real_part, weights[0]) + block_mult_back(imag_part, weights[1]),
        block_mult_back(imag_part, weights[0]) - block_mult_back(real_part, weights[1]),
    )


def latitude_tables(length):
    index_row = jnp.arange(length, dtype=jnp.int32)
    phase_angle = (
        2.0 * math.pi / length * (index_row[:, None] * index_row[None, :] % length).astype(jnp.float32)
    )
    scaling = 1.0 / math.sqrt(length)
    return (jnp.cos(phase_angle) * scaling, -jnp.sin(phase_angle) * scaling)


def to_columns(real_part, imag_part, link_type):
    stacked = jnp.stack([real_part, imag_part]).astype(link_type)
    moved = lax.all_to_all(stacked, "space", 3, 2, tiled=True).astype(jnp.float32)
    return (moved[0], moved[1])


def to_rows(real_part, imag_part, link_type):
    stacked = jnp.stack([real_part, imag_part]).astype(link_type)
    moved = lax.all_to_all(stacked, "space", 2, 3, tiled=True).astype(jnp.float32)
    return (moved[0], moved[1])


def enter_spectrum(real_part, imag_part, tables_lat, link_type=jnp.float32):
    table_cos, table_sin = tables_lat
    real_part, imag_part = to_columns(real_part, imag_part, link_type)
    return complex_latitude(table_cos, table_sin, real_part, imag_part, False)


def leave_spectrum(real_part, imag_part, tables_lat, link_type=jnp.float32):
    table_cos, table_sin = tables_lat
    real_part, imag_part = complex_latitude(table_cos, table_sin, real_part, imag_part, True)
    return to_rows(real_part, imag_part, link_type)


def token_sums(first_term, second_term):
    pair = jnp.stack([first_term, second_term])
    count = lax.axis_size("feat")
    position = lax.axis_index("feat")
    shifted = jnp.stack(
        [pair]
        + [
            lax.ppermute(pair, "feat", [(i, (i + count - shift) % count) for i in range(count)])
            for shift in range(1, count)
        ]
    )
    ordered = shifted[(jnp.arange(count) + count - position) % count]
    total = ordered[0]
    for source in range(1, count):
        total = total + ordered[source]
    return (total[0], total[1])


def ring_send(block):
    count = lax.axis_size("feat")
    return [block] + [
        lax.ppermute(block, "feat", [(i, (i + shift) % count) for i in range(count)])
        for shift in range(1, count)
    ]


def ring_assemble(parts):
    count = len(parts)
    position = lax.axis_index("feat")
    block = parts[0]
    width = block.shape[-1]
    whole = jnp.zeros(block.shape[:-1] + (width * count,), block.dtype)
    for shift, moved in enumerate(parts):
        source = (position + count - shift) % count
        whole = lax.dynamic_update_slice_in_dim(whole, moved, source * width, axis=block.ndim - 1)
    return whole


def channel_share(term):
    return lax.psum_scatter(
        term.astype(jnp.bfloat16), "feat", scatter_dimension=3, tiled=True
    ).astype(jnp.float32)


def gelu_value(field):
    return 0.5 * field * (1.0 + lax.erf(field * (1.0 / math.sqrt(2.0))))


def gelu_slope(field):
    return 0.5 * (1.0 + lax.erf(field * (1.0 / math.sqrt(2.0)))) + field * jnp.exp(
        -0.5 * field * field
    ) * (1.0 / math.sqrt(2.0 * math.pi))


def per_device(inputs, cotangent, spec_w1, spec_b1, spec_w2, spec_b2, up_weight, down_weight):
    full_width = up_weight.shape[0]
    block_size = spec_w1.shape[2]
    tables_lon = padded_tables(inputs.shape[2], lax.axis_size("space"))
    tables_lat = latitude_tables(inputs.shape[1] * lax.axis_size("space"))
    tables_lon, tables_lat = lax.optimization_barrier((tables_lon, tables_lat))
    cos_fwd, sin_fwd, cos_inv, sin_inv = tables_lon
    values = inputs.astype(jnp.float32)
    cotangent_parts = ring_send(cotangent)
    first_sum, second_sum = token_sums(jnp.sum(values, axis=-1), jnp.sum(values * values, axis=-1))
    mean_one = first_sum[..., None] / full_width
    rstd_one = lax.rsqrt(second_sum[..., None] / full_width - mean_one * mean_one + EPSILON)
    normed = (values - mean_one) * rstd_one
    spec_real, spec_imag = enter_spectrum(
        lon_forward(normed, cos_fwd), lon_forward(normed, sin_fwd), tables_lat
    )
    spec_shape = spec_real.shape
    bias_one = to_blocks(spec_b1, block_size)
    bias_two = to_blocks(spec_b2, block_size)
    first_real, first_imag = block_product(
        to_blocks(spec_real, block_size), to_blocks(spec_imag, block_size), spec_w1
    )
    first_real = jax.nn.relu(first_real + bias_one[0])
    first_imag = jax.nn.relu(first_imag + bias_one[1])
    second_real, second_imag = block_product(first_real, first_imag, spec_w2)
    second_real = second_real + bias_two[0]
    second_imag = second_imag + bias_two[1]
    shrunk_real = (second_real - jnp.clip(second_real, -SHRINK_LEVEL, SHRINK_LEVEL)).reshape(
        spec_shape
    )
    shrunk_imag = (second_imag - jnp.clip(second_imag, -SHRINK_LEVEL, SHRINK_LEVEL)).reshape(
        spec_shape
    )
    shrunk_real, shrunk_imag, cotangent_parts = lax.optimization_barrier(
        (shrunk_real, shrunk_imag, cotangent_parts)
    )
    whole_cotangent = ring_assemble(cotangent_parts)
    back_real, back_imag = leave_spectrum(shrunk_real, shrunk_imag, tables_lat)
    filtered = lon_back(back_real, cos_inv) + lon_back(back_imag, sin_inv)
    residual = (filtered + normed + values).astype(jnp.bfloat16)
    residual_vals = residual.astype(jnp.float32)
    whole_residual = lax.all_gather(residual, "feat", axis=3, tiled=True)
    whole_vals = whole_residual.astype(jnp.float32)
    mean_two = jnp.sum(whole_vals, axis=-1, keepdims=True) / full_width
    square_two = jnp.sum(whole_vals * whole_vals, axis=-1, keepdims=True) / full_width
    rstd_two = lax.rsqrt(square_two - mean_two * mean_two + EPSILON)
    vhat = (whole_vals - mean_two) * rstd_two
    hidden = jnp.einsum(
        "brwd,dh->brwh", vhat.astype(jnp.bfloat16), up_weight, preferred_element_type=jnp.float32
    )
    activated = gelu_value(hidden).astype(jnp.bfloat16)
    mixed_term = jnp.einsum(
        "brwh,hd->brwd", activated, down_weight, preferred_element_type=jnp.float32
    )
    output = (residual_vals + channel_share(mixed_term)).astype(jnp.bfloat16)
    grad_act = jnp.einsum(
        "brwd,hd->brwh", whole_cotangent, down_weight, preferred_element_type=jnp.float32
    )
    grad_hidden = (grad_act * gelu_slope(hidden)).astype(jnp.bfloat16)
    grad_term = jnp.einsum(
        "brwh,dh->brwd", grad_hidden, up_weight, preferred_element_type=jnp.float32
    )
    total_one, total_two = token_sums(
        jnp.sum(grad_term, axis=-1), jnp.sum(grad_term * vhat, axis=-1)
    )
    grad_vhat = channel_share(grad_term)
    own_hat = (residual_vals - mean_two) * rstd_two
    grad_residual = cotangent.astype(jnp.float32) + rstd_two * (
        grad_vhat
        - total_one[..., None] / full_width
        - own_hat * (total_two[..., None] / full_width)
    )
    grad_real, grad_imag = enter_spectrum(
        lon_forward(grad_residual, cos_inv), lon_forward(grad_residual, sin_inv), tables_lat, jnp.bfloat16
    )
    grad_real = jnp.where(
        jnp.abs(second_real) > SHRINK_LEVEL, to_blocks(grad_real, block_size), 0.0
    )
    grad_imag = jnp.where(
        jnp.abs(second_imag) > SHRINK_LEVEL, to_blocks(grad_imag, block_size), 0.0
    )
    first_grad_real, first_grad_imag = block_adjoint(grad_real, grad_imag, spec_w2)
    first_grad_real = jnp.where(first_real > 0.0, first_grad_real, 0.0)
    first_grad_imag = jnp.where(first_imag > 0.0, first_grad_imag, 0.0)
    spec_grad_real, spec_grad_imag = block_adjoint(first_grad_real, first_grad_imag, spec_w1)
    rows_real, rows_imag = leave_spectrum(
        spec_grad_real.reshape(spec_shape), spec_grad_imag.reshape(spec_shape), tables_lat, jnp.bfloat16
    )
    grad_normed = grad_residual + lon_back(rows_real, cos_fwd) + lon_back(rows_imag, sin_fwd)
    norm_one, norm_two = token_sums(
        jnp.sum(grad_normed, axis=-1), jnp.sum(grad_normed * normed, axis=-1)
    )
    grad_input = grad_residual + rstd_one * (
        grad_normed - norm_one[..., None] / full_width - normed * (norm_two[..., None] / full_width)
    )
    return (output, grad_input.astype(jnp.bfloat16))


def solution(mesh):
    return jax.shard_map(
        per_device,
        mesh=mesh,
        in_specs=(
            P(None, "space", None, "feat"),
            P(None, "space", None, "feat"),
            P(None, "feat", None, None),
            P(None, "feat"),
            P(None, "feat", None, None),
            P(None, "feat"),
            P(None, "feat"),
            P("feat", None),
        ),
        out_specs=(P(None, "space", None, "feat"), P(None, "space", None, "feat")),
        check_vma=False,
    )
```

```python
import math

import jax
import jax.numpy as jnp
from jax import lax
from jax.sharding import PartitionSpec as P

EPSILON = 1e-05
SHRINK_LEVEL = 0.1
HIGHEST = lax.Precision.HIGHEST


def longitude_tables(width_lon):
    mode_count = width_lon // 2 + 1
    cell_index = jnp.arange(width_lon, dtype=jnp.int32)[:, None]
    wave_number = jnp.arange(mode_count, dtype=jnp.int32)[None, :]
    phase_angle = (
        2.0 * math.pi / width_lon * (cell_index * wave_number % width_lon).astype(jnp.float32)
    )
    scaling = 1.0 / math.sqrt(width_lon)
    cos_fwd = jnp.cos(phase_angle) * scaling
    sin_fwd = -jnp.sin(phase_angle) * scaling
    doubled = jnp.where((wave_number == 0) | (wave_number * 2 == width_lon), 1.0, 2.0).astype(
        jnp.float32
    )
    return (cos_fwd, sin_fwd, cos_fwd * doubled, sin_fwd * doubled)


def padded_tables(width_lon, multiple):
    tables = longitude_tables(width_lon)
    modes = tables[0].shape[1]
    extra = -modes % multiple
    return tuple(jnp.pad(table, ((0, 0), (0, extra))) for table in tables)


def lat_apply(table, field):
    return jnp.einsum("gh,bhkc->bgkc", table, field, precision=HIGHEST)


def complex_latitude(table_cos, table_sin, real_part, imag_part, inverse):
    if inverse:
        return (
            lat_apply(table_cos, real_part) + lat_apply(table_sin, imag_part),
            lat_apply(table_cos, imag_part) - lat_apply(table_sin, real_part),
        )
    return (
        lat_apply(table_cos, real_part) - lat_apply(table_sin, imag_part),
        lat_apply(table_cos, imag_part) + lat_apply(table_sin, real_part),
    )


def lon_forward(field, table):
    return jnp.einsum("brwc,wk->brkc", field, table, precision=HIGHEST)


def lon_back(spec, table):
    return jnp.einsum("brkc,wk->brwc", spec, table, precision=HIGHEST)


def to_blocks(field, block_size):
    return field.reshape(field.shape[:-1] + (field.shape[-1] // block_size, block_size))


def block_mult(field, weights):
    return jnp.einsum("...nc,nce->...ne", field, weights, precision=HIGHEST)


def block_mult_back(field, weights):
    return jnp.einsum("...ne,nce->...nc", field, weights, precision=HIGHEST)


def block_product(real_part, imag_part, weights):
    return (
        block_mult(real_part, weights[0]) - block_mult(imag_part, weights[1]),
        block_mult(real_part, weights[1]) + block_mult(imag_part, weights[0]),
    )


def block_adjoint(real_part, imag_part, weights):
    return (
        block_mult_back(real_part, weights[0]) + block_mult_back(imag_part, weights[1]),
        block_mult_back(imag_part, weights[0]) - block_mult_back(real_part, weights[1]),
    )


def latitude_tables(length):
    index_row = jnp.arange(length, dtype=jnp.int32)
    phase_angle = (
        2.0 * math.pi / length * (index_row[:, None] * index_row[None, :] % length).astype(jnp.float32)
    )
    scaling = 1.0 / math.sqrt(length)
    return (jnp.cos(phase_angle) * scaling, -jnp.sin(phase_angle) * scaling)


def to_columns(real_part, imag_part, link_type):
    stacked = jnp.stack([real_part, imag_part]).astype(link_type)
    moved = lax.all_to_all(stacked, "space", 3, 2, tiled=True).astype(jnp.float32)
    return (moved[0], moved[1])


def to_rows(real_part, imag_part, link_type):
    stacked = jnp.stack([real_part, imag_part]).astype(link_type)
    moved = lax.all_to_all(stacked, "space", 2, 3, tiled=True).astype(jnp.float32)
    return (moved[0], moved[1])


def enter_spectrum(real_part, imag_part, tables_lat, link_type=jnp.float32):
    table_cos, table_sin = tables_lat
    real_part, imag_part = to_columns(real_part, imag_part, link_type)
    return complex_latitude(table_cos, table_sin, real_part, imag_part, False)


def leave_spectrum(real_part, imag_part, tables_lat, link_type=jnp.float32):
    table_cos, table_sin = tables_lat
    real_part, imag_part = complex_latitude(table_cos, table_sin, real_part, imag_part, True)
    return to_rows(real_part, imag_part, link_type)


def complex_operator(real_block, imag_block):
    return jnp.stack(
        [jnp.stack([real_block, -imag_block]), jnp.stack([imag_block, real_block])]
    )


def lat_stacked(operator, field):
    return jnp.einsum("pqkh,qbhlc->pbklc", operator, field, precision=HIGHEST)


def lon_stacked_forward(field, tables):
    return jnp.einsum("brwc,pwk->pbrkc", field, tables, precision=HIGHEST)


def lon_stacked_back(spec, tables):
    return jnp.einsum("pbrkc,pwk->brwc", spec, tables, precision=HIGHEST)


def block_operator(weights):
    return jnp.moveaxis(complex_operator(weights[0], weights[1]), 2, 0)


def block_stacked(field, operator):
    return jnp.einsum("qbklnc,npqce->pbklne", field, operator, precision=HIGHEST)


def block_stacked_adjoint(field, operator):
    return jnp.einsum("pbklne,npqce->qbklnc", field, operator, precision=HIGHEST)


def stacked_columns(field, link_type):
    return lax.all_to_all(field.astype(link_type), "space", 3, 2, tiled=True).astype(jnp.float32)


def stacked_rows(field, link_type):
    return lax.all_to_all(field.astype(link_type), "space", 2, 3, tiled=True).astype(jnp.float32)


def token_sums(first_term, second_term):
    pair = jnp.stack([first_term, second_term])
    count = lax.axis_size("feat")
    position = lax.axis_index("feat")
    shifted = jnp.stack(
        [pair]
        + [
            lax.ppermute(pair, "feat", [(i, (i + count - shift) % count) for i in range(count)])
            for shift in range(1, count)
        ]
    )
    ordered = shifted[(jnp.arange(count) + count - position) % count]
    total = ordered[0]
    for source in range(1, count):
        total = total + ordered[source]
    return (total[0], total[1])


def ring_send(block):
    count = lax.axis_size("feat")
    return [block] + [
        lax.ppermute(block, "feat", [(i, (i + shift) % count) for i in range(count)])
        for shift in range(1, count)
    ]


def ring_assemble(parts):
    count = len(parts)
    position = lax.axis_index("feat")
    block = parts[0]
    width = block.shape[-1]
    whole = jnp.zeros(block.shape[:-1] + (width * count,), block.dtype)
    for shift, moved in enumerate(parts):
        source = (position + count - shift) % count
        whole = lax.dynamic_update_slice_in_dim(whole, moved, source * width, axis=block.ndim - 1)
    return whole


def channel_share(term):
    return lax.psum_scatter(
        term.astype(jnp.bfloat16), "feat", scatter_dimension=3, tiled=True
    ).astype(jnp.float32)


def gelu_value(field):
    return 0.5 * field * (1.0 + lax.erf(field * (1.0 / math.sqrt(2.0))))


def gelu_slope(field):
    return 0.5 * (1.0 + lax.erf(field * (1.0 / math.sqrt(2.0)))) + field * jnp.exp(
        -0.5 * field * field
    ) * (1.0 / math.sqrt(2.0 * math.pi))


def per_device(inputs, cotangent, spec_w1, spec_b1, spec_w2, spec_b2, up_weight, down_weight):
    full_width = up_weight.shape[0]
    block_size = spec_w1.shape[2]
    tables_lon = padded_tables(inputs.shape[2], lax.axis_size("space"))
    tables_lat = latitude_tables(inputs.shape[1] * lax.axis_size("space"))
    cos_fwd, sin_fwd, cos_inv, sin_inv = tables_lon
    table_cos, table_sin = tables_lat
    operators = (
        jnp.stack([cos_fwd, sin_fwd]),
        jnp.stack([cos_inv, sin_inv]),
        complex_operator(table_cos, table_sin),
        complex_operator(table_cos, -table_sin),
        block_operator(spec_w1),
        block_operator(spec_w2),
    )
    operators = lax.optimization_barrier(operators)
    lon_fwd_tables, lon_inv_tables, lat_forward_op, lat_inverse_op, first_op, second_op = operators
    values = inputs.astype(jnp.float32)
    cotangent_parts = ring_send(cotangent)
    first_sum, second_sum = token_sums(jnp.sum(values, axis=-1), jnp.sum(values * values, axis=-1))
    mean_one = first_sum[..., None] / full_width
    rstd_one = lax.rsqrt(second_sum[..., None] / full_width - mean_one * mean_one + EPSILON)
    normed = (values - mean_one) * rstd_one
    spec = lat_stacked(
        lat_forward_op, stacked_columns(lon_stacked_forward(normed, lon_fwd_tables), jnp.float32)
    )
    spec_blocks = to_blocks(spec, block_size)
    bias_one = to_blocks(spec_b1, block_size)[:, None, None, None]
    bias_two = to_blocks(spec_b2, block_size)[:, None, None, None]
    first = jax.nn.relu(block_stacked(spec_blocks, first_op) + bias_one)
    second = block_stacked(first, second_op) + bias_two
    shrunk = (second - jnp.clip(second, -SHRINK_LEVEL, SHRINK_LEVEL)).reshape(spec.shape)
    shrunk, cotangent_parts = lax.optimization_barrier((shrunk, cotangent_parts))
    whole_cotangent = ring_assemble(cotangent_parts)
    filtered = lon_stacked_back(
        stacked_rows(lat_stacked(lat_inverse_op, shrunk), jnp.float32), lon_inv_tables
    )
    residual = (filtered + normed + values).astype(jnp.bfloat16)
    residual_vals = residual.astype(jnp.float32)
    whole_residual = lax.all_gather(residual, "feat", axis=3, tiled=True)
    whole_vals = whole_residual.astype(jnp.float32)
    mean_two = jnp.sum(whole_vals, axis=-1, keepdims=True) / full_width
    square_two = jnp.sum(whole_vals * whole_vals, axis=-1, keepdims=True) / full_width
    rstd_two = lax.rsqrt(square_two - mean_two * mean_two + EPSILON)
    vhat = (whole_vals - mean_two) * rstd_two
    hidden = jnp.einsum(
        "brwd,dh->brwh", vhat.astype(jnp.bfloat16), up_weight, preferred_element_type=jnp.float32
    )
    activated = gelu_value(hidden).astype(jnp.bfloat16)
    mixed_term = jnp.einsum(
        "brwh,hd->brwd", activated, down_weight, preferred_element_type=jnp.float32
    )
    output = (residual_vals + channel_share(mixed_term)).astype(jnp.bfloat16)
    grad_act = jnp.einsum(
        "brwd,hd->brwh", whole_cotangent, down_weight, preferred_element_type=jnp.float32
    )
    grad_hidden = (grad_act * gelu_slope(hidden)).astype(jnp.bfloat16)
    grad_term = jnp.einsum(
        "brwh,dh->brwd", grad_hidden, up_weight, preferred_element_type=jnp.float32
    )
    total_one, total_two = token_sums(
        jnp.sum(grad_term, axis=-1), jnp.sum(grad_term * vhat, axis=-1)
    )
    grad_vhat = channel_share(grad_term)
    own_hat = (residual_vals - mean_two) * rstd_two
    grad_residual = cotangent.astype(jnp.float32) + rstd_two * (
        grad_vhat
        - total_one[..., None] / full_width
        - own_hat * (total_two[..., None] / full_width)
    )
    grad_spec = lat_stacked(
        lat_forward_op,
        stacked_columns(lon_stacked_forward(grad_residual, lon_inv_tables), jnp.bfloat16),
    )
    grad_second = jnp.where(
        jnp.abs(second) > SHRINK_LEVEL, to_blocks(grad_spec, block_size), 0.0
    )
    grad_first = jnp.where(first > 0.0, block_stacked_adjoint(grad_second, second_op), 0.0)
    grad_spectrum = block_stacked_adjoint(grad_first, first_op).reshape(spec.shape)
    grad_normed = grad_residual + lon_stacked_back(
        stacked_rows(lat_stacked(lat_inverse_op, grad_spectrum), jnp.bfloat16), lon_fwd_tables
    )
    norm_one, norm_two = token_sums(
        jnp.sum(grad_normed, axis=-1), jnp.sum(grad_normed * normed, axis=-1)
    )
    grad_input = grad_residual + rstd_one * (
        grad_normed - norm_one[..., None] / full_width - normed * (norm_two[..., None] / full_width)
    )
    return (output, grad_input.astype(jnp.bfloat16))


def solution(mesh):
    return jax.shard_map(
        per_device,
        mesh=mesh,
        in_specs=(
            P(None, "space", None, "feat"),
            P(None, "space", None, "feat"),
            P(None, "feat", None, None),
            P(None, "feat"),
            P(None, "feat", None, None),
            P(None, "feat"),
            P(None, "feat"),
            P("feat", None),
        ),
        out_specs=(P(None, "space", None, "feat"), P(None, "space", None, "feat")),
        check_vma=False,
    )
```

```python
import math

import jax
import jax.numpy as jnp
from jax import lax
from jax.sharding import PartitionSpec as P

EPSILON = 1e-05
SHRINK_LEVEL = 0.1
HIGHEST = lax.Precision.HIGHEST


def longitude_tables(width_lon):
    mode_count = width_lon // 2 + 1
    cell_index = jnp.arange(width_lon, dtype=jnp.int32)[:, None]
    wave_number = jnp.arange(mode_count, dtype=jnp.int32)[None, :]
    phase_angle = (
        2.0 * math.pi / width_lon * (cell_index * wave_number % width_lon).astype(jnp.float32)
    )
    scaling = 1.0 / math.sqrt(width_lon)
    cos_fwd = jnp.cos(phase_angle) * scaling
    sin_fwd = -jnp.sin(phase_angle) * scaling
    doubled = jnp.where((wave_number == 0) | (wave_number * 2 == width_lon), 1.0, 2.0).astype(
        jnp.float32
    )
    return (cos_fwd, sin_fwd, cos_fwd * doubled, sin_fwd * doubled)


def padded_tables(width_lon, multiple):
    tables = longitude_tables(width_lon)
    modes = tables[0].shape[1]
    extra = -modes % multiple
    return tuple(jnp.pad(table, ((0, 0), (0, extra))) for table in tables)


def lat_apply(table, field):
    return jnp.einsum("gh,bhkc->bgkc", table, field, precision=HIGHEST)


def complex_latitude(table_cos, table_sin, real_part, imag_part, inverse):
    if inverse:
        return (
            lat_apply(table_cos, real_part) + lat_apply(table_sin, imag_part),
            lat_apply(table_cos, imag_part) - lat_apply(table_sin, real_part),
        )
    return (
        lat_apply(table_cos, real_part) - lat_apply(table_sin, imag_part),
        lat_apply(table_cos, imag_part) + lat_apply(table_sin, real_part),
    )


def lon_forward(field, table):
    return jnp.einsum("brwc,wk->brkc", field, table, precision=HIGHEST)


def lon_back(spec, table):
    return jnp.einsum("brkc,wk->brwc", spec, table, precision=HIGHEST)


def to_blocks(field, block_size):
    return field.reshape(field.shape[:-1] + (field.shape[-1] // block_size, block_size))


def block_mult(field, weights):
    return jnp.einsum("...nc,nce->...ne", field, weights, precision=HIGHEST)


def block_mult_back(field, weights):
    return jnp.einsum("...ne,nce->...nc", field, weights, precision=HIGHEST)


def block_product(real_part, imag_part, weights):
    return (
        block_mult(real_part, weights[0]) - block_mult(imag_part, weights[1]),
        block_mult(real_part, weights[1]) + block_mult(imag_part, weights[0]),
    )


def block_adjoint(real_part, imag_part, weights):
    return (
        block_mult_back(real_part, weights[0]) + block_mult_back(imag_part, weights[1]),
        block_mult_back(imag_part, weights[0]) - block_mult_back(real_part, weights[1]),
    )


def latitude_tables(length):
    index_row = jnp.arange(length, dtype=jnp.int32)
    phase_angle = (
        2.0 * math.pi / length * (index_row[:, None] * index_row[None, :] % length).astype(jnp.float32)
    )
    scaling = 1.0 / math.sqrt(length)
    return (jnp.cos(phase_angle) * scaling, -jnp.sin(phase_angle) * scaling)


def to_columns(real_part, imag_part, link_type):
    stacked = jnp.stack([real_part, imag_part]).astype(link_type)
    moved = lax.all_to_all(stacked, "space", 3, 2, tiled=True).astype(jnp.float32)
    return (moved[0], moved[1])


def to_rows(real_part, imag_part, link_type):
    stacked = jnp.stack([real_part, imag_part]).astype(link_type)
    moved = lax.all_to_all(stacked, "space", 2, 3, tiled=True).astype(jnp.float32)
    return (moved[0], moved[1])


def enter_spectrum(real_part, imag_part, tables_lat, link_type=jnp.float32):
    table_cos, table_sin = tables_lat
    real_part, imag_part = to_columns(real_part, imag_part, link_type)
    return complex_latitude(table_cos, table_sin, real_part, imag_part, False)


def leave_spectrum(real_part, imag_part, tables_lat, link_type=jnp.float32):
    table_cos, table_sin = tables_lat
    real_part, imag_part = complex_latitude(table_cos, table_sin, real_part, imag_part, True)
    return to_rows(real_part, imag_part, link_type)


def complex_operator(real_block, imag_block):
    return jnp.stack(
        [jnp.stack([real_block, -imag_block]), jnp.stack([imag_block, real_block])]
    )


def lat_stacked(operator, field):
    return jnp.einsum("pqkh,qbhlc->pbklc", operator, field, precision=HIGHEST)


def lon_stacked_forward(field, tables):
    return jnp.einsum("brwc,pwk->pbrkc", field, tables, precision=HIGHEST)


def lon_stacked_back(spec, tables):
    return jnp.einsum("pbrkc,pwk->brwc", spec, tables, precision=HIGHEST)


def block_operator(weights):
    return jnp.moveaxis(complex_operator(weights[0], weights[1]), 2, 0)


def block_stacked(field, operator):
    return jnp.einsum("qbklnc,npqce->pbklne", field, operator, precision=HIGHEST)


def block_stacked_adjoint(field, operator):
    return jnp.einsum("pbklne,npqce->qbklnc", field, operator, precision=HIGHEST)


def stacked_columns(field, link_type):
    return lax.all_to_all(field.astype(link_type), "space", 3, 2, tiled=True).astype(jnp.float32)


def stacked_rows(field, link_type):
    return lax.all_to_all(field.astype(link_type), "space", 2, 3, tiled=True).astype(jnp.float32)


def token_sums(first_term, second_term):
    pair = jnp.stack([first_term, second_term])
    count = lax.axis_size("feat")
    position = lax.axis_index("feat")
    shifted = jnp.stack(
        [pair]
        + [
            lax.ppermute(pair, "feat", [(i, (i + count - shift) % count) for i in range(count)])
            for shift in range(1, count)
        ]
    )
    ordered = shifted[(jnp.arange(count) + count - position) % count]
    total = ordered[0]
    for source in range(1, count):
        total = total + ordered[source]
    return (total[0], total[1])


def ring_send(block):
    count = lax.axis_size("feat")
    return [block] + [
        lax.ppermute(block, "feat", [(i, (i + shift) % count) for i in range(count)])
        for shift in range(1, count)
    ]


def ring_assemble(parts):
    count = len(parts)
    position = lax.axis_index("feat")
    block = parts[0]
    width = block.shape[-1]
    whole = jnp.zeros(block.shape[:-1] + (width * count,), block.dtype)
    for shift, moved in enumerate(parts):
        source = (position + count - shift) % count
        whole = lax.dynamic_update_slice_in_dim(whole, moved, source * width, axis=block.ndim - 1)
    return whole


def channel_share(term):
    return lax.psum_scatter(
        term.astype(jnp.bfloat16), "feat", scatter_dimension=3, tiled=True
    ).astype(jnp.float32)


def gelu_value(field):
    return 0.5 * field * (1.0 + lax.erf(field * (1.0 / math.sqrt(2.0))))


def gelu_slope(field):
    return 0.5 * (1.0 + lax.erf(field * (1.0 / math.sqrt(2.0)))) + field * jnp.exp(
        -0.5 * field * field
    ) * (1.0 / math.sqrt(2.0 * math.pi))


def mixer(residual, whole_cotangent, cotangent, up_weight, down_weight):
    full_width = up_weight.shape[0]
    residual_vals = residual.astype(jnp.float32)
    whole_residual = lax.all_gather(residual, "feat", axis=3, tiled=True)
    whole_vals = whole_residual.astype(jnp.float32)
    mean_two = jnp.sum(whole_vals, axis=-1, keepdims=True) / full_width
    square_two = jnp.sum(whole_vals * whole_vals, axis=-1, keepdims=True) / full_width
    rstd_two = lax.rsqrt(square_two - mean_two * mean_two + EPSILON)
    vhat = (whole_vals - mean_two) * rstd_two
    hidden = jnp.einsum(
        "brwd,dh->brwh", vhat.astype(jnp.bfloat16), up_weight, preferred_element_type=jnp.float32
    )
    activated = gelu_value(hidden).astype(jnp.bfloat16)
    mixed_term = jnp.einsum(
        "brwh,hd->brwd", activated, down_weight, preferred_element_type=jnp.float32
    )
    grad_act = jnp.einsum(
        "brwd,hd->brwh", whole_cotangent, down_weight, preferred_element_type=jnp.float32
    )
    grad_hidden = (grad_act * gelu_slope(hidden)).astype(jnp.bfloat16)
    grad_term = jnp.einsum(
        "brwh,dh->brwd", grad_hidden, up_weight, preferred_element_type=jnp.float32
    )
    total_one, total_two = token_sums(
        jnp.sum(grad_term, axis=-1), jnp.sum(grad_term * vhat, axis=-1)
    )
    grad_vhat = channel_share(grad_term)
    own_hat = (residual_vals - mean_two) * rstd_two
    grad_residual = cotangent.astype(jnp.float32) + rstd_two * (
        grad_vhat
        - total_one[..., None] / full_width
        - own_hat * (total_two[..., None] / full_width)
    )
    return (mixed_term, grad_vhat, grad_residual)


def per_device(inputs, cotangent, spec_w1, spec_b1, spec_w2, spec_b2, up_weight, down_weight):
    full_width = up_weight.shape[0]
    block_size = spec_w1.shape[2]
    tables_lon = padded_tables(inputs.shape[2], lax.axis_size("space"))
    tables_lat = latitude_tables(inputs.shape[1] * lax.axis_size("space"))
    cos_fwd, sin_fwd, cos_inv, sin_inv = tables_lon
    table_cos, table_sin = tables_lat
    operators = (
        jnp.stack([cos_fwd, sin_fwd]),
        jnp.stack([cos_inv, sin_inv]),
        complex_operator(table_cos, table_sin),
        complex_operator(table_cos, -table_sin),
        block_operator(spec_w1),
        block_operator(spec_w2),
    )
    operators = lax.optimization_barrier(operators)
    lon_fwd_tables, lon_inv_tables, lat_forward_op, lat_inverse_op, first_op, second_op = operators
    values = inputs.astype(jnp.float32)
    cotangent_parts = ring_send(cotangent)
    first_sum, second_sum = token_sums(jnp.sum(values, axis=-1), jnp.sum(values * values, axis=-1))
    mean_one = first_sum[..., None] / full_width
    rstd_one = lax.rsqrt(second_sum[..., None] / full_width - mean_one * mean_one + EPSILON)
    normed = (values - mean_one) * rstd_one
    spec = lat_stacked(
        lat_forward_op, stacked_columns(lon_stacked_forward(normed, lon_fwd_tables), jnp.float32)
    )
    spec_blocks = to_blocks(spec, block_size)
    bias_one = to_blocks(spec_b1, block_size)[:, None, None, None]
    bias_two = to_blocks(spec_b2, block_size)[:, None, None, None]
    first = jax.nn.relu(block_stacked(spec_blocks, first_op) + bias_one)
    second = block_stacked(first, second_op) + bias_two
    shrunk = (second - jnp.clip(second, -SHRINK_LEVEL, SHRINK_LEVEL)).reshape(spec.shape)
    shrunk, cotangent_parts = lax.optimization_barrier((shrunk, cotangent_parts))
    whole_cotangent = ring_assemble(cotangent_parts)
    filtered = lon_stacked_back(
        stacked_rows(lat_stacked(lat_inverse_op, shrunk), jnp.float32), lon_inv_tables
    )
    residual = (filtered + normed + values).astype(jnp.bfloat16)
    residual_vals = residual.astype(jnp.float32)
    pieces = [
        mixer(
            residual[half : half + 1],
            whole_cotangent[half : half + 1],
            cotangent[half : half + 1],
            up_weight,
            down_weight,
        )
        for half in range(residual.shape[0])
    ]
    mixed_term = jnp.concatenate([piece[0] for piece in pieces], axis=0)
    mixed_term, last_share = lax.optimization_barrier((mixed_term, pieces[-1][1]))
    output = (residual.astype(jnp.float32) + channel_share(mixed_term)).astype(jnp.bfloat16)
    grad_residual = jnp.concatenate([piece[2] for piece in pieces[:-1]] + [pieces[-1][2]], axis=0)
    grad_spec = lat_stacked(
        lat_forward_op,
        stacked_columns(lon_stacked_forward(grad_residual, lon_inv_tables), jnp.bfloat16),
    )
    grad_second = jnp.where(
        jnp.abs(second) > SHRINK_LEVEL, to_blocks(grad_spec, block_size), 0.0
    )
    grad_first = jnp.where(first > 0.0, block_stacked_adjoint(grad_second, second_op), 0.0)
    grad_spectrum = block_stacked_adjoint(grad_first, first_op).reshape(spec.shape)
    grad_normed = grad_residual + lon_stacked_back(
        stacked_rows(lat_stacked(lat_inverse_op, grad_spectrum), jnp.bfloat16), lon_fwd_tables
    )
    norm_one, norm_two = token_sums(
        jnp.sum(grad_normed, axis=-1), jnp.sum(grad_normed * normed, axis=-1)
    )
    grad_input = grad_residual + rstd_one * (
        grad_normed - norm_one[..., None] / full_width - normed * (norm_two[..., None] / full_width)
    )
    return (output, grad_input.astype(jnp.bfloat16))


def solution(mesh):
    return jax.shard_map(
        per_device,
        mesh=mesh,
        in_specs=(
            P(None, "space", None, "feat"),
            P(None, "space", None, "feat"),
            P(None, "feat", None, None),
            P(None, "feat"),
            P(None, "feat", None, None),
            P(None, "feat"),
            P(None, "feat"),
            P("feat", None),
        ),
        out_specs=(P(None, "space", None, "feat"), P(None, "space", None, "feat")),
        check_vma=False,
    )
```

```python
import math

import jax
import jax.numpy as jnp
from jax import lax
from jax.sharding import PartitionSpec as P

EPSILON = 1e-05
SHRINK_LEVEL = 0.1
HIGHEST = lax.Precision.HIGHEST


def longitude_tables(width_lon):
    mode_count = width_lon // 2 + 1
    cell_index = jnp.arange(width_lon, dtype=jnp.int32)[:, None]
    wave_number = jnp.arange(mode_count, dtype=jnp.int32)[None, :]
    phase_angle = (
        2.0 * math.pi / width_lon * (cell_index * wave_number % width_lon).astype(jnp.float32)
    )
    scaling = 1.0 / math.sqrt(width_lon)
    cos_fwd = jnp.cos(phase_angle) * scaling
    sin_fwd = -jnp.sin(phase_angle) * scaling
    doubled = jnp.where((wave_number == 0) | (wave_number * 2 == width_lon), 1.0, 2.0).astype(
        jnp.float32
    )
    return (cos_fwd, sin_fwd, cos_fwd * doubled, sin_fwd * doubled)


def padded_tables(width_lon, multiple):
    tables = longitude_tables(width_lon)
    modes = tables[0].shape[1]
    extra = -modes % multiple
    return tuple(jnp.pad(table, ((0, 0), (0, extra))) for table in tables)


def lat_apply(table, field):
    return jnp.einsum("gh,bhkc->bgkc", table, field, precision=HIGHEST)


def complex_latitude(table_cos, table_sin, real_part, imag_part, inverse):
    if inverse:
        return (
            lat_apply(table_cos, real_part) + lat_apply(table_sin, imag_part),
            lat_apply(table_cos, imag_part) - lat_apply(table_sin, real_part),
        )
    return (
        lat_apply(table_cos, real_part) - lat_apply(table_sin, imag_part),
        lat_apply(table_cos, imag_part) + lat_apply(table_sin, real_part),
    )


def lon_forward(field, table):
    return jnp.einsum("brwc,wk->brkc", field, table, precision=HIGHEST)


def lon_back(spec, table):
    return jnp.einsum("brkc,wk->brwc", spec, table, precision=HIGHEST)


def to_blocks(field, block_size):
    return field.reshape(field.shape[:-1] + (field.shape[-1] // block_size, block_size))


def block_mult(field, weights):
    return jnp.einsum("...nc,nce->...ne", field, weights, precision=HIGHEST)


def block_mult_back(field, weights):
    return jnp.einsum("...ne,nce->...nc", field, weights, precision=HIGHEST)


def block_product(real_part, imag_part, weights):
    return (
        block_mult(real_part, weights[0]) - block_mult(imag_part, weights[1]),
        block_mult(real_part, weights[1]) + block_mult(imag_part, weights[0]),
    )


def block_adjoint(real_part, imag_part, weights):
    return (
        block_mult_back(real_part, weights[0]) + block_mult_back(imag_part, weights[1]),
        block_mult_back(imag_part, weights[0]) - block_mult_back(real_part, weights[1]),
    )


def latitude_tables(length):
    index_row = jnp.arange(length, dtype=jnp.int32)
    phase_angle = (
        2.0 * math.pi / length * (index_row[:, None] * index_row[None, :] % length).astype(jnp.float32)
    )
    scaling = 1.0 / math.sqrt(length)
    return (jnp.cos(phase_angle) * scaling, -jnp.sin(phase_angle) * scaling)


def to_columns(real_part, imag_part, link_type):
    stacked = jnp.stack([real_part, imag_part]).astype(link_type)
    moved = lax.all_to_all(stacked, "space", 3, 2, tiled=True).astype(jnp.float32)
    return (moved[0], moved[1])


def to_rows(real_part, imag_part, link_type):
    stacked = jnp.stack([real_part, imag_part]).astype(link_type)
    moved = lax.all_to_all(stacked, "space", 2, 3, tiled=True).astype(jnp.float32)
    return (moved[0], moved[1])


def enter_spectrum(real_part, imag_part, tables_lat, link_type=jnp.float32):
    table_cos, table_sin = tables_lat
    real_part, imag_part = to_columns(real_part, imag_part, link_type)
    return complex_latitude(table_cos, table_sin, real_part, imag_part, False)


def leave_spectrum(real_part, imag_part, tables_lat, link_type=jnp.float32):
    table_cos, table_sin = tables_lat
    real_part, imag_part = complex_latitude(table_cos, table_sin, real_part, imag_part, True)
    return to_rows(real_part, imag_part, link_type)


def complex_operator(real_block, imag_block):
    return jnp.stack(
        [jnp.stack([real_block, -imag_block]), jnp.stack([imag_block, real_block])]
    )


def lat_stacked(operator, field):
    return jnp.einsum("pqkh,qbhlc->pbklc", operator, field, precision=HIGHEST)


def lon_stacked_forward(field, tables):
    return jnp.einsum("brwc,pwk->pbrkc", field, tables, precision=HIGHEST)


def lon_stacked_back(spec, tables):
    return jnp.einsum("pbrkc,pwk->brwc", spec, tables, precision=HIGHEST)


def block_operator(weights):
    return jnp.moveaxis(complex_operator(weights[0], weights[1]), 2, 0)


def block_stacked(field, operator):
    return jnp.einsum("qbklnc,npqce->pbklne", field, operator, precision=HIGHEST)


def block_stacked_adjoint(field, operator):
    return jnp.einsum("pbklne,npqce->qbklnc", field, operator, precision=HIGHEST)


def stacked_columns(field, link_type):
    return lax.all_to_all(field.astype(link_type), "space", 3, 2, tiled=True).astype(jnp.float32)


def stacked_rows(field, link_type):
    return lax.all_to_all(field.astype(link_type), "space", 2, 3, tiled=True).astype(jnp.float32)


def token_sums(first_term, second_term):
    pair = jnp.stack([first_term, second_term])
    count = lax.axis_size("feat")
    position = lax.axis_index("feat")
    shifted = jnp.stack(
        [pair]
        + [
            lax.ppermute(pair, "feat", [(i, (i + count - shift) % count) for i in range(count)])
            for shift in range(1, count)
        ]
    )
    ordered = shifted[(jnp.arange(count) + count - position) % count]
    total = ordered[0]
    for source in range(1, count):
        total = total + ordered[source]
    return (total[0], total[1])


def ring_send(block):
    count = lax.axis_size("feat")
    return [block] + [
        lax.ppermute(block, "feat", [(i, (i + shift) % count) for i in range(count)])
        for shift in range(1, count)
    ]


def ring_assemble(parts):
    count = len(parts)
    position = lax.axis_index("feat")
    block = parts[0]
    width = block.shape[-1]
    whole = jnp.zeros(block.shape[:-1] + (width * count,), block.dtype)
    for shift, moved in enumerate(parts):
        source = (position + count - shift) % count
        whole = lax.dynamic_update_slice_in_dim(whole, moved, source * width, axis=block.ndim - 1)
    return whole


def channel_share(term):
    return lax.psum_scatter(
        term.astype(jnp.bfloat16), "feat", scatter_dimension=3, tiled=True
    ).astype(jnp.float32)


def permute_gather(block):
    return ring_assemble(ring_send(block))


def permute_scatter(term):
    count = lax.axis_size("feat")
    position = lax.axis_index("feat")
    width = term.shape[-1] // count
    total = lax.dynamic_slice_in_dim(term, position * width, width, axis=term.ndim - 1)
    for shift in range(1, count):
        target = (position + shift) % count
        chunk = lax.dynamic_slice_in_dim(term, target * width, width, axis=term.ndim - 1)
        moved = lax.ppermute(
            chunk.astype(jnp.bfloat16), "feat", [(i, (i + shift) % count) for i in range(count)]
        )
        total = total + moved.astype(jnp.float32)
    return total


def split_gather(block):
    return jnp.concatenate(
        [lax.all_gather(block[:1], "feat", axis=3, tiled=True), permute_gather(block[1:])], axis=0
    )


def split_scatter(term):
    return jnp.concatenate([channel_share(term[:1]), permute_scatter(term[1:])], axis=0)


def gelu_value(field):
    return 0.5 * field * (1.0 + lax.erf(field * (1.0 / math.sqrt(2.0))))


def gelu_slope(field):
    return 0.5 * (1.0 + lax.erf(field * (1.0 / math.sqrt(2.0)))) + field * jnp.exp(
        -0.5 * field * field
    ) * (1.0 / math.sqrt(2.0 * math.pi))


def per_device(inputs, cotangent, spec_w1, spec_b1, spec_w2, spec_b2, up_weight, down_weight):
    full_width = up_weight.shape[0]
    block_size = spec_w1.shape[2]
    tables_lon = padded_tables(inputs.shape[2], lax.axis_size("space"))
    tables_lat = latitude_tables(inputs.shape[1] * lax.axis_size("space"))
    cos_fwd, sin_fwd, cos_inv, sin_inv = tables_lon
    table_cos, table_sin = tables_lat
    operators = (
        jnp.stack([cos_fwd, sin_fwd]),
        jnp.stack([cos_inv, sin_inv]),
        complex_operator(table_cos, table_sin),
        complex_operator(table_cos, -table_sin),
        block_operator(spec_w1),
        block_operator(spec_w2),
    )
    operators = lax.optimization_barrier(operators)
    lon_fwd_tables, lon_inv_tables, lat_forward_op, lat_inverse_op, first_op, second_op = operators
    values = inputs.astype(jnp.float32)
    cotangent_parts = ring_send(cotangent)
    first_sum, second_sum = token_sums(jnp.sum(values, axis=-1), jnp.sum(values * values, axis=-1))
    mean_one = first_sum[..., None] / full_width
    rstd_one = lax.rsqrt(second_sum[..., None] / full_width - mean_one * mean_one + EPSILON)
    normed = (values - mean_one) * rstd_one
    spec = lat_stacked(
        lat_forward_op, stacked_columns(lon_stacked_forward(normed, lon_fwd_tables), jnp.float32)
    )
    spec_blocks = to_blocks(spec, block_size)
    bias_one = to_blocks(spec_b1, block_size)[:, None, None, None]
    bias_two = to_blocks(spec_b2, block_size)[:, None, None, None]
    first = jax.nn.relu(block_stacked(spec_blocks, first_op) + bias_one)
    second = block_stacked(first, second_op) + bias_two
    shrunk = (second - jnp.clip(second, -SHRINK_LEVEL, SHRINK_LEVEL)).reshape(spec.shape)
    shrunk, cotangent_parts = lax.optimization_barrier((shrunk, cotangent_parts))
    whole_cotangent = ring_assemble(cotangent_parts)
    filtered = lon_stacked_back(
        stacked_rows(lat_stacked(lat_inverse_op, shrunk), jnp.float32), lon_inv_tables
    )
    residual = (filtered + normed + values).astype(jnp.bfloat16)
    residual_vals = residual.astype(jnp.float32)
    whole_residual = split_gather(residual)
    whole_vals = whole_residual.astype(jnp.float32)
    mean_two = jnp.sum(whole_vals, axis=-1, keepdims=True) / full_width
    square_two = jnp.sum(whole_vals * whole_vals, axis=-1, keepdims=True) / full_width
    rstd_two = lax.rsqrt(square_two - mean_two * mean_two + EPSILON)
    vhat = (whole_vals - mean_two) * rstd_two
    hidden = jnp.einsum(
        "brwd,dh->brwh", vhat.astype(jnp.bfloat16), up_weight, preferred_element_type=jnp.float32
    )
    activated = gelu_value(hidden).astype(jnp.bfloat16)
    mixed_term = jnp.einsum(
        "brwh,hd->brwd", activated, down_weight, preferred_element_type=jnp.float32
    )
    output = (residual_vals + channel_share(mixed_term)).astype(jnp.bfloat16)
    grad_act = jnp.einsum(
        "brwd,hd->brwh", whole_cotangent, down_weight, preferred_element_type=jnp.float32
    )
    grad_hidden = (grad_act * gelu_slope(hidden)).astype(jnp.bfloat16)
    grad_term = jnp.einsum(
        "brwh,dh->brwd", grad_hidden, up_weight, preferred_element_type=jnp.float32
    )
    total_one, total_two = token_sums(
        jnp.sum(grad_term, axis=-1), jnp.sum(grad_term * vhat, axis=-1)
    )
    grad_vhat = split_scatter(grad_term)
    own_hat = (residual_vals - mean_two) * rstd_two
    grad_residual = cotangent.astype(jnp.float32) + rstd_two * (
        grad_vhat
        - total_one[..., None] / full_width
        - own_hat * (total_two[..., None] / full_width)
    )
    grad_spec = lat_stacked(
        lat_forward_op,
        stacked_columns(lon_stacked_forward(grad_residual, lon_inv_tables), jnp.bfloat16),
    )
    grad_second = jnp.where(
        jnp.abs(second) > SHRINK_LEVEL, to_blocks(grad_spec, block_size), 0.0
    )
    grad_first = jnp.where(first > 0.0, block_stacked_adjoint(grad_second, second_op), 0.0)
    grad_spectrum = block_stacked_adjoint(grad_first, first_op).reshape(spec.shape)
    grad_normed = grad_residual + lon_stacked_back(
        stacked_rows(lat_stacked(lat_inverse_op, grad_spectrum), jnp.bfloat16), lon_fwd_tables
    )
    norm_one, norm_two = token_sums(
        jnp.sum(grad_normed, axis=-1), jnp.sum(grad_normed * normed, axis=-1)
    )
    grad_input = grad_residual + rstd_one * (
        grad_normed - norm_one[..., None] / full_width - normed * (norm_two[..., None] / full_width)
    )
    return (output, grad_input.astype(jnp.bfloat16))


def solution(mesh):
    return jax.shard_map(
        per_device,
        mesh=mesh,
        in_specs=(
            P(None, "space", None, "feat"),
            P(None, "space", None, "feat"),
            P(None, "feat", None, None),
            P(None, "feat"),
            P(None, "feat", None, None),
            P(None, "feat"),
            P(None, "feat"),
            P("feat", None),
        ),
        out_specs=(P(None, "space", None, "feat"), P(None, "space", None, "feat")),
        check_vma=False,
    )
```

```python
import math

import jax
import jax.numpy as jnp
from jax import lax
from jax.sharding import PartitionSpec as P

EPSILON = 1e-05
SHRINK_LEVEL = 0.1
HIGHEST = lax.Precision.HIGHEST


def longitude_tables(width_lon):
    mode_count = width_lon // 2 + 1
    cell_index = jnp.arange(width_lon, dtype=jnp.int32)[:, None]
    wave_number = jnp.arange(mode_count, dtype=jnp.int32)[None, :]
    phase_angle = (
        2.0 * math.pi / width_lon * (cell_index * wave_number % width_lon).astype(jnp.float32)
    )
    scaling = 1.0 / math.sqrt(width_lon)
    cos_fwd = jnp.cos(phase_angle) * scaling
    sin_fwd = -jnp.sin(phase_angle) * scaling
    doubled = jnp.where((wave_number == 0) | (wave_number * 2 == width_lon), 1.0, 2.0).astype(
        jnp.float32
    )
    return (cos_fwd, sin_fwd, cos_fwd * doubled, sin_fwd * doubled)


def padded_tables(width_lon, multiple):
    tables = longitude_tables(width_lon)
    modes = tables[0].shape[1]
    extra = -modes % multiple
    return tuple(jnp.pad(table, ((0, 0), (0, extra))) for table in tables)


def lat_apply(table, field):
    return jnp.einsum("gh,bhkc->bgkc", table, field, precision=HIGHEST)


def complex_latitude(table_cos, table_sin, real_part, imag_part, inverse):
    if inverse:
        return (
            lat_apply(table_cos, real_part) + lat_apply(table_sin, imag_part),
            lat_apply(table_cos, imag_part) - lat_apply(table_sin, real_part),
        )
    return (
        lat_apply(table_cos, real_part) - lat_apply(table_sin, imag_part),
        lat_apply(table_cos, imag_part) + lat_apply(table_sin, real_part),
    )


def lon_forward(field, table):
    return jnp.einsum("brwc,wk->brkc", field, table, precision=HIGHEST)


def lon_back(spec, table):
    return jnp.einsum("brkc,wk->brwc", spec, table, precision=HIGHEST)


def to_blocks(field, block_size):
    return field.reshape(field.shape[:-1] + (field.shape[-1] // block_size, block_size))


def block_mult(field, weights):
    return jnp.einsum("...nc,nce->...ne", field, weights, precision=HIGHEST)


def block_mult_back(field, weights):
    return jnp.einsum("...ne,nce->...nc", field, weights, precision=HIGHEST)


def block_product(real_part, imag_part, weights):
    return (
        block_mult(real_part, weights[0]) - block_mult(imag_part, weights[1]),
        block_mult(real_part, weights[1]) + block_mult(imag_part, weights[0]),
    )


def block_adjoint(real_part, imag_part, weights):
    return (
        block_mult_back(real_part, weights[0]) + block_mult_back(imag_part, weights[1]),
        block_mult_back(imag_part, weights[0]) - block_mult_back(real_part, weights[1]),
    )


def latitude_tables(length):
    index_row = jnp.arange(length, dtype=jnp.int32)
    phase_angle = (
        2.0 * math.pi / length * (index_row[:, None] * index_row[None, :] % length).astype(jnp.float32)
    )
    scaling = 1.0 / math.sqrt(length)
    return (jnp.cos(phase_angle) * scaling, -jnp.sin(phase_angle) * scaling)


def to_columns(real_part, imag_part, link_type):
    stacked = jnp.stack([real_part, imag_part]).astype(link_type)
    moved = lax.all_to_all(stacked, "space", 3, 2, tiled=True).astype(jnp.float32)
    return (moved[0], moved[1])


def to_rows(real_part, imag_part, link_type):
    stacked = jnp.stack([real_part, imag_part]).astype(link_type)
    moved = lax.all_to_all(stacked, "space", 2, 3, tiled=True).astype(jnp.float32)
    return (moved[0], moved[1])


def enter_spectrum(real_part, imag_part, tables_lat, link_type=jnp.float32):
    table_cos, table_sin = tables_lat
    real_part, imag_part = to_columns(real_part, imag_part, link_type)
    return complex_latitude(table_cos, table_sin, real_part, imag_part, False)


def leave_spectrum(real_part, imag_part, tables_lat, link_type=jnp.float32):
    table_cos, table_sin = tables_lat
    real_part, imag_part = complex_latitude(table_cos, table_sin, real_part, imag_part, True)
    return to_rows(real_part, imag_part, link_type)


def complex_operator(real_block, imag_block):
    return jnp.stack(
        [jnp.stack([real_block, -imag_block]), jnp.stack([imag_block, real_block])]
    )


def lat_stacked(operator, field):
    return jnp.einsum("pqkh,qbhlc->pbklc", operator, field, precision=lax.Precision.HIGH)


def lon_stacked_forward(field, tables):
    return jnp.einsum("brwc,pwk->pbrkc", field, tables, precision=lax.Precision.HIGH)


def lon_stacked_back(spec, tables):
    return jnp.einsum("pbrkc,pwk->brwc", spec, tables, precision=lax.Precision.HIGH)


def block_operator(weights):
    return jnp.moveaxis(complex_operator(weights[0], weights[1]), 2, 0)


def block_stacked(field, operator):
    return jnp.einsum("qbklnc,npqce->pbklne", field, operator, precision=lax.Precision.HIGH)


def block_stacked_adjoint(field, operator):
    return jnp.einsum("pbklne,npqce->qbklnc", field, operator, precision=lax.Precision.HIGH)


def stacked_columns(field, link_type):
    return lax.all_to_all(field.astype(link_type), "space", 3, 2, tiled=True).astype(jnp.float32)


def stacked_rows(field, link_type):
    return lax.all_to_all(field.astype(link_type), "space", 2, 3, tiled=True).astype(jnp.float32)


def token_sums(first_term, second_term):
    pair = jnp.stack([first_term, second_term])
    count = lax.axis_size("feat")
    position = lax.axis_index("feat")
    shifted = jnp.stack(
        [pair]
        + [
            lax.ppermute(pair, "feat", [(i, (i + count - shift) % count) for i in range(count)])
            for shift in range(1, count)
        ]
    )
    ordered = shifted[(jnp.arange(count) + count - position) % count]
    total = ordered[0]
    for source in range(1, count):
        total = total + ordered[source]
    return (total[0], total[1])


def ring_send(block):
    count = lax.axis_size("feat")
    return [block] + [
        lax.ppermute(block, "feat", [(i, (i + shift) % count) for i in range(count)])
        for shift in range(1, count)
    ]


def ring_assemble(parts):
    count = len(parts)
    position = lax.axis_index("feat")
    block = parts[0]
    width = block.shape[-1]
    whole = jnp.zeros(block.shape[:-1] + (width * count,), block.dtype)
    for shift, moved in enumerate(parts):
        source = (position + count - shift) % count
        whole = lax.dynamic_update_slice_in_dim(whole, moved, source * width, axis=block.ndim - 1)
    return whole


def channel_share(term):
    return lax.psum_scatter(
        term.astype(jnp.bfloat16), "feat", scatter_dimension=3, tiled=True
    ).astype(jnp.float32)


def gelu_value(field):
    return 0.5 * field * (1.0 + lax.erf(field * (1.0 / math.sqrt(2.0))))


def gelu_slope(field):
    return 0.5 * (1.0 + lax.erf(field * (1.0 / math.sqrt(2.0)))) + field * jnp.exp(
        -0.5 * field * field
    ) * (1.0 / math.sqrt(2.0 * math.pi))


def per_device(inputs, cotangent, spec_w1, spec_b1, spec_w2, spec_b2, up_weight, down_weight):
    full_width = up_weight.shape[0]
    block_size = spec_w1.shape[2]
    tables_lon = padded_tables(inputs.shape[2], lax.axis_size("space"))
    tables_lat = latitude_tables(inputs.shape[1] * lax.axis_size("space"))
    cos_fwd, sin_fwd, cos_inv, sin_inv = tables_lon
    table_cos, table_sin = tables_lat
    operators = (
        jnp.stack([cos_fwd, sin_fwd]),
        jnp.stack([cos_inv, sin_inv]),
        complex_operator(table_cos, table_sin),
        complex_operator(table_cos, -table_sin),
        block_operator(spec_w1),
        block_operator(spec_w2),
    )
    operators = lax.optimization_barrier(operators)
    lon_fwd_tables, lon_inv_tables, lat_forward_op, lat_inverse_op, first_op, second_op = operators
    values = inputs.astype(jnp.float32)
    cotangent_parts = ring_send(cotangent)
    first_sum, second_sum = token_sums(jnp.sum(values, axis=-1), jnp.sum(values * values, axis=-1))
    mean_one = first_sum[..., None] / full_width
    rstd_one = lax.rsqrt(second_sum[..., None] / full_width - mean_one * mean_one + EPSILON)
    normed = (values - mean_one) * rstd_one
    spec = lat_stacked(
        lat_forward_op, stacked_columns(lon_stacked_forward(normed, lon_fwd_tables), jnp.float32)
    )
    spec_blocks = to_blocks(spec, block_size)
    bias_one = to_blocks(spec_b1, block_size)[:, None, None, None]
    bias_two = to_blocks(spec_b2, block_size)[:, None, None, None]
    first = jax.nn.relu(block_stacked(spec_blocks, first_op) + bias_one)
    second = block_stacked(first, second_op) + bias_two
    shrunk = (second - jnp.clip(second, -SHRINK_LEVEL, SHRINK_LEVEL)).reshape(spec.shape)
    shrunk, cotangent_parts = lax.optimization_barrier((shrunk, cotangent_parts))
    whole_cotangent = ring_assemble(cotangent_parts)
    filtered = lon_stacked_back(
        stacked_rows(lat_stacked(lat_inverse_op, shrunk), jnp.float32), lon_inv_tables
    )
    residual = (filtered + normed + values).astype(jnp.bfloat16)
    residual_vals = residual.astype(jnp.float32)
    whole_residual = lax.all_gather(residual, "feat", axis=3, tiled=True)
    whole_vals = whole_residual.astype(jnp.float32)
    mean_two = jnp.sum(whole_vals, axis=-1, keepdims=True) / full_width
    square_two = jnp.sum(whole_vals * whole_vals, axis=-1, keepdims=True) / full_width
    rstd_two = lax.rsqrt(square_two - mean_two * mean_two + EPSILON)
    vhat = (whole_vals - mean_two) * rstd_two
    hidden = jnp.einsum(
        "brwd,dh->brwh", vhat.astype(jnp.bfloat16), up_weight, preferred_element_type=jnp.float32
    )
    activated = gelu_value(hidden).astype(jnp.bfloat16)
    mixed_term = jnp.einsum(
        "brwh,hd->brwd", activated, down_weight, preferred_element_type=jnp.float32
    )
    output = (residual_vals + channel_share(mixed_term)).astype(jnp.bfloat16)
    grad_act = jnp.einsum(
        "brwd,hd->brwh", whole_cotangent, down_weight, preferred_element_type=jnp.float32
    )
    grad_hidden = (grad_act * gelu_slope(hidden)).astype(jnp.bfloat16)
    grad_term = jnp.einsum(
        "brwh,dh->brwd", grad_hidden, up_weight, preferred_element_type=jnp.float32
    )
    total_one, total_two = token_sums(
        jnp.sum(grad_term, axis=-1), jnp.sum(grad_term * vhat, axis=-1)
    )
    grad_vhat = channel_share(grad_term)
    own_hat = (residual_vals - mean_two) * rstd_two
    grad_residual = cotangent.astype(jnp.float32) + rstd_two * (
        grad_vhat
        - total_one[..., None] / full_width
        - own_hat * (total_two[..., None] / full_width)
    )
    grad_spec = lat_stacked(
        lat_forward_op,
        stacked_columns(lon_stacked_forward(grad_residual, lon_inv_tables), jnp.bfloat16),
    )
    grad_second = jnp.where(
        jnp.abs(second) > SHRINK_LEVEL, to_blocks(grad_spec, block_size), 0.0
    )
    grad_first = jnp.where(first > 0.0, block_stacked_adjoint(grad_second, second_op), 0.0)
    grad_spectrum = block_stacked_adjoint(grad_first, first_op).reshape(spec.shape)
    grad_normed = grad_residual + lon_stacked_back(
        stacked_rows(lat_stacked(lat_inverse_op, grad_spectrum), jnp.bfloat16), lon_fwd_tables
    )
    norm_one, norm_two = token_sums(
        jnp.sum(grad_normed, axis=-1), jnp.sum(grad_normed * normed, axis=-1)
    )
    grad_input = grad_residual + rstd_one * (
        grad_normed - norm_one[..., None] / full_width - normed * (norm_two[..., None] / full_width)
    )
    return (output, grad_input.astype(jnp.bfloat16))


def solution(mesh):
    return jax.shard_map(
        per_device,
        mesh=mesh,
        in_specs=(
            P(None, "space", None, "feat"),
            P(None, "space", None, "feat"),
            P(None, "feat", None, None),
            P(None, "feat"),
            P(None, "feat", None, None),
            P(None, "feat"),
            P(None, "feat"),
            P("feat", None),
        ),
        out_specs=(P(None, "space", None, "feat"), P(None, "space", None, "feat")),
        check_vma=False,
    )
```

```python
import math

import jax
import jax.numpy as jnp
from jax import lax
from jax.sharding import PartitionSpec as P

EPSILON = 1e-05
SHRINK_LEVEL = 0.1
HIGHEST = lax.Precision.HIGHEST


def longitude_tables(width_lon):
    mode_count = width_lon // 2 + 1
    cell_index = jnp.arange(width_lon, dtype=jnp.int32)[:, None]
    wave_number = jnp.arange(mode_count, dtype=jnp.int32)[None, :]
    phase_angle = (
        2.0 * math.pi / width_lon * (cell_index * wave_number % width_lon).astype(jnp.float32)
    )
    scaling = 1.0 / math.sqrt(width_lon)
    cos_fwd = jnp.cos(phase_angle) * scaling
    sin_fwd = -jnp.sin(phase_angle) * scaling
    doubled = jnp.where((wave_number == 0) | (wave_number * 2 == width_lon), 1.0, 2.0).astype(
        jnp.float32
    )
    return (cos_fwd, sin_fwd, cos_fwd * doubled, sin_fwd * doubled)


def padded_tables(width_lon, multiple):
    tables = longitude_tables(width_lon)
    modes = tables[0].shape[1]
    extra = -modes % multiple
    return tuple(jnp.pad(table, ((0, 0), (0, extra))) for table in tables)


def lat_apply(table, field):
    return jnp.einsum("gh,bhkc->bgkc", table, field, precision=HIGHEST)


def complex_latitude(table_cos, table_sin, real_part, imag_part, inverse):
    if inverse:
        return (
            lat_apply(table_cos, real_part) + lat_apply(table_sin, imag_part),
            lat_apply(table_cos, imag_part) - lat_apply(table_sin, real_part),
        )
    return (
        lat_apply(table_cos, real_part) - lat_apply(table_sin, imag_part),
        lat_apply(table_cos, imag_part) + lat_apply(table_sin, real_part),
    )


def lon_forward(field, table):
    return jnp.einsum("brwc,wk->brkc", field, table, precision=HIGHEST)


def lon_back(spec, table):
    return jnp.einsum("brkc,wk->brwc", spec, table, precision=HIGHEST)


def to_blocks(field, block_size):
    return field.reshape(field.shape[:-1] + (field.shape[-1] // block_size, block_size))


def block_mult(field, weights):
    return jnp.einsum("...nc,nce->...ne", field, weights, precision=HIGHEST)


def block_mult_back(field, weights):
    return jnp.einsum("...ne,nce->...nc", field, weights, precision=HIGHEST)


def block_product(real_part, imag_part, weights):
    return (
        block_mult(real_part, weights[0]) - block_mult(imag_part, weights[1]),
        block_mult(real_part, weights[1]) + block_mult(imag_part, weights[0]),
    )


def block_adjoint(real_part, imag_part, weights):
    return (
        block_mult_back(real_part, weights[0]) + block_mult_back(imag_part, weights[1]),
        block_mult_back(imag_part, weights[0]) - block_mult_back(real_part, weights[1]),
    )


def latitude_tables(length):
    index_row = jnp.arange(length, dtype=jnp.int32)
    phase_angle = (
        2.0 * math.pi / length * (index_row[:, None] * index_row[None, :] % length).astype(jnp.float32)
    )
    scaling = 1.0 / math.sqrt(length)
    return (jnp.cos(phase_angle) * scaling, -jnp.sin(phase_angle) * scaling)


def to_columns(real_part, imag_part, link_type):
    stacked = jnp.stack([real_part, imag_part]).astype(link_type)
    moved = lax.all_to_all(stacked, "space", 3, 2, tiled=True).astype(jnp.float32)
    return (moved[0], moved[1])


def to_rows(real_part, imag_part, link_type):
    stacked = jnp.stack([real_part, imag_part]).astype(link_type)
    moved = lax.all_to_all(stacked, "space", 2, 3, tiled=True).astype(jnp.float32)
    return (moved[0], moved[1])


def enter_spectrum(real_part, imag_part, tables_lat, link_type=jnp.float32):
    table_cos, table_sin = tables_lat
    real_part, imag_part = to_columns(real_part, imag_part, link_type)
    return complex_latitude(table_cos, table_sin, real_part, imag_part, False)


def leave_spectrum(real_part, imag_part, tables_lat, link_type=jnp.float32):
    table_cos, table_sin = tables_lat
    real_part, imag_part = complex_latitude(table_cos, table_sin, real_part, imag_part, True)
    return to_rows(real_part, imag_part, link_type)


def complex_operator(real_block, imag_block):
    return jnp.stack(
        [jnp.stack([real_block, -imag_block]), jnp.stack([imag_block, real_block])]
    )


def lat_stacked(operator, field):
    return jnp.einsum("pqkh,qbhlc->pbklc", operator, field, precision=lax.Precision.HIGH)


def lon_stacked_forward(field, tables):
    return jnp.einsum("brwc,pwk->pbrkc", field, tables, precision=lax.Precision.HIGH)


def lon_stacked_back(spec, tables):
    return jnp.einsum("pbrkc,pwk->brwc", spec, tables, precision=lax.Precision.HIGH)


def block_operator(weights):
    return jnp.moveaxis(complex_operator(weights[0], weights[1]), 2, 0)


def block_stacked(field, operator):
    return jnp.einsum("qbklnc,npqce->pbklne", field, operator, precision=lax.Precision.HIGH)


def block_stacked_adjoint(field, operator):
    return jnp.einsum("pbklne,npqce->qbklnc", field, operator, precision=lax.Precision.HIGH)


def stacked_columns(field, link_type):
    return lax.all_to_all(field.astype(link_type), "space", 3, 2, tiled=True).astype(jnp.float32)


def stacked_rows(field, link_type):
    return lax.all_to_all(field.astype(link_type), "space", 2, 3, tiled=True).astype(jnp.float32)


def token_sums(first_term, second_term):
    pair = jnp.stack([first_term, second_term])
    count = lax.axis_size("feat")
    position = lax.axis_index("feat")
    shifted = jnp.stack(
        [pair]
        + [
            lax.ppermute(pair, "feat", [(i, (i + count - shift) % count) for i in range(count)])
            for shift in range(1, count)
        ]
    )
    ordered = shifted[(jnp.arange(count) + count - position) % count]
    total = ordered[0]
    for source in range(1, count):
        total = total + ordered[source]
    return (total[0], total[1])


def ring_send(block):
    count = lax.axis_size("feat")
    return [block] + [
        lax.ppermute(block, "feat", [(i, (i + shift) % count) for i in range(count)])
        for shift in range(1, count)
    ]


def ring_assemble(parts):
    count = len(parts)
    position = lax.axis_index("feat")
    block = parts[0]
    width = block.shape[-1]
    whole = jnp.zeros(block.shape[:-1] + (width * count,), block.dtype)
    for shift, moved in enumerate(parts):
        source = (position + count - shift) % count
        whole = lax.dynamic_update_slice_in_dim(whole, moved, source * width, axis=block.ndim - 1)
    return whole


def channel_share(term):
    return lax.psum_scatter(
        term.astype(jnp.bfloat16), "feat", scatter_dimension=3, tiled=True
    ).astype(jnp.float32)


def gelu_value(field):
    return 0.5 * field * (1.0 + lax.erf(field * (1.0 / math.sqrt(2.0))))


def gelu_slope(field):
    return 0.5 * (1.0 + lax.erf(field * (1.0 / math.sqrt(2.0)))) + field * jnp.exp(
        -0.5 * field * field
    ) * (1.0 / math.sqrt(2.0 * math.pi))


def per_device(inputs, cotangent, spec_w1, spec_b1, spec_w2, spec_b2, up_weight, down_weight):
    full_width = up_weight.shape[0]
    block_size = spec_w1.shape[2]
    tables_lon = padded_tables(inputs.shape[2], lax.axis_size("space"))
    tables_lat = latitude_tables(inputs.shape[1] * lax.axis_size("space"))
    cos_fwd, sin_fwd, cos_inv, sin_inv = tables_lon
    table_cos, table_sin = tables_lat
    operators = (
        jnp.stack([cos_fwd, sin_fwd]),
        jnp.stack([cos_inv, sin_inv]),
        complex_operator(table_cos, table_sin),
        complex_operator(table_cos, -table_sin),
        block_operator(spec_w1),
        block_operator(spec_w2),
    )
    operators = lax.optimization_barrier(operators)
    lon_fwd_tables, lon_inv_tables, lat_forward_op, lat_inverse_op, first_op, second_op = operators
    values = inputs.astype(jnp.float32)
    cotangent_parts = ring_send(cotangent)
    first_sum, second_sum = token_sums(jnp.sum(values, axis=-1), jnp.sum(values * values, axis=-1))
    mean_one = first_sum[..., None] / full_width
    rstd_one = lax.rsqrt(second_sum[..., None] / full_width - mean_one * mean_one + EPSILON)
    normed = (values - mean_one) * rstd_one
    spec = lat_stacked(
        lat_forward_op, stacked_columns(lon_stacked_forward(normed, lon_fwd_tables), jnp.float32)
    )
    spec_blocks = to_blocks(spec, block_size)
    bias_one = to_blocks(spec_b1, block_size)[:, None, None, None]
    bias_two = to_blocks(spec_b2, block_size)[:, None, None, None]
    first = jax.nn.relu(block_stacked(spec_blocks, first_op) + bias_one)
    second = block_stacked(first, second_op) + bias_two
    shrunk = (second - jnp.clip(second, -SHRINK_LEVEL, SHRINK_LEVEL)).reshape(spec.shape)
    shrunk, cotangent_parts = lax.optimization_barrier((shrunk, cotangent_parts))
    whole_cotangent = ring_assemble(cotangent_parts)
    filtered = lon_stacked_back(
        stacked_rows(lat_stacked(lat_inverse_op, shrunk), jnp.float32), lon_inv_tables
    )
    residual = (filtered + normed + values).astype(jnp.bfloat16)
    residual_vals = residual.astype(jnp.float32)
    whole_residual = lax.all_gather(residual, "feat", axis=3, tiled=True)
    grad_act = jnp.einsum(
        "brwd,hd->brwh", whole_cotangent, down_weight, preferred_element_type=jnp.float32
    )
    whole_residual, grad_act = lax.optimization_barrier((whole_residual, grad_act))
    whole_vals = whole_residual.astype(jnp.float32)
    mean_two = jnp.sum(whole_vals, axis=-1, keepdims=True) / full_width
    square_two = jnp.sum(whole_vals * whole_vals, axis=-1, keepdims=True) / full_width
    rstd_two = lax.rsqrt(square_two - mean_two * mean_two + EPSILON)
    vhat = (whole_vals - mean_two) * rstd_two
    hidden = jnp.einsum(
        "brwd,dh->brwh", vhat.astype(jnp.bfloat16), up_weight, preferred_element_type=jnp.float32
    )
    activated = gelu_value(hidden).astype(jnp.bfloat16)
    mixed_term = jnp.einsum(
        "brwh,hd->brwd", activated, down_weight, preferred_element_type=jnp.float32
    )
    output = (residual_vals + channel_share(mixed_term)).astype(jnp.bfloat16)
    grad_hidden = (grad_act * gelu_slope(hidden)).astype(jnp.bfloat16)
    grad_term = jnp.einsum(
        "brwh,dh->brwd", grad_hidden, up_weight, preferred_element_type=jnp.float32
    )
    total_one, total_two = token_sums(
        jnp.sum(grad_term, axis=-1), jnp.sum(grad_term * vhat, axis=-1)
    )
    grad_vhat = channel_share(grad_term)
    own_hat = (residual_vals - mean_two) * rstd_two
    grad_residual = cotangent.astype(jnp.float32) + rstd_two * (
        grad_vhat
        - total_one[..., None] / full_width
        - own_hat * (total_two[..., None] / full_width)
    )
    grad_spec = lat_stacked(
        lat_forward_op,
        stacked_columns(lon_stacked_forward(grad_residual, lon_inv_tables), jnp.bfloat16),
    )
    grad_second = jnp.where(
        jnp.abs(second) > SHRINK_LEVEL, to_blocks(grad_spec, block_size), 0.0
    )
    grad_first = jnp.where(first > 0.0, block_stacked_adjoint(grad_second, second_op), 0.0)
    grad_spectrum = block_stacked_adjoint(grad_first, first_op).reshape(spec.shape)
    grad_normed = grad_residual + lon_stacked_back(
        stacked_rows(lat_stacked(lat_inverse_op, grad_spectrum), jnp.bfloat16), lon_fwd_tables
    )
    norm_one, norm_two = token_sums(
        jnp.sum(grad_normed, axis=-1), jnp.sum(grad_normed * normed, axis=-1)
    )
    grad_input = grad_residual + rstd_one * (
        grad_normed - norm_one[..., None] / full_width - normed * (norm_two[..., None] / full_width)
    )
    return (output, grad_input.astype(jnp.bfloat16))


def solution(mesh):
    return jax.shard_map(
        per_device,
        mesh=mesh,
        in_specs=(
            P(None, "space", None, "feat"),
            P(None, "space", None, "feat"),
            P(None, "feat", None, None),
            P(None, "feat"),
            P(None, "feat", None, None),
            P(None, "feat"),
            P(None, "feat"),
            P("feat", None),
        ),
        out_specs=(P(None, "space", None, "feat"), P(None, "space", None, "feat")),
        check_vma=False,
    )
```

```python
import math

import jax
import jax.numpy as jnp
from jax import lax
from jax.sharding import PartitionSpec as P

EPSILON = 1e-05
SHRINK_LEVEL = 0.1
HIGHEST = lax.Precision.HIGHEST


def longitude_tables(width_lon):
    mode_count = width_lon // 2 + 1
    cell_index = jnp.arange(width_lon, dtype=jnp.int32)[:, None]
    wave_number = jnp.arange(mode_count, dtype=jnp.int32)[None, :]
    phase_angle = (
        2.0 * math.pi / width_lon * (cell_index * wave_number % width_lon).astype(jnp.float32)
    )
    scaling = 1.0 / math.sqrt(width_lon)
    cos_fwd = jnp.cos(phase_angle) * scaling
    sin_fwd = -jnp.sin(phase_angle) * scaling
    doubled = jnp.where((wave_number == 0) | (wave_number * 2 == width_lon), 1.0, 2.0).astype(
        jnp.float32
    )
    return (cos_fwd, sin_fwd, cos_fwd * doubled, sin_fwd * doubled)


def padded_tables(width_lon, multiple):
    tables = longitude_tables(width_lon)
    modes = tables[0].shape[1]
    extra = -modes % multiple
    return tuple(jnp.pad(table, ((0, 0), (0, extra))) for table in tables)


def lat_apply(table, field):
    return jnp.einsum("gh,bhkc->bgkc", table, field, precision=HIGHEST)


def complex_latitude(table_cos, table_sin, real_part, imag_part, inverse):
    if inverse:
        return (
            lat_apply(table_cos, real_part) + lat_apply(table_sin, imag_part),
            lat_apply(table_cos, imag_part) - lat_apply(table_sin, real_part),
        )
    return (
        lat_apply(table_cos, real_part) - lat_apply(table_sin, imag_part),
        lat_apply(table_cos, imag_part) + lat_apply(table_sin, real_part),
    )


def lon_forward(field, table):
    return jnp.einsum("brwc,wk->brkc", field, table, precision=HIGHEST)


def lon_back(spec, table):
    return jnp.einsum("brkc,wk->brwc", spec, table, precision=HIGHEST)


def to_blocks(field, block_size):
    return field.reshape(field.shape[:-1] + (field.shape[-1] // block_size, block_size))


def block_mult(field, weights):
    return jnp.einsum("...nc,nce->...ne", field, weights, precision=HIGHEST)


def block_mult_back(field, weights):
    return jnp.einsum("...ne,nce->...nc", field, weights, precision=HIGHEST)


def block_product(real_part, imag_part, weights):
    return (
        block_mult(real_part, weights[0]) - block_mult(imag_part, weights[1]),
        block_mult(real_part, weights[1]) + block_mult(imag_part, weights[0]),
    )


def block_adjoint(real_part, imag_part, weights):
    return (
        block_mult_back(real_part, weights[0]) + block_mult_back(imag_part, weights[1]),
        block_mult_back(imag_part, weights[0]) - block_mult_back(real_part, weights[1]),
    )


def latitude_tables(length):
    index_row = jnp.arange(length, dtype=jnp.int32)
    phase_angle = (
        2.0 * math.pi / length * (index_row[:, None] * index_row[None, :] % length).astype(jnp.float32)
    )
    scaling = 1.0 / math.sqrt(length)
    return (jnp.cos(phase_angle) * scaling, -jnp.sin(phase_angle) * scaling)


def to_columns(real_part, imag_part, link_type):
    stacked = jnp.stack([real_part, imag_part]).astype(link_type)
    moved = lax.all_to_all(stacked, "space", 3, 2, tiled=True).astype(jnp.float32)
    return (moved[0], moved[1])


def to_rows(real_part, imag_part, link_type):
    stacked = jnp.stack([real_part, imag_part]).astype(link_type)
    moved = lax.all_to_all(stacked, "space", 2, 3, tiled=True).astype(jnp.float32)
    return (moved[0], moved[1])


def enter_spectrum(real_part, imag_part, tables_lat, link_type=jnp.float32):
    table_cos, table_sin = tables_lat
    real_part, imag_part = to_columns(real_part, imag_part, link_type)
    return complex_latitude(table_cos, table_sin, real_part, imag_part, False)


def leave_spectrum(real_part, imag_part, tables_lat, link_type=jnp.float32):
    table_cos, table_sin = tables_lat
    real_part, imag_part = complex_latitude(table_cos, table_sin, real_part, imag_part, True)
    return to_rows(real_part, imag_part, link_type)


def complex_operator(real_block, imag_block):
    return jnp.stack(
        [jnp.stack([real_block, -imag_block]), jnp.stack([imag_block, real_block])]
    )


def lat_stacked(operator, field):
    return jnp.einsum("pqkh,qbhlc->pbklc", operator, field, precision=lax.Precision.HIGH)


def lon_stacked_forward(field, tables):
    return jnp.einsum("brwc,pwk->pbrkc", field, tables, precision=lax.Precision.HIGH)


def lon_stacked_back(spec, tables):
    return jnp.einsum("pbrkc,pwk->brwc", spec, tables, precision=lax.Precision.HIGH)


def block_operator(weights):
    return jnp.moveaxis(complex_operator(weights[0], weights[1]), 2, 0)


def block_stacked(field, operator):
    return jnp.einsum("qbklnc,npqce->pbklne", field, operator, precision=lax.Precision.HIGH)


def block_stacked_adjoint(field, operator):
    return jnp.einsum("pbklne,npqce->qbklnc", field, operator, precision=lax.Precision.HIGH)


def stacked_columns(field, link_type):
    return lax.all_to_all(field.astype(link_type), "space", 3, 2, tiled=True).astype(jnp.float32)


def stacked_rows(field, link_type):
    return lax.all_to_all(field.astype(link_type), "space", 2, 3, tiled=True).astype(jnp.float32)


def token_sums(first_term, second_term):
    pair = jnp.stack([first_term, second_term])
    count = lax.axis_size("feat")
    position = lax.axis_index("feat")
    shifted = jnp.stack(
        [pair]
        + [
            lax.ppermute(pair, "feat", [(i, (i + count - shift) % count) for i in range(count)])
            for shift in range(1, count)
        ]
    )
    ordered = shifted[(jnp.arange(count) + count - position) % count]
    total = ordered[0]
    for source in range(1, count):
        total = total + ordered[source]
    return (total[0], total[1])


def ring_send(block):
    count = lax.axis_size("feat")
    return [block] + [
        lax.ppermute(block, "feat", [(i, (i + shift) % count) for i in range(count)])
        for shift in range(1, count)
    ]


def ring_assemble(parts):
    count = len(parts)
    position = lax.axis_index("feat")
    block = parts[0]
    width = block.shape[-1]
    whole = jnp.zeros(block.shape[:-1] + (width * count,), block.dtype)
    for shift, moved in enumerate(parts):
        source = (position + count - shift) % count
        whole = lax.dynamic_update_slice_in_dim(whole, moved, source * width, axis=block.ndim - 1)
    return whole


def channel_share(term):
    count = lax.axis_size("feat")
    width = term.shape[-1] // count
    chunks = jnp.stack([term[..., j * width : (j + 1) * width] for j in range(count)])
    got = lax.all_to_all(chunks.astype(jnp.bfloat16), "feat", 0, 0, tiled=True)
    total = got[0].astype(jnp.float32)
    for source in range(1, count):
        total = total + got[source].astype(jnp.float32)
    return total


def channel_gather(block):
    count = lax.axis_size("feat")
    copies = jnp.broadcast_to(block[None], (count,) + block.shape)
    got = lax.all_to_all(copies, "feat", 0, 0, tiled=True)
    return jnp.concatenate([got[j] for j in range(count)], axis=-1)


def gelu_value(field):
    return 0.5 * field * (1.0 + lax.erf(field * (1.0 / math.sqrt(2.0))))


def gelu_slope(field):
    return 0.5 * (1.0 + lax.erf(field * (1.0 / math.sqrt(2.0)))) + field * jnp.exp(
        -0.5 * field * field
    ) * (1.0 / math.sqrt(2.0 * math.pi))


def per_device(inputs, cotangent, spec_w1, spec_b1, spec_w2, spec_b2, up_weight, down_weight):
    full_width = up_weight.shape[0]
    block_size = spec_w1.shape[2]
    tables_lon = padded_tables(inputs.shape[2], lax.axis_size("space"))
    tables_lat = latitude_tables(inputs.shape[1] * lax.axis_size("space"))
    cos_fwd, sin_fwd, cos_inv, sin_inv = tables_lon
    table_cos, table_sin = tables_lat
    operators = (
        jnp.stack([cos_fwd, sin_fwd]),
        jnp.stack([cos_inv, sin_inv]),
        complex_operator(table_cos, table_sin),
        complex_operator(table_cos, -table_sin),
        block_operator(spec_w1),
        block_operator(spec_w2),
    )
    operators = lax.optimization_barrier(operators)
    lon_fwd_tables, lon_inv_tables, lat_forward_op, lat_inverse_op, first_op, second_op = operators
    values = inputs.astype(jnp.float32)
    cotangent_parts = ring_send(cotangent)
    first_sum, second_sum = token_sums(jnp.sum(values, axis=-1), jnp.sum(values * values, axis=-1))
    mean_one = first_sum[..., None] / full_width
    rstd_one = lax.rsqrt(second_sum[..., None] / full_width - mean_one * mean_one + EPSILON)
    normed = (values - mean_one) * rstd_one
    spec = lat_stacked(
        lat_forward_op, stacked_columns(lon_stacked_forward(normed, lon_fwd_tables), jnp.float32)
    )
    spec_blocks = to_blocks(spec, block_size)
    bias_one = to_blocks(spec_b1, block_size)[:, None, None, None]
    bias_two = to_blocks(spec_b2, block_size)[:, None, None, None]
    first = jax.nn.relu(block_stacked(spec_blocks, first_op) + bias_one)
    second = block_stacked(first, second_op) + bias_two
    shrunk = (second - jnp.clip(second, -SHRINK_LEVEL, SHRINK_LEVEL)).reshape(spec.shape)
    shrunk, cotangent_parts = lax.optimization_barrier((shrunk, cotangent_parts))
    whole_cotangent = ring_assemble(cotangent_parts)
    filtered = lon_stacked_back(
        stacked_rows(lat_stacked(lat_inverse_op, shrunk), jnp.float32), lon_inv_tables
    )
    residual = (filtered + normed + values).astype(jnp.bfloat16)
    residual_vals = residual.astype(jnp.float32)
    whole_residual = channel_gather(residual)
    grad_act = jnp.einsum(
        "brwd,hd->brwh", whole_cotangent, down_weight, preferred_element_type=jnp.float32
    )
    whole_residual, grad_act = lax.optimization_barrier((whole_residual, grad_act))
    whole_vals = whole_residual.astype(jnp.float32)
    mean_two = jnp.sum(whole_vals, axis=-1, keepdims=True) / full_width
    square_two = jnp.sum(whole_vals * whole_vals, axis=-1, keepdims=True) / full_width
    rstd_two = lax.rsqrt(square_two - mean_two * mean_two + EPSILON)
    vhat = (whole_vals - mean_two) * rstd_two
    hidden = jnp.einsum(
        "brwd,dh->brwh", vhat.astype(jnp.bfloat16), up_weight, preferred_element_type=jnp.float32
    )
    activated = gelu_value(hidden).astype(jnp.bfloat16)
    mixed_term = jnp.einsum(
        "brwh,hd->brwd", activated, down_weight, preferred_element_type=jnp.float32
    )
    output = (residual_vals + channel_share(mixed_term)).astype(jnp.bfloat16)
    grad_hidden = (grad_act * gelu_slope(hidden)).astype(jnp.bfloat16)
    grad_term = jnp.einsum(
        "brwh,dh->brwd", grad_hidden, up_weight, preferred_element_type=jnp.float32
    )
    total_one, total_two = token_sums(
        jnp.sum(grad_term, axis=-1), jnp.sum(grad_term * vhat, axis=-1)
    )
    grad_vhat = channel_share(grad_term)
    own_hat = (residual_vals - mean_two) * rstd_two
    grad_residual = cotangent.astype(jnp.float32) + rstd_two * (
        grad_vhat
        - total_one[..., None] / full_width
        - own_hat * (total_two[..., None] / full_width)
    )
    grad_spec = lat_stacked(
        lat_forward_op,
        stacked_columns(lon_stacked_forward(grad_residual, lon_inv_tables), jnp.bfloat16),
    )
    grad_second = jnp.where(
        jnp.abs(second) > SHRINK_LEVEL, to_blocks(grad_spec, block_size), 0.0
    )
    grad_first = jnp.where(first > 0.0, block_stacked_adjoint(grad_second, second_op), 0.0)
    grad_spectrum = block_stacked_adjoint(grad_first, first_op).reshape(spec.shape)
    grad_normed = grad_residual + lon_stacked_back(
        stacked_rows(lat_stacked(lat_inverse_op, grad_spectrum), jnp.bfloat16), lon_fwd_tables
    )
    norm_one, norm_two = token_sums(
        jnp.sum(grad_normed, axis=-1), jnp.sum(grad_normed * normed, axis=-1)
    )
    grad_input = grad_residual + rstd_one * (
        grad_normed - norm_one[..., None] / full_width - normed * (norm_two[..., None] / full_width)
    )
    return (output, grad_input.astype(jnp.bfloat16))


def solution(mesh):
    return jax.shard_map(
        per_device,
        mesh=mesh,
        in_specs=(
            P(None, "space", None, "feat"),
            P(None, "space", None, "feat"),
            P(None, "feat", None, None),
            P(None, "feat"),
            P(None, "feat", None, None),
            P(None, "feat"),
            P(None, "feat"),
            P("feat", None),
        ),
        out_specs=(P(None, "space", None, "feat"), P(None, "space", None, "feat")),
        check_vma=False,
    )
```

```python
import math

import jax
import jax.numpy as jnp
from jax import lax
from jax.sharding import PartitionSpec as P

EPSILON = 1e-05
SHRINK_LEVEL = 0.1
HIGHEST = lax.Precision.HIGHEST


def longitude_tables(width_lon):
    mode_count = width_lon // 2 + 1
    cell_index = jnp.arange(width_lon, dtype=jnp.int32)[:, None]
    wave_number = jnp.arange(mode_count, dtype=jnp.int32)[None, :]
    phase_angle = (
        2.0 * math.pi / width_lon * (cell_index * wave_number % width_lon).astype(jnp.float32)
    )
    scaling = 1.0 / math.sqrt(width_lon)
    cos_fwd = jnp.cos(phase_angle) * scaling
    sin_fwd = -jnp.sin(phase_angle) * scaling
    doubled = jnp.where((wave_number == 0) | (wave_number * 2 == width_lon), 1.0, 2.0).astype(
        jnp.float32
    )
    return (cos_fwd, sin_fwd, cos_fwd * doubled, sin_fwd * doubled)


def padded_tables(width_lon, multiple):
    tables = longitude_tables(width_lon)
    modes = tables[0].shape[1]
    extra = -modes % multiple
    return tuple(jnp.pad(table, ((0, 0), (0, extra))) for table in tables)


def lat_apply(table, field):
    return jnp.einsum("gh,bhkc->bgkc", table, field, precision=HIGHEST)


def complex_latitude(table_cos, table_sin, real_part, imag_part, inverse):
    if inverse:
        return (
            lat_apply(table_cos, real_part) + lat_apply(table_sin, imag_part),
            lat_apply(table_cos, imag_part) - lat_apply(table_sin, real_part),
        )
    return (
        lat_apply(table_cos, real_part) - lat_apply(table_sin, imag_part),
        lat_apply(table_cos, imag_part) + lat_apply(table_sin, real_part),
    )


def lon_forward(field, table):
    return jnp.einsum("brwc,wk->brkc", field, table, precision=HIGHEST)


def lon_back(spec, table):
    return jnp.einsum("brkc,wk->brwc", spec, table, precision=HIGHEST)


def to_blocks(field, block_size):
    return field.reshape(field.shape[:-1] + (field.shape[-1] // block_size, block_size))


def block_mult(field, weights):
    return jnp.einsum("...nc,nce->...ne", field, weights, precision=HIGHEST)


def block_mult_back(field, weights):
    return jnp.einsum("...ne,nce->...nc", field, weights, precision=HIGHEST)


def block_product(real_part, imag_part, weights):
    return (
        block_mult(real_part, weights[0]) - block_mult(imag_part, weights[1]),
        block_mult(real_part, weights[1]) + block_mult(imag_part, weights[0]),
    )


def block_adjoint(real_part, imag_part, weights):
    return (
        block_mult_back(real_part, weights[0]) + block_mult_back(imag_part, weights[1]),
        block_mult_back(imag_part, weights[0]) - block_mult_back(real_part, weights[1]),
    )


def latitude_tables(length):
    index_row = jnp.arange(length, dtype=jnp.int32)
    phase_angle = (
        2.0 * math.pi / length * (index_row[:, None] * index_row[None, :] % length).astype(jnp.float32)
    )
    scaling = 1.0 / math.sqrt(length)
    return (jnp.cos(phase_angle) * scaling, -jnp.sin(phase_angle) * scaling)


def to_columns(real_part, imag_part, link_type):
    stacked = jnp.stack([real_part, imag_part]).astype(link_type)
    moved = lax.all_to_all(stacked, "space", 3, 2, tiled=True).astype(jnp.float32)
    return (moved[0], moved[1])


def to_rows(real_part, imag_part, link_type):
    stacked = jnp.stack([real_part, imag_part]).astype(link_type)
    moved = lax.all_to_all(stacked, "space", 2, 3, tiled=True).astype(jnp.float32)
    return (moved[0], moved[1])


def enter_spectrum(real_part, imag_part, tables_lat, link_type=jnp.float32):
    table_cos, table_sin = tables_lat
    real_part, imag_part = to_columns(real_part, imag_part, link_type)
    return complex_latitude(table_cos, table_sin, real_part, imag_part, False)


def leave_spectrum(real_part, imag_part, tables_lat, link_type=jnp.float32):
    table_cos, table_sin = tables_lat
    real_part, imag_part = complex_latitude(table_cos, table_sin, real_part, imag_part, True)
    return to_rows(real_part, imag_part, link_type)


def complex_operator(real_block, imag_block):
    return jnp.stack(
        [jnp.stack([real_block, -imag_block]), jnp.stack([imag_block, real_block])]
    )


def lat_stacked(operator, field):
    return jnp.einsum("pqkh,qbhlc->pbklc", operator, field, precision=lax.Precision.HIGH)


def lon_stacked_forward(field, tables):
    return jnp.einsum("brwc,pwk->pbrkc", field, tables, precision=lax.Precision.HIGH)


def lon_stacked_back(spec, tables):
    return jnp.einsum("pbrkc,pwk->brwc", spec, tables, precision=lax.Precision.HIGH)


def block_operator(weights):
    return jnp.moveaxis(complex_operator(weights[0], weights[1]), 2, 0)


def block_stacked(field, operator):
    return jnp.einsum("qbklnc,npqce->pbklne", field, operator, precision=lax.Precision.HIGH)


def block_stacked_adjoint(field, operator):
    return jnp.einsum("pbklne,npqce->qbklnc", field, operator, precision=lax.Precision.HIGH)


def stacked_columns(field, link_type):
    return lax.all_to_all(field.astype(link_type), "space", 3, 2, tiled=True).astype(jnp.float32)


def stacked_rows(field, link_type):
    return lax.all_to_all(field.astype(link_type), "space", 2, 3, tiled=True).astype(jnp.float32)


def token_sums(first_term, second_term):
    pair = jnp.stack([first_term, second_term])
    count = lax.axis_size("feat")
    position = lax.axis_index("feat")
    shifted = jnp.stack(
        [pair]
        + [
            lax.ppermute(pair, "feat", [(i, (i + count - shift) % count) for i in range(count)])
            for shift in range(1, count)
        ]
    )
    ordered = shifted[(jnp.arange(count) + count - position) % count]
    total = ordered[0]
    for source in range(1, count):
        total = total + ordered[source]
    return (total[0], total[1])


def ring_send(block):
    count = lax.axis_size("feat")
    return [block] + [
        lax.ppermute(block, "feat", [(i, (i + shift) % count) for i in range(count)])
        for shift in range(1, count)
    ]


def ring_assemble(parts):
    count = len(parts)
    position = lax.axis_index("feat")
    block = parts[0]
    width = block.shape[-1]
    whole = jnp.zeros(block.shape[:-1] + (width * count,), block.dtype)
    for shift, moved in enumerate(parts):
        source = (position + count - shift) % count
        whole = lax.dynamic_update_slice_in_dim(whole, moved, source * width, axis=block.ndim - 1)
    return whole


def channel_share(term):
    return lax.psum_scatter(
        term.astype(jnp.bfloat16), "feat", scatter_dimension=3, tiled=True
    ).astype(jnp.float32)


def gelu_value(field):
    return 0.5 * field * (1.0 + lax.erf(field * (1.0 / math.sqrt(2.0))))


def gelu_slope(field):
    return 0.5 * (1.0 + lax.erf(field * (1.0 / math.sqrt(2.0)))) + field * jnp.exp(
        -0.5 * field * field
    ) * (1.0 / math.sqrt(2.0 * math.pi))


def per_device(inputs, cotangent, spec_w1, spec_b1, spec_w2, spec_b2, up_weight, down_weight):
    full_width = up_weight.shape[0]
    block_size = spec_w1.shape[2]
    tables_lon = padded_tables(inputs.shape[2], lax.axis_size("space"))
    tables_lat = latitude_tables(inputs.shape[1] * lax.axis_size("space"))
    cos_fwd, sin_fwd, cos_inv, sin_inv = tables_lon
    table_cos, table_sin = tables_lat
    operators = (
        jnp.stack([cos_fwd, sin_fwd]),
        jnp.stack([cos_inv, sin_inv]),
        complex_operator(table_cos, table_sin),
        complex_operator(table_cos, -table_sin),
        block_operator(spec_w1),
        block_operator(spec_w2),
    )
    operators = lax.optimization_barrier(operators)
    lon_fwd_tables, lon_inv_tables, lat_forward_op, lat_inverse_op, first_op, second_op = operators
    values = inputs.astype(jnp.float32)
    cotangent_parts = ring_send(cotangent)
    first_sum, second_sum = token_sums(jnp.sum(values, axis=-1), jnp.sum(values * values, axis=-1))
    mean_one = first_sum[..., None] / full_width
    rstd_one = lax.rsqrt(second_sum[..., None] / full_width - mean_one * mean_one + EPSILON)
    normed = (values - mean_one) * rstd_one
    spec = lat_stacked(
        lat_forward_op, stacked_columns(lon_stacked_forward(normed, lon_fwd_tables), jnp.float32)
    )
    spec_blocks = to_blocks(spec, block_size)
    bias_one = to_blocks(spec_b1, block_size)[:, None, None, None]
    bias_two = to_blocks(spec_b2, block_size)[:, None, None, None]
    first = jax.nn.relu(block_stacked(spec_blocks, first_op) + bias_one)
    second = block_stacked(first, second_op) + bias_two
    shrunk = (second - jnp.clip(second, -SHRINK_LEVEL, SHRINK_LEVEL)).reshape(spec.shape)
    shrunk, cotangent_parts = lax.optimization_barrier((shrunk, cotangent_parts))
    whole_cotangent = ring_assemble(cotangent_parts)
    filtered = lon_stacked_back(
        stacked_rows(lat_stacked(lat_inverse_op, shrunk), jnp.bfloat16), lon_inv_tables
    )
    residual = (filtered + normed + values).astype(jnp.bfloat16)
    residual_vals = residual.astype(jnp.float32)
    whole_residual = lax.all_gather(residual, "feat", axis=3, tiled=True)
    grad_act = jnp.einsum(
        "brwd,hd->brwh", whole_cotangent, down_weight, preferred_element_type=jnp.float32
    )
    whole_residual, grad_act = lax.optimization_barrier((whole_residual, grad_act))
    whole_vals = whole_residual.astype(jnp.float32)
    mean_two = jnp.sum(whole_vals, axis=-1, keepdims=True) / full_width
    square_two = jnp.sum(whole_vals * whole_vals, axis=-1, keepdims=True) / full_width
    rstd_two = lax.rsqrt(square_two - mean_two * mean_two + EPSILON)
    vhat = (whole_vals - mean_two) * rstd_two
    hidden = jnp.einsum(
        "brwd,dh->brwh", vhat.astype(jnp.bfloat16), up_weight, preferred_element_type=jnp.float32
    )
    activated = gelu_value(hidden).astype(jnp.bfloat16)
    mixed_term = jnp.einsum(
        "brwh,hd->brwd", activated, down_weight, preferred_element_type=jnp.float32
    )
    output = (residual_vals + channel_share(mixed_term)).astype(jnp.bfloat16)
    grad_hidden = (grad_act * gelu_slope(hidden)).astype(jnp.bfloat16)
    grad_term = jnp.einsum(
        "brwh,dh->brwd", grad_hidden, up_weight, preferred_element_type=jnp.float32
    )
    total_one, total_two = token_sums(
        jnp.sum(grad_term, axis=-1), jnp.sum(grad_term * vhat, axis=-1)
    )
    grad_vhat = channel_share(grad_term)
    own_hat = (residual_vals - mean_two) * rstd_two
    grad_residual = cotangent.astype(jnp.float32) + rstd_two * (
        grad_vhat
        - total_one[..., None] / full_width
        - own_hat * (total_two[..., None] / full_width)
    )
    grad_spec = lat_stacked(
        lat_forward_op,
        stacked_columns(lon_stacked_forward(grad_residual, lon_inv_tables), jnp.bfloat16),
    )
    grad_second = jnp.where(
        jnp.abs(second) > SHRINK_LEVEL, to_blocks(grad_spec, block_size), 0.0
    )
    grad_first = jnp.where(first > 0.0, block_stacked_adjoint(grad_second, second_op), 0.0)
    grad_spectrum = block_stacked_adjoint(grad_first, first_op).reshape(spec.shape)
    grad_normed = grad_residual + lon_stacked_back(
        stacked_rows(lat_stacked(lat_inverse_op, grad_spectrum), jnp.bfloat16), lon_fwd_tables
    )
    norm_one, norm_two = token_sums(
        jnp.sum(grad_normed, axis=-1), jnp.sum(grad_normed * normed, axis=-1)
    )
    grad_input = grad_residual + rstd_one * (
        grad_normed - norm_one[..., None] / full_width - normed * (norm_two[..., None] / full_width)
    )
    return (output, grad_input.astype(jnp.bfloat16))


def solution(mesh):
    return jax.shard_map(
        per_device,
        mesh=mesh,
        in_specs=(
            P(None, "space", None, "feat"),
            P(None, "space", None, "feat"),
            P(None, "feat", None, None),
            P(None, "feat"),
            P(None, "feat", None, None),
            P(None, "feat"),
            P(None, "feat"),
            P("feat", None),
        ),
        out_specs=(P(None, "space", None, "feat"), P(None, "space", None, "feat")),
        check_vma=False,
    )
```

```python
import math

import jax
import jax.numpy as jnp
from jax import lax
from jax.sharding import PartitionSpec as P

EPSILON = 1e-05
SHRINK_LEVEL = 0.1
HIGHEST = lax.Precision.HIGHEST


def longitude_tables(width_lon):
    mode_count = width_lon // 2 + 1
    cell_index = jnp.arange(width_lon, dtype=jnp.int32)[:, None]
    wave_number = jnp.arange(mode_count, dtype=jnp.int32)[None, :]
    phase_angle = (
        2.0 * math.pi / width_lon * (cell_index * wave_number % width_lon).astype(jnp.float32)
    )
    scaling = 1.0 / math.sqrt(width_lon)
    cos_fwd = jnp.cos(phase_angle) * scaling
    sin_fwd = -jnp.sin(phase_angle) * scaling
    doubled = jnp.where((wave_number == 0) | (wave_number * 2 == width_lon), 1.0, 2.0).astype(
        jnp.float32
    )
    return (cos_fwd, sin_fwd, cos_fwd * doubled, sin_fwd * doubled)


def padded_tables(width_lon, multiple):
    tables = longitude_tables(width_lon)
    modes = tables[0].shape[1]
    extra = -modes % multiple
    return tuple(jnp.pad(table, ((0, 0), (0, extra))) for table in tables)


def lat_apply(table, field):
    return jnp.einsum("gh,bhkc->bgkc", table, field, precision=HIGHEST)


def complex_latitude(table_cos, table_sin, real_part, imag_part, inverse):
    if inverse:
        return (
            lat_apply(table_cos, real_part) + lat_apply(table_sin, imag_part),
            lat_apply(table_cos, imag_part) - lat_apply(table_sin, real_part),
        )
    return (
        lat_apply(table_cos, real_part) - lat_apply(table_sin, imag_part),
        lat_apply(table_cos, imag_part) + lat_apply(table_sin, real_part),
    )


def lon_forward(field, table):
    return jnp.einsum("brwc,wk->brkc", field, table, precision=HIGHEST)


def lon_back(spec, table):
    return jnp.einsum("brkc,wk->brwc", spec, table, precision=HIGHEST)


def to_blocks(field, block_size):
    return field.reshape(field.shape[:-1] + (field.shape[-1] // block_size, block_size))


def block_mult(field, weights):
    return jnp.einsum("...nc,nce->...ne", field, weights, precision=HIGHEST)


def block_mult_back(field, weights):
    return jnp.einsum("...ne,nce->...nc", field, weights, precision=HIGHEST)


def block_product(real_part, imag_part, weights):
    return (
        block_mult(real_part, weights[0]) - block_mult(imag_part, weights[1]),
        block_mult(real_part, weights[1]) + block_mult(imag_part, weights[0]),
    )


def block_adjoint(real_part, imag_part, weights):
    return (
        block_mult_back(real_part, weights[0]) + block_mult_back(imag_part, weights[1]),
        block_mult_back(imag_part, weights[0]) - block_mult_back(real_part, weights[1]),
    )


def latitude_tables(length):
    index_row = jnp.arange(length, dtype=jnp.int32)
    phase_angle = (
        2.0 * math.pi / length * (index_row[:, None] * index_row[None, :] % length).astype(jnp.float32)
    )
    scaling = 1.0 / math.sqrt(length)
    return (jnp.cos(phase_angle) * scaling, -jnp.sin(phase_angle) * scaling)


def to_columns(real_part, imag_part, link_type):
    stacked = jnp.stack([real_part, imag_part]).astype(link_type)
    moved = lax.all_to_all(stacked, "space", 3, 2, tiled=True).astype(jnp.float32)
    return (moved[0], moved[1])


def to_rows(real_part, imag_part, link_type):
    stacked = jnp.stack([real_part, imag_part]).astype(link_type)
    moved = lax.all_to_all(stacked, "space", 2, 3, tiled=True).astype(jnp.float32)
    return (moved[0], moved[1])


def enter_spectrum(real_part, imag_part, tables_lat, link_type=jnp.float32):
    table_cos, table_sin = tables_lat
    real_part, imag_part = to_columns(real_part, imag_part, link_type)
    return complex_latitude(table_cos, table_sin, real_part, imag_part, False)


def leave_spectrum(real_part, imag_part, tables_lat, link_type=jnp.float32):
    table_cos, table_sin = tables_lat
    real_part, imag_part = complex_latitude(table_cos, table_sin, real_part, imag_part, True)
    return to_rows(real_part, imag_part, link_type)


def complex_operator(real_block, imag_block):
    return jnp.stack(
        [jnp.stack([real_block, -imag_block]), jnp.stack([imag_block, real_block])]
    )


def lat_stacked(operator, field, precision=lax.Precision.HIGH):
    return jnp.einsum("pqkh,qbhlc->pbklc", operator, field, precision=precision)


def lon_stacked_forward(field, tables, precision=lax.Precision.HIGH):
    return jnp.einsum("brwc,pwk->pbrkc", field, tables, precision=precision)


def lon_stacked_back(spec, tables, precision=lax.Precision.HIGH):
    return jnp.einsum("pbrkc,pwk->brwc", spec, tables, precision=precision)


def block_operator(weights):
    return jnp.moveaxis(complex_operator(weights[0], weights[1]), 2, 0)


def block_stacked(field, operator):
    return jnp.einsum("qbklnc,npqce->pbklne", field, operator, precision=lax.Precision.HIGH)


def block_stacked_adjoint(field, operator):
    return jnp.einsum("pbklne,npqce->qbklnc", field, operator, precision=lax.Precision.DEFAULT)


def stacked_columns(field, link_type):
    return lax.all_to_all(field.astype(link_type), "space", 3, 2, tiled=True).astype(jnp.float32)


def stacked_rows(field, link_type):
    return lax.all_to_all(field.astype(link_type), "space", 2, 3, tiled=True).astype(jnp.float32)


def token_sums(first_term, second_term):
    pair = jnp.stack([first_term, second_term])
    count = lax.axis_size("feat")
    position = lax.axis_index("feat")
    shifted = jnp.stack(
        [pair]
        + [
            lax.ppermute(pair, "feat", [(i, (i + count - shift) % count) for i in range(count)])
            for shift in range(1, count)
        ]
    )
    ordered = shifted[(jnp.arange(count) + count - position) % count]
    total = ordered[0]
    for source in range(1, count):
        total = total + ordered[source]
    return (total[0], total[1])


def ring_send(block):
    count = lax.axis_size("feat")
    return [block] + [
        lax.ppermute(block, "feat", [(i, (i + shift) % count) for i in range(count)])
        for shift in range(1, count)
    ]


def ring_assemble(parts):
    count = len(parts)
    position = lax.axis_index("feat")
    block = parts[0]
    width = block.shape[-1]
    whole = jnp.zeros(block.shape[:-1] + (width * count,), block.dtype)
    for shift, moved in enumerate(parts):
        source = (position + count - shift) % count
        whole = lax.dynamic_update_slice_in_dim(whole, moved, source * width, axis=block.ndim - 1)
    return whole


def channel_share(term):
    return lax.psum_scatter(
        term.astype(jnp.bfloat16), "feat", scatter_dimension=3, tiled=True
    ).astype(jnp.float32)


def gelu_value(field):
    return 0.5 * field * (1.0 + lax.erf(field * (1.0 / math.sqrt(2.0))))


def gelu_slope(field):
    return 0.5 * (1.0 + lax.erf(field * (1.0 / math.sqrt(2.0)))) + field * jnp.exp(
        -0.5 * field * field
    ) * (1.0 / math.sqrt(2.0 * math.pi))


def per_device(inputs, cotangent, spec_w1, spec_b1, spec_w2, spec_b2, up_weight, down_weight):
    full_width = up_weight.shape[0]
    block_size = spec_w1.shape[2]
    tables_lon = padded_tables(inputs.shape[2], lax.axis_size("space"))
    tables_lat = latitude_tables(inputs.shape[1] * lax.axis_size("space"))
    cos_fwd, sin_fwd, cos_inv, sin_inv = tables_lon
    table_cos, table_sin = tables_lat
    operators = (
        jnp.stack([cos_fwd, sin_fwd]),
        jnp.stack([cos_inv, sin_inv]),
        complex_operator(table_cos, table_sin),
        complex_operator(table_cos, -table_sin),
        block_operator(spec_w1),
        block_operator(spec_w2),
    )
    operators = lax.optimization_barrier(operators)
    lon_fwd_tables, lon_inv_tables, lat_forward_op, lat_inverse_op, first_op, second_op = operators
    values = inputs.astype(jnp.float32)
    cotangent_parts = ring_send(cotangent)
    first_sum, second_sum = token_sums(jnp.sum(values, axis=-1), jnp.sum(values * values, axis=-1))
    mean_one = first_sum[..., None] / full_width
    rstd_one = lax.rsqrt(second_sum[..., None] / full_width - mean_one * mean_one + EPSILON)
    normed = (values - mean_one) * rstd_one
    spec = lat_stacked(
        lat_forward_op, stacked_columns(lon_stacked_forward(normed, lon_fwd_tables), jnp.float32)
    )
    spec_blocks = to_blocks(spec, block_size)
    bias_one = to_blocks(spec_b1, block_size)[:, None, None, None]
    bias_two = to_blocks(spec_b2, block_size)[:, None, None, None]
    first = jax.nn.relu(block_stacked(spec_blocks, first_op) + bias_one)
    second = block_stacked(first, second_op) + bias_two
    shrunk = (second - jnp.clip(second, -SHRINK_LEVEL, SHRINK_LEVEL)).reshape(spec.shape)
    shrunk, cotangent_parts = lax.optimization_barrier((shrunk, cotangent_parts))
    whole_cotangent = ring_assemble(cotangent_parts)
    filtered = lon_stacked_back(
        stacked_rows(lat_stacked(lat_inverse_op, shrunk), jnp.bfloat16), lon_inv_tables
    )
    residual = (filtered + normed + values).astype(jnp.bfloat16)
    residual_vals = residual.astype(jnp.float32)
    whole_residual = lax.all_gather(residual, "feat", axis=3, tiled=True)
    grad_act = jnp.einsum(
        "brwd,hd->brwh", whole_cotangent, down_weight, preferred_element_type=jnp.float32
    )
    whole_residual, grad_act = lax.optimization_barrier((whole_residual, grad_act))
    whole_vals = whole_residual.astype(jnp.float32)
    mean_two = jnp.sum(whole_vals, axis=-1, keepdims=True) / full_width
    square_two = jnp.sum(whole_vals * whole_vals, axis=-1, keepdims=True) / full_width
    rstd_two = lax.rsqrt(square_two - mean_two * mean_two + EPSILON)
    vhat = (whole_vals - mean_two) * rstd_two
    hidden = jnp.einsum(
        "brwd,dh->brwh", vhat.astype(jnp.bfloat16), up_weight, preferred_element_type=jnp.float32
    )
    activated = gelu_value(hidden).astype(jnp.bfloat16)
    mixed_term = jnp.einsum(
        "brwh,hd->brwd", activated, down_weight, preferred_element_type=jnp.float32
    )
    output = (residual_vals + channel_share(mixed_term)).astype(jnp.bfloat16)
    grad_hidden = (grad_act * gelu_slope(hidden)).astype(jnp.bfloat16)
    grad_term = jnp.einsum(
        "brwh,dh->brwd", grad_hidden, up_weight, preferred_element_type=jnp.float32
    )
    total_one, total_two = token_sums(
        jnp.sum(grad_term, axis=-1), jnp.sum(grad_term * vhat, axis=-1)
    )
    grad_vhat = channel_share(grad_term)
    own_hat = (residual_vals - mean_two) * rstd_two
    grad_residual = cotangent.astype(jnp.float32) + rstd_two * (
        grad_vhat
        - total_one[..., None] / full_width
        - own_hat * (total_two[..., None] / full_width)
    )
    grad_spec = lat_stacked(
        lat_forward_op,
        stacked_columns(
            lon_stacked_forward(grad_residual, lon_inv_tables, lax.Precision.DEFAULT), jnp.bfloat16
        ),
        lax.Precision.DEFAULT,
    )
    grad_second = jnp.where(
        jnp.abs(second) > SHRINK_LEVEL, to_blocks(grad_spec, block_size), 0.0
    )
    grad_first = jnp.where(first > 0.0, block_stacked_adjoint(grad_second, second_op), 0.0)
    grad_spectrum = block_stacked_adjoint(grad_first, first_op).reshape(spec.shape)
    grad_normed = grad_residual + lon_stacked_back(
        stacked_rows(
            lat_stacked(lat_inverse_op, grad_spectrum, lax.Precision.DEFAULT), jnp.bfloat16
        ),
        lon_fwd_tables,
        lax.Precision.DEFAULT,
    )
    norm_one, norm_two = token_sums(
        jnp.sum(grad_normed, axis=-1), jnp.sum(grad_normed * normed, axis=-1)
    )
    grad_input = grad_residual + rstd_one * (
        grad_normed - norm_one[..., None] / full_width - normed * (norm_two[..., None] / full_width)
    )
    return (output, grad_input.astype(jnp.bfloat16))


def solution(mesh):
    return jax.shard_map(
        per_device,
        mesh=mesh,
        in_specs=(
            P(None, "space", None, "feat"),
            P(None, "space", None, "feat"),
            P(None, "feat", None, None),
            P(None, "feat"),
            P(None, "feat", None, None),
            P(None, "feat"),
            P(None, "feat"),
            P("feat", None),
        ),
        out_specs=(P(None, "space", None, "feat"), P(None, "space", None, "feat")),
        check_vma=False,
    )
```

```python
import math

import jax
import jax.numpy as jnp
from jax import lax
from jax.sharding import PartitionSpec as P

EPSILON = 1e-05
SHRINK_LEVEL = 0.1
HIGHEST = lax.Precision.HIGHEST


def longitude_tables(width_lon):
    mode_count = width_lon // 2 + 1
    cell_index = jnp.arange(width_lon, dtype=jnp.int32)[:, None]
    wave_number = jnp.arange(mode_count, dtype=jnp.int32)[None, :]
    phase_angle = (
        2.0 * math.pi / width_lon * (cell_index * wave_number % width_lon).astype(jnp.float32)
    )
    scaling = 1.0 / math.sqrt(width_lon)
    cos_fwd = jnp.cos(phase_angle) * scaling
    sin_fwd = -jnp.sin(phase_angle) * scaling
    doubled = jnp.where((wave_number == 0) | (wave_number * 2 == width_lon), 1.0, 2.0).astype(
        jnp.float32
    )
    return (cos_fwd, sin_fwd, cos_fwd * doubled, sin_fwd * doubled)


def padded_tables(width_lon, multiple):
    tables = longitude_tables(width_lon)
    modes = tables[0].shape[1]
    extra = -modes % multiple
    return tuple(jnp.pad(table, ((0, 0), (0, extra))) for table in tables)


def lat_apply(table, field):
    return jnp.einsum("gh,bhkc->bgkc", table, field, precision=HIGHEST)


def complex_latitude(table_cos, table_sin, real_part, imag_part, inverse):
    if inverse:
        return (
            lat_apply(table_cos, real_part) + lat_apply(table_sin, imag_part),
            lat_apply(table_cos, imag_part) - lat_apply(table_sin, real_part),
        )
    return (
        lat_apply(table_cos, real_part) - lat_apply(table_sin, imag_part),
        lat_apply(table_cos, imag_part) + lat_apply(table_sin, real_part),
    )


def lon_forward(field, table):
    return jnp.einsum("brwc,wk->brkc", field, table, precision=HIGHEST)


def lon_back(spec, table):
    return jnp.einsum("brkc,wk->brwc", spec, table, precision=HIGHEST)


def to_blocks(field, block_size):
    return field.reshape(field.shape[:-1] + (field.shape[-1] // block_size, block_size))


def block_mult(field, weights):
    return jnp.einsum("...nc,nce->...ne", field, weights, precision=HIGHEST)


def block_mult_back(field, weights):
    return jnp.einsum("...ne,nce->...nc", field, weights, precision=HIGHEST)


def block_product(real_part, imag_part, weights):
    return (
        block_mult(real_part, weights[0]) - block_mult(imag_part, weights[1]),
        block_mult(real_part, weights[1]) + block_mult(imag_part, weights[0]),
    )


def block_adjoint(real_part, imag_part, weights):
    return (
        block_mult_back(real_part, weights[0]) + block_mult_back(imag_part, weights[1]),
        block_mult_back(imag_part, weights[0]) - block_mult_back(real_part, weights[1]),
    )


def latitude_tables(length):
    index_row = jnp.arange(length, dtype=jnp.int32)
    phase_angle = (
        2.0 * math.pi / length * (index_row[:, None] * index_row[None, :] % length).astype(jnp.float32)
    )
    scaling = 1.0 / math.sqrt(length)
    return (jnp.cos(phase_angle) * scaling, -jnp.sin(phase_angle) * scaling)


def to_columns(real_part, imag_part, link_type):
    stacked = jnp.stack([real_part, imag_part]).astype(link_type)
    moved = lax.all_to_all(stacked, "space", 3, 2, tiled=True).astype(jnp.float32)
    return (moved[0], moved[1])


def to_rows(real_part, imag_part, link_type):
    stacked = jnp.stack([real_part, imag_part]).astype(link_type)
    moved = lax.all_to_all(stacked, "space", 2, 3, tiled=True).astype(jnp.float32)
    return (moved[0], moved[1])


def enter_spectrum(real_part, imag_part, tables_lat, link_type=jnp.float32):
    table_cos, table_sin = tables_lat
    real_part, imag_part = to_columns(real_part, imag_part, link_type)
    return complex_latitude(table_cos, table_sin, real_part, imag_part, False)


def leave_spectrum(real_part, imag_part, tables_lat, link_type=jnp.float32):
    table_cos, table_sin = tables_lat
    real_part, imag_part = complex_latitude(table_cos, table_sin, real_part, imag_part, True)
    return to_rows(real_part, imag_part, link_type)


def complex_operator(real_block, imag_block):
    return jnp.stack(
        [jnp.stack([real_block, -imag_block]), jnp.stack([imag_block, real_block])]
    )


def lat_stacked(operator, field, precision=lax.Precision.HIGH):
    return jnp.einsum("pqkh,qbhlc->pbklc", operator, field, precision=precision)


def lon_stacked_forward(field, tables, precision=lax.Precision.HIGH):
    return jnp.einsum("brwc,pwk->pbrkc", field, tables, precision=precision)


def lon_stacked_back(spec, tables, precision=lax.Precision.HIGH):
    return jnp.einsum("pbrkc,pwk->brwc", spec, tables, precision=precision)


def block_operator(weights):
    return jnp.moveaxis(complex_operator(weights[0], weights[1]), 2, 0)


def block_stacked(field, operator):
    return jnp.einsum("qbklnc,npqce->pbklne", field, operator, precision=lax.Precision.HIGH)


def block_stacked_adjoint(field, operator):
    return jnp.einsum("pbklne,npqce->qbklnc", field, operator, precision=lax.Precision.DEFAULT)


def stacked_columns(field, link_type):
    return lax.all_to_all(field.astype(link_type), "space", 3, 2, tiled=True).astype(jnp.float32)


def stacked_rows(field, link_type):
    return lax.all_to_all(field.astype(link_type), "space", 2, 3, tiled=True).astype(jnp.float32)


def token_sums(first_term, second_term):
    pair = jnp.stack([first_term, second_term])
    count = lax.axis_size("feat")
    position = lax.axis_index("feat")
    shifted = jnp.stack(
        [pair]
        + [
            lax.ppermute(pair, "feat", [(i, (i + count - shift) % count) for i in range(count)])
            for shift in range(1, count)
        ]
    )
    ordered = shifted[(jnp.arange(count) + count - position) % count]
    total = ordered[0]
    for source in range(1, count):
        total = total + ordered[source]
    return (total[0], total[1])


def ring_send(block):
    count = lax.axis_size("feat")
    return [block] + [
        lax.ppermute(block, "feat", [(i, (i + shift) % count) for i in range(count)])
        for shift in range(1, count)
    ]


def ring_assemble(parts):
    count = len(parts)
    position = lax.axis_index("feat")
    block = parts[0]
    width = block.shape[-1]
    whole = jnp.zeros(block.shape[:-1] + (width * count,), block.dtype)
    for shift, moved in enumerate(parts):
        source = (position + count - shift) % count
        whole = lax.dynamic_update_slice_in_dim(whole, moved, source * width, axis=block.ndim - 1)
    return whole


def channel_share(term):
    return lax.psum_scatter(
        term.astype(jnp.bfloat16), "feat", scatter_dimension=3, tiled=True
    ).astype(jnp.float32)


def gelu_value(field):
    return 0.5 * field * (1.0 + lax.erf(field * (1.0 / math.sqrt(2.0))))


def gelu_slope(field):
    return 0.5 * (1.0 + lax.erf(field * (1.0 / math.sqrt(2.0)))) + field * jnp.exp(
        -0.5 * field * field
    ) * (1.0 / math.sqrt(2.0 * math.pi))


def per_device(inputs, cotangent, spec_w1, spec_b1, spec_w2, spec_b2, up_weight, down_weight):
    full_width = up_weight.shape[0]
    block_size = spec_w1.shape[2]
    tables_lon = padded_tables(inputs.shape[2], lax.axis_size("space"))
    tables_lat = latitude_tables(inputs.shape[1] * lax.axis_size("space"))
    cos_fwd, sin_fwd, cos_inv, sin_inv = tables_lon
    table_cos, table_sin = tables_lat
    operators = (
        jnp.stack([cos_fwd, sin_fwd]),
        jnp.stack([cos_inv, sin_inv]),
        complex_operator(table_cos, table_sin),
        complex_operator(table_cos, -table_sin),
        block_operator(spec_w1),
        block_operator(spec_w2),
    )
    operators = lax.optimization_barrier(operators)
    lon_fwd_tables, lon_inv_tables, lat_forward_op, lat_inverse_op, first_op, second_op = operators
    values = inputs.astype(jnp.float32)
    cotangent_parts = ring_send(cotangent)
    first_sum, second_sum = token_sums(jnp.sum(values, axis=-1), jnp.sum(values * values, axis=-1))
    mean_one = first_sum[..., None] / full_width
    rstd_one = lax.rsqrt(second_sum[..., None] / full_width - mean_one * mean_one + EPSILON)
    normed = (values - mean_one) * rstd_one
    spec = lat_stacked(
        lat_forward_op, stacked_columns(lon_stacked_forward(normed, lon_fwd_tables), jnp.float32)
    )
    spec_blocks = to_blocks(spec, block_size)
    bias_one = to_blocks(spec_b1, block_size)[:, None, None, None]
    bias_two = to_blocks(spec_b2, block_size)[:, None, None, None]
    first = jax.nn.relu(block_stacked(spec_blocks, first_op) + bias_one)
    second = block_stacked(first, second_op) + bias_two
    shrunk = (second - jnp.clip(second, -SHRINK_LEVEL, SHRINK_LEVEL)).reshape(spec.shape)
    shrunk, cotangent_parts = lax.optimization_barrier((shrunk, cotangent_parts))
    whole_cotangent = ring_assemble(cotangent_parts)
    filtered = lon_stacked_back(
        stacked_rows(lat_stacked(lat_inverse_op, shrunk, lax.Precision.DEFAULT), jnp.bfloat16),
        lon_inv_tables,
        lax.Precision.DEFAULT,
    )
    residual = (filtered + normed + values).astype(jnp.bfloat16)
    residual_vals = residual.astype(jnp.float32)
    whole_residual = lax.all_gather(residual, "feat", axis=3, tiled=True)
    grad_act = jnp.einsum(
        "brwd,hd->brwh", whole_cotangent, down_weight, preferred_element_type=jnp.float32
    )
    whole_residual, grad_act = lax.optimization_barrier((whole_residual, grad_act))
    whole_vals = whole_residual.astype(jnp.float32)
    mean_two = jnp.sum(whole_vals, axis=-1, keepdims=True) / full_width
    square_two = jnp.sum(whole_vals * whole_vals, axis=-1, keepdims=True) / full_width
    rstd_two = lax.rsqrt(square_two - mean_two * mean_two + EPSILON)
    vhat = (whole_vals - mean_two) * rstd_two
    hidden = jnp.einsum(
        "brwd,dh->brwh", vhat.astype(jnp.bfloat16), up_weight, preferred_element_type=jnp.float32
    )
    activated = gelu_value(hidden).astype(jnp.bfloat16)
    mixed_term = jnp.einsum(
        "brwh,hd->brwd", activated, down_weight, preferred_element_type=jnp.float32
    )
    output = (residual_vals + channel_share(mixed_term)).astype(jnp.bfloat16)
    grad_hidden = (grad_act * gelu_slope(hidden)).astype(jnp.bfloat16)
    grad_term = jnp.einsum(
        "brwh,dh->brwd", grad_hidden, up_weight, preferred_element_type=jnp.float32
    )
    total_one, total_two = token_sums(
        jnp.sum(grad_term, axis=-1), jnp.sum(grad_term * vhat, axis=-1)
    )
    grad_vhat = channel_share(grad_term)
    own_hat = (residual_vals - mean_two) * rstd_two
    grad_residual = cotangent.astype(jnp.float32) + rstd_two * (
        grad_vhat
        - total_one[..., None] / full_width
        - own_hat * (total_two[..., None] / full_width)
    )
    grad_spec = lat_stacked(
        lat_forward_op,
        stacked_columns(
            lon_stacked_forward(grad_residual, lon_inv_tables, lax.Precision.DEFAULT), jnp.bfloat16
        ),
        lax.Precision.DEFAULT,
    )
    grad_second = jnp.where(
        jnp.abs(second) > SHRINK_LEVEL, to_blocks(grad_spec, block_size), 0.0
    )
    grad_first = jnp.where(first > 0.0, block_stacked_adjoint(grad_second, second_op), 0.0)
    grad_spectrum = block_stacked_adjoint(grad_first, first_op).reshape(spec.shape)
    grad_normed = grad_residual + lon_stacked_back(
        stacked_rows(
            lat_stacked(lat_inverse_op, grad_spectrum, lax.Precision.DEFAULT), jnp.bfloat16
        ),
        lon_fwd_tables,
        lax.Precision.DEFAULT,
    )
    norm_one, norm_two = token_sums(
        jnp.sum(grad_normed, axis=-1), jnp.sum(grad_normed * normed, axis=-1)
    )
    grad_input = grad_residual + rstd_one * (
        grad_normed - norm_one[..., None] / full_width - normed * (norm_two[..., None] / full_width)
    )
    return (output, grad_input.astype(jnp.bfloat16))


def solution(mesh):
    return jax.shard_map(
        per_device,
        mesh=mesh,
        in_specs=(
            P(None, "space", None, "feat"),
            P(None, "space", None, "feat"),
            P(None, "feat", None, None),
            P(None, "feat"),
            P(None, "feat", None, None),
            P(None, "feat"),
            P(None, "feat"),
            P("feat", None),
        ),
        out_specs=(P(None, "space", None, "feat"), P(None, "space", None, "feat")),
        check_vma=False,
    )
```

```python
import math

import jax
import jax.numpy as jnp
from jax import lax
from jax.sharding import PartitionSpec as P

EPSILON = 1e-05
SHRINK_LEVEL = 0.1
HIGHEST = lax.Precision.HIGHEST


def longitude_tables(width_lon):
    mode_count = width_lon // 2 + 1
    cell_index = jnp.arange(width_lon, dtype=jnp.int32)[:, None]
    wave_number = jnp.arange(mode_count, dtype=jnp.int32)[None, :]
    phase_angle = (
        2.0 * math.pi / width_lon * (cell_index * wave_number % width_lon).astype(jnp.float32)
    )
    scaling = 1.0 / math.sqrt(width_lon)
    cos_fwd = jnp.cos(phase_angle) * scaling
    sin_fwd = -jnp.sin(phase_angle) * scaling
    doubled = jnp.where((wave_number == 0) | (wave_number * 2 == width_lon), 1.0, 2.0).astype(
        jnp.float32
    )
    return (cos_fwd, sin_fwd, cos_fwd * doubled, sin_fwd * doubled)


def padded_tables(width_lon, multiple):
    tables = longitude_tables(width_lon)
    modes = tables[0].shape[1]
    extra = -modes % multiple
    return tuple(jnp.pad(table, ((0, 0), (0, extra))) for table in tables)


def lat_apply(table, field):
    return jnp.einsum("gh,bhkc->bgkc", table, field, precision=HIGHEST)


def complex_latitude(table_cos, table_sin, real_part, imag_part, inverse):
    if inverse:
        return (
            lat_apply(table_cos, real_part) + lat_apply(table_sin, imag_part),
            lat_apply(table_cos, imag_part) - lat_apply(table_sin, real_part),
        )
    return (
        lat_apply(table_cos, real_part) - lat_apply(table_sin, imag_part),
        lat_apply(table_cos, imag_part) + lat_apply(table_sin, real_part),
    )


def lon_forward(field, table):
    return jnp.einsum("brwc,wk->brkc", field, table, precision=HIGHEST)


def lon_back(spec, table):
    return jnp.einsum("brkc,wk->brwc", spec, table, precision=HIGHEST)


def to_blocks(field, block_size):
    return field.reshape(field.shape[:-1] + (field.shape[-1] // block_size, block_size))


def block_mult(field, weights):
    return jnp.einsum("...nc,nce->...ne", field, weights, precision=HIGHEST)


def block_mult_back(field, weights):
    return jnp.einsum("...ne,nce->...nc", field, weights, precision=HIGHEST)


def block_product(real_part, imag_part, weights):
    return (
        block_mult(real_part, weights[0]) - block_mult(imag_part, weights[1]),
        block_mult(real_part, weights[1]) + block_mult(imag_part, weights[0]),
    )


def block_adjoint(real_part, imag_part, weights):
    return (
        block_mult_back(real_part, weights[0]) + block_mult_back(imag_part, weights[1]),
        block_mult_back(imag_part, weights[0]) - block_mult_back(real_part, weights[1]),
    )


def latitude_tables(length):
    index_row = jnp.arange(length, dtype=jnp.int32)
    phase_angle = (
        2.0 * math.pi / length * (index_row[:, None] * index_row[None, :] % length).astype(jnp.float32)
    )
    scaling = 1.0 / math.sqrt(length)
    return (jnp.cos(phase_angle) * scaling, -jnp.sin(phase_angle) * scaling)


def to_columns(real_part, imag_part, link_type):
    stacked = jnp.stack([real_part, imag_part]).astype(link_type)
    moved = lax.all_to_all(stacked, "space", 3, 2, tiled=True).astype(jnp.float32)
    return (moved[0], moved[1])


def to_rows(real_part, imag_part, link_type):
    stacked = jnp.stack([real_part, imag_part]).astype(link_type)
    moved = lax.all_to_all(stacked, "space", 2, 3, tiled=True).astype(jnp.float32)
    return (moved[0], moved[1])


def enter_spectrum(real_part, imag_part, tables_lat, link_type=jnp.float32):
    table_cos, table_sin = tables_lat
    real_part, imag_part = to_columns(real_part, imag_part, link_type)
    return complex_latitude(table_cos, table_sin, real_part, imag_part, False)


def leave_spectrum(real_part, imag_part, tables_lat, link_type=jnp.float32):
    table_cos, table_sin = tables_lat
    real_part, imag_part = complex_latitude(table_cos, table_sin, real_part, imag_part, True)
    return to_rows(real_part, imag_part, link_type)


def complex_operator(real_block, imag_block):
    return jnp.stack(
        [jnp.stack([real_block, -imag_block]), jnp.stack([imag_block, real_block])]
    )


def lat_stacked(operator, field, precision=lax.Precision.HIGH):
    return jnp.einsum("pqkh,qbhlc->pbklc", operator, field, precision=precision)


def lon_stacked_forward(field, tables, precision=lax.Precision.HIGH):
    return jnp.einsum("brwc,pwk->pbrkc", field, tables, precision=precision)


def lon_stacked_back(spec, tables, precision=lax.Precision.HIGH):
    return jnp.einsum("pbrkc,pwk->brwc", spec, tables, precision=precision)


def block_operator(weights):
    return jnp.moveaxis(complex_operator(weights[0], weights[1]), 2, 0)


def block_stacked(field, operator):
    return jnp.einsum("qbklnc,npqce->pbklne", field, operator, precision=lax.Precision.HIGH)


def block_stacked_adjoint(field, operator):
    return jnp.einsum("pbklne,npqce->qbklnc", field, operator, precision=lax.Precision.DEFAULT)


def stacked_columns(field, link_type):
    return lax.all_to_all(field.astype(link_type), "space", 3, 2, tiled=True).astype(jnp.float32)


def stacked_rows(field, link_type):
    return lax.all_to_all(field.astype(link_type), "space", 2, 3, tiled=True).astype(jnp.float32)


def token_sums(first_term, second_term):
    pair = jnp.stack([first_term, second_term])
    count = lax.axis_size("feat")
    position = lax.axis_index("feat")
    shifted = jnp.stack(
        [pair]
        + [
            lax.ppermute(pair, "feat", [(i, (i + count - shift) % count) for i in range(count)])
            for shift in range(1, count)
        ]
    )
    ordered = shifted[(jnp.arange(count) + count - position) % count]
    total = ordered[0]
    for source in range(1, count):
        total = total + ordered[source]
    return (total[0], total[1])


def ring_send(block):
    count = lax.axis_size("feat")
    return [block] + [
        lax.ppermute(block, "feat", [(i, (i + shift) % count) for i in range(count)])
        for shift in range(1, count)
    ]


def ring_assemble(parts):
    count = len(parts)
    position = lax.axis_index("feat")
    block = parts[0]
    width = block.shape[-1]
    whole = jnp.zeros(block.shape[:-1] + (width * count,), block.dtype)
    for shift, moved in enumerate(parts):
        source = (position + count - shift) % count
        whole = lax.dynamic_update_slice_in_dim(whole, moved, source * width, axis=block.ndim - 1)
    return whole


def channel_share(term):
    return lax.psum_scatter(
        term.astype(jnp.bfloat16), "feat", scatter_dimension=3, tiled=True
    ).astype(jnp.float32)


def gelu_value(field):
    return 0.5 * field * (1.0 + lax.erf(field * (1.0 / math.sqrt(2.0))))


def gelu_slope(field):
    return 0.5 * (1.0 + lax.erf(field * (1.0 / math.sqrt(2.0)))) + field * jnp.exp(
        -0.5 * field * field
    ) * (1.0 / math.sqrt(2.0 * math.pi))


def per_device(inputs, cotangent, spec_w1, spec_b1, spec_w2, spec_b2, up_weight, down_weight):
    full_width = up_weight.shape[0]
    block_size = spec_w1.shape[2]
    tables_lon = padded_tables(inputs.shape[2], lax.axis_size("space"))
    tables_lat = latitude_tables(inputs.shape[1] * lax.axis_size("space"))
    cos_fwd, sin_fwd, cos_inv, sin_inv = tables_lon
    table_cos, table_sin = tables_lat
    operators = (
        jnp.stack([cos_fwd, sin_fwd]),
        jnp.stack([cos_inv, sin_inv]),
        complex_operator(table_cos, table_sin),
        complex_operator(table_cos, -table_sin),
        block_operator(spec_w1),
        block_operator(spec_w2),
    )
    operators = lax.optimization_barrier(operators)
    lon_fwd_tables, lon_inv_tables, lat_forward_op, lat_inverse_op, first_op, second_op = operators
    values = inputs.astype(jnp.float32)
    cotangent_parts = lax.all_gather(cotangent, "feat", axis=3, tiled=True)
    first_sum, second_sum = token_sums(jnp.sum(values, axis=-1), jnp.sum(values * values, axis=-1))
    mean_one = first_sum[..., None] / full_width
    rstd_one = lax.rsqrt(second_sum[..., None] / full_width - mean_one * mean_one + EPSILON)
    normed = (values - mean_one) * rstd_one
    spec = lat_stacked(
        lat_forward_op, stacked_columns(lon_stacked_forward(normed, lon_fwd_tables), jnp.float32)
    )
    spec_blocks = to_blocks(spec, block_size)
    bias_one = to_blocks(spec_b1, block_size)[:, None, None, None]
    bias_two = to_blocks(spec_b2, block_size)[:, None, None, None]
    first = jax.nn.relu(block_stacked(spec_blocks, first_op) + bias_one)
    second = block_stacked(first, second_op) + bias_two
    shrunk = (second - jnp.clip(second, -SHRINK_LEVEL, SHRINK_LEVEL)).reshape(spec.shape)
    shrunk, cotangent_parts = lax.optimization_barrier((shrunk, cotangent_parts))
    whole_cotangent = cotangent_parts
    filtered = lon_stacked_back(
        stacked_rows(lat_stacked(lat_inverse_op, shrunk, lax.Precision.DEFAULT), jnp.bfloat16),
        lon_inv_tables,
        lax.Precision.DEFAULT,
    )
    residual = (filtered + normed + values).astype(jnp.bfloat16)
    residual_vals = residual.astype(jnp.float32)
    whole_residual = lax.all_gather(residual, "feat", axis=3, tiled=True)
    grad_act = jnp.einsum(
        "brwd,hd->brwh", whole_cotangent, down_weight, preferred_element_type=jnp.float32
    )
    whole_residual, grad_act = lax.optimization_barrier((whole_residual, grad_act))
    whole_vals = whole_residual.astype(jnp.float32)
    mean_two = jnp.sum(whole_vals, axis=-1, keepdims=True) / full_width
    square_two = jnp.sum(whole_vals * whole_vals, axis=-1, keepdims=True) / full_width
    rstd_two = lax.rsqrt(square_two - mean_two * mean_two + EPSILON)
    vhat = (whole_vals - mean_two) * rstd_two
    hidden = jnp.einsum(
        "brwd,dh->brwh", vhat.astype(jnp.bfloat16), up_weight, preferred_element_type=jnp.float32
    )
    activated = gelu_value(hidden).astype(jnp.bfloat16)
    mixed_term = jnp.einsum(
        "brwh,hd->brwd", activated, down_weight, preferred_element_type=jnp.float32
    )
    output = (residual_vals + channel_share(mixed_term)).astype(jnp.bfloat16)
    grad_hidden = (grad_act * gelu_slope(hidden)).astype(jnp.bfloat16)
    grad_term = jnp.einsum(
        "brwh,dh->brwd", grad_hidden, up_weight, preferred_element_type=jnp.float32
    )
    total_one, total_two = token_sums(
        jnp.sum(grad_term, axis=-1), jnp.sum(grad_term * vhat, axis=-1)
    )
    grad_vhat = channel_share(grad_term)
    own_hat = (residual_vals - mean_two) * rstd_two
    grad_residual = cotangent.astype(jnp.float32) + rstd_two * (
        grad_vhat
        - total_one[..., None] / full_width
        - own_hat * (total_two[..., None] / full_width)
    )
    grad_spec = lat_stacked(
        lat_forward_op,
        stacked_columns(
            lon_stacked_forward(grad_residual, lon_inv_tables, lax.Precision.DEFAULT), jnp.bfloat16
        ),
        lax.Precision.DEFAULT,
    )
    grad_second = jnp.where(
        jnp.abs(second) > SHRINK_LEVEL, to_blocks(grad_spec, block_size), 0.0
    )
    grad_first = jnp.where(first > 0.0, block_stacked_adjoint(grad_second, second_op), 0.0)
    grad_spectrum = block_stacked_adjoint(grad_first, first_op).reshape(spec.shape)
    grad_normed = grad_residual + lon_stacked_back(
        stacked_rows(
            lat_stacked(lat_inverse_op, grad_spectrum, lax.Precision.DEFAULT), jnp.bfloat16
        ),
        lon_fwd_tables,
        lax.Precision.DEFAULT,
    )
    norm_one, norm_two = token_sums(
        jnp.sum(grad_normed, axis=-1), jnp.sum(grad_normed * normed, axis=-1)
    )
    grad_input = grad_residual + rstd_one * (
        grad_normed - norm_one[..., None] / full_width - normed * (norm_two[..., None] / full_width)
    )
    return (output, grad_input.astype(jnp.bfloat16))


def solution(mesh):
    return jax.shard_map(
        per_device,
        mesh=mesh,
        in_specs=(
            P(None, "space", None, "feat"),
            P(None, "space", None, "feat"),
            P(None, "feat", None, None),
            P(None, "feat"),
            P(None, "feat", None, None),
            P(None, "feat"),
            P(None, "feat"),
            P("feat", None),
        ),
        out_specs=(P(None, "space", None, "feat"), P(None, "space", None, "feat")),
        check_vma=False,
    )
```

```python
import math

import jax
import jax.numpy as jnp
from jax import lax
from jax.sharding import PartitionSpec as P

EPSILON = 1e-05
SHRINK_LEVEL = 0.1
HIGHEST = lax.Precision.HIGHEST


def longitude_tables(width_lon):
    mode_count = width_lon // 2 + 1
    cell_index = jnp.arange(width_lon, dtype=jnp.int32)[:, None]
    wave_number = jnp.arange(mode_count, dtype=jnp.int32)[None, :]
    phase_angle = (
        2.0 * math.pi / width_lon * (cell_index * wave_number % width_lon).astype(jnp.float32)
    )
    scaling = 1.0 / math.sqrt(width_lon)
    cos_fwd = jnp.cos(phase_angle) * scaling
    sin_fwd = -jnp.sin(phase_angle) * scaling
    doubled = jnp.where((wave_number == 0) | (wave_number * 2 == width_lon), 1.0, 2.0).astype(
        jnp.float32
    )
    return (cos_fwd, sin_fwd, cos_fwd * doubled, sin_fwd * doubled)


def padded_tables(width_lon, multiple):
    tables = longitude_tables(width_lon)
    modes = tables[0].shape[1]
    extra = -modes % multiple
    return tuple(jnp.pad(table, ((0, 0), (0, extra))) for table in tables)


def lat_apply(table, field):
    return jnp.einsum("gh,bhkc->bgkc", table, field, precision=HIGHEST)


def complex_latitude(table_cos, table_sin, real_part, imag_part, inverse):
    if inverse:
        return (
            lat_apply(table_cos, real_part) + lat_apply(table_sin, imag_part),
            lat_apply(table_cos, imag_part) - lat_apply(table_sin, real_part),
        )
    return (
        lat_apply(table_cos, real_part) - lat_apply(table_sin, imag_part),
        lat_apply(table_cos, imag_part) + lat_apply(table_sin, real_part),
    )


def lon_forward(field, table):
    return jnp.einsum("brwc,wk->brkc", field, table, precision=HIGHEST)


def lon_back(spec, table):
    return jnp.einsum("brkc,wk->brwc", spec, table, precision=HIGHEST)


def to_blocks(field, block_size):
    return field.reshape(field.shape[:-1] + (field.shape[-1] // block_size, block_size))


def block_mult(field, weights):
    return jnp.einsum("...nc,nce->...ne", field, weights, precision=HIGHEST)


def block_mult_back(field, weights):
    return jnp.einsum("...ne,nce->...nc", field, weights, precision=HIGHEST)


def block_product(real_part, imag_part, weights):
    return (
        block_mult(real_part, weights[0]) - block_mult(imag_part, weights[1]),
        block_mult(real_part, weights[1]) + block_mult(imag_part, weights[0]),
    )


def block_adjoint(real_part, imag_part, weights):
    return (
        block_mult_back(real_part, weights[0]) + block_mult_back(imag_part, weights[1]),
        block_mult_back(imag_part, weights[0]) - block_mult_back(real_part, weights[1]),
    )


def latitude_tables(length):
    index_row = jnp.arange(length, dtype=jnp.int32)
    phase_angle = (
        2.0 * math.pi / length * (index_row[:, None] * index_row[None, :] % length).astype(jnp.float32)
    )
    scaling = 1.0 / math.sqrt(length)
    return (jnp.cos(phase_angle) * scaling, -jnp.sin(phase_angle) * scaling)


def to_columns(real_part, imag_part, link_type):
    stacked = jnp.stack([real_part, imag_part]).astype(link_type)
    moved = lax.all_to_all(stacked, "space", 3, 2, tiled=True).astype(jnp.float32)
    return (moved[0], moved[1])


def to_rows(real_part, imag_part, link_type):
    stacked = jnp.stack([real_part, imag_part]).astype(link_type)
    moved = lax.all_to_all(stacked, "space", 2, 3, tiled=True).astype(jnp.float32)
    return (moved[0], moved[1])


def enter_spectrum(real_part, imag_part, tables_lat, link_type=jnp.float32):
    table_cos, table_sin = tables_lat
    real_part, imag_part = to_columns(real_part, imag_part, link_type)
    return complex_latitude(table_cos, table_sin, real_part, imag_part, False)


def leave_spectrum(real_part, imag_part, tables_lat, link_type=jnp.float32):
    table_cos, table_sin = tables_lat
    real_part, imag_part = complex_latitude(table_cos, table_sin, real_part, imag_part, True)
    return to_rows(real_part, imag_part, link_type)


def complex_operator(real_block, imag_block):
    return jnp.stack(
        [jnp.stack([real_block, -imag_block]), jnp.stack([imag_block, real_block])]
    )


def lat_stacked(operator, field, precision=lax.Precision.HIGH):
    return jnp.einsum("pqkh,qbhlc->pbklc", operator, field, precision=precision)


def lon_stacked_forward(field, tables, precision=lax.Precision.HIGH):
    return jnp.einsum("brwc,pwk->pbrkc", field, tables, precision=precision)


def lon_stacked_back(spec, tables, precision=lax.Precision.HIGH):
    return jnp.einsum("pbrkc,pwk->brwc", spec, tables, precision=precision)


def block_operator(weights):
    return jnp.moveaxis(complex_operator(weights[0], weights[1]), 2, 0)


def block_stacked(field, operator):
    return jnp.einsum("qbklnc,npqce->pbklne", field, operator, precision=lax.Precision.HIGH)


def block_stacked_adjoint(field, operator):
    return jnp.einsum("pbklne,npqce->qbklnc", field, operator, precision=lax.Precision.DEFAULT)


def stacked_columns(field, link_type):
    return lax.all_to_all(field.astype(link_type), "space", 3, 2, tiled=True).astype(jnp.float32)


def stacked_rows(field, link_type):
    return lax.all_to_all(field.astype(link_type), "space", 2, 3, tiled=True).astype(jnp.float32)


def token_sums(first_term, second_term):
    pair = jnp.stack([first_term, second_term])
    count = lax.axis_size("feat")
    shifted = jnp.stack(
        [pair]
        + [
            lax.ppermute(pair, "feat", [(i, (i + count - shift) % count) for i in range(count)])
            for shift in range(1, count)
        ]
    )
    total = shifted[0]
    for source in range(1, count):
        total = total + shifted[source]
    return (total[0], total[1])


def ring_send(block):
    count = lax.axis_size("feat")
    return [block] + [
        lax.ppermute(block, "feat", [(i, (i + shift) % count) for i in range(count)])
        for shift in range(1, count)
    ]


def ring_assemble(parts):
    count = len(parts)
    position = lax.axis_index("feat")
    block = parts[0]
    width = block.shape[-1]
    whole = jnp.zeros(block.shape[:-1] + (width * count,), block.dtype)
    for shift, moved in enumerate(parts):
        source = (position + count - shift) % count
        whole = lax.dynamic_update_slice_in_dim(whole, moved, source * width, axis=block.ndim - 1)
    return whole


def channel_share(term):
    return lax.psum_scatter(
        term.astype(jnp.bfloat16), "feat", scatter_dimension=3, tiled=True
    ).astype(jnp.float32)


def gelu_value(field):
    return 0.5 * field * (1.0 + lax.erf(field * (1.0 / math.sqrt(2.0))))


def gelu_slope(field):
    return 0.5 * (1.0 + lax.erf(field * (1.0 / math.sqrt(2.0)))) + field * jnp.exp(
        -0.5 * field * field
    ) * (1.0 / math.sqrt(2.0 * math.pi))


def per_device(inputs, cotangent, spec_w1, spec_b1, spec_w2, spec_b2, up_weight, down_weight):
    full_width = up_weight.shape[0]
    block_size = spec_w1.shape[2]
    tables_lon = padded_tables(inputs.shape[2], lax.axis_size("space"))
    tables_lat = latitude_tables(inputs.shape[1] * lax.axis_size("space"))
    cos_fwd, sin_fwd, cos_inv, sin_inv = tables_lon
    table_cos, table_sin = tables_lat
    operators = (
        jnp.stack([cos_fwd, sin_fwd]),
        jnp.stack([cos_inv, sin_inv]),
        complex_operator(table_cos, table_sin),
        complex_operator(table_cos, -table_sin),
        block_operator(spec_w1),
        block_operator(spec_w2),
    )
    operators = lax.optimization_barrier(operators)
    lon_fwd_tables, lon_inv_tables, lat_forward_op, lat_inverse_op, first_op, second_op = operators
    values = inputs.astype(jnp.float32)
    cotangent_parts = lax.all_gather(cotangent, "feat", axis=3, tiled=True)
    first_sum, second_sum = token_sums(jnp.sum(values, axis=-1), jnp.sum(values * values, axis=-1))
    mean_one = first_sum[..., None] / full_width
    rstd_one = lax.rsqrt(second_sum[..., None] / full_width - mean_one * mean_one + EPSILON)
    normed = (values - mean_one) * rstd_one
    spec = lat_stacked(
        lat_forward_op, stacked_columns(lon_stacked_forward(normed, lon_fwd_tables), jnp.float32)
    )
    spec_blocks = to_blocks(spec, block_size)
    bias_one = to_blocks(spec_b1, block_size)[:, None, None, None]
    bias_two = to_blocks(spec_b2, block_size)[:, None, None, None]
    first = jax.nn.relu(block_stacked(spec_blocks, first_op) + bias_one)
    second = block_stacked(first, second_op) + bias_two
    shrunk = (second - jnp.clip(second, -SHRINK_LEVEL, SHRINK_LEVEL)).reshape(spec.shape)
    shrunk, cotangent_parts = lax.optimization_barrier((shrunk, cotangent_parts))
    whole_cotangent = cotangent_parts
    filtered = lon_stacked_back(
        stacked_rows(lat_stacked(lat_inverse_op, shrunk, lax.Precision.DEFAULT), jnp.bfloat16),
        lon_inv_tables,
        lax.Precision.DEFAULT,
    )
    residual = (filtered + normed + values).astype(jnp.bfloat16)
    residual_vals = residual.astype(jnp.float32)
    whole_residual = lax.all_gather(residual, "feat", axis=3, tiled=True)
    grad_act = jnp.einsum(
        "brwd,hd->brwh", whole_cotangent, down_weight, preferred_element_type=jnp.float32
    )
    whole_residual, grad_act = lax.optimization_barrier((whole_residual, grad_act))
    whole_vals = whole_residual.astype(jnp.float32)
    mean_two = jnp.sum(whole_vals, axis=-1, keepdims=True) / full_width
    square_two = jnp.sum(whole_vals * whole_vals, axis=-1, keepdims=True) / full_width
    rstd_two = lax.rsqrt(square_two - mean_two * mean_two + EPSILON)
    vhat = (whole_vals - mean_two) * rstd_two
    hidden = jnp.einsum(
        "brwd,dh->brwh", vhat.astype(jnp.bfloat16), up_weight, preferred_element_type=jnp.float32
    )
    activated = gelu_value(hidden).astype(jnp.bfloat16)
    mixed_term = jnp.einsum(
        "brwh,hd->brwd", activated, down_weight, preferred_element_type=jnp.float32
    )
    output = (residual_vals + channel_share(mixed_term)).astype(jnp.bfloat16)
    grad_hidden = (grad_act * gelu_slope(hidden)).astype(jnp.bfloat16)
    grad_term = jnp.einsum(
        "brwh,dh->brwd", grad_hidden, up_weight, preferred_element_type=jnp.float32
    )
    total_one, total_two = token_sums(
        jnp.sum(grad_term, axis=-1), jnp.sum(grad_term * vhat, axis=-1)
    )
    grad_vhat = channel_share(grad_term)
    own_hat = (residual_vals - mean_two) * rstd_two
    grad_residual = cotangent.astype(jnp.float32) + rstd_two * (
        grad_vhat
        - total_one[..., None] / full_width
        - own_hat * (total_two[..., None] / full_width)
    )
    grad_spec = lat_stacked(
        lat_forward_op,
        stacked_columns(
            lon_stacked_forward(grad_residual, lon_inv_tables, lax.Precision.DEFAULT), jnp.bfloat16
        ),
        lax.Precision.DEFAULT,
    )
    grad_second = jnp.where(
        jnp.abs(second) > SHRINK_LEVEL, to_blocks(grad_spec, block_size), 0.0
    )
    grad_first = jnp.where(first > 0.0, block_stacked_adjoint(grad_second, second_op), 0.0)
    grad_spectrum = block_stacked_adjoint(grad_first, first_op).reshape(spec.shape)
    grad_normed = grad_residual + lon_stacked_back(
        stacked_rows(
            lat_stacked(lat_inverse_op, grad_spectrum, lax.Precision.DEFAULT), jnp.bfloat16
        ),
        lon_fwd_tables,
        lax.Precision.DEFAULT,
    )
    norm_one, norm_two = token_sums(
        jnp.sum(grad_normed, axis=-1), jnp.sum(grad_normed * normed, axis=-1)
    )
    grad_input = grad_residual + rstd_one * (
        grad_normed - norm_one[..., None] / full_width - normed * (norm_two[..., None] / full_width)
    )
    return (output, grad_input.astype(jnp.bfloat16))


def solution(mesh):
    return jax.shard_map(
        per_device,
        mesh=mesh,
        in_specs=(
            P(None, "space", None, "feat"),
            P(None, "space", None, "feat"),
            P(None, "feat", None, None),
            P(None, "feat"),
            P(None, "feat", None, None),
            P(None, "feat"),
            P(None, "feat"),
            P("feat", None),
        ),
        out_specs=(P(None, "space", None, "feat"), P(None, "space", None, "feat")),
        check_vma=False,
    )
```
